32 devices in a mesh: row: 8 (over y, x, core), col: 4 (over z).
Axes of the slice: x: 2, y: 2, z: 4, core: 2. Of those that a mesh axis runs over, the one named last changes fastest.
Arguments:
- pair: bfloat16 [256, 256, 128], P('row', 'col'), may hold values from -6 to 6
- mask: int32 [256], replicated, may hold values 0 or 1
- w_agate: bfloat16 [128, 128], replicated, may hold values from -0.5 to 0.5
- w_aproj: bfloat16 [128, 128], replicated, may hold values from -0.5 to 0.5
- w_bgate: bfloat16 [128, 128], replicated, may hold values from -0.5 to 0.5
- w_bproj: bfloat16 [128, 128], replicated, may hold values from -0.5 to 0.5
- w_gate: bfloat16 [128, 128], replicated, may hold values from -0.5 to 0.5
- w_out: bfloat16 [128, 128], replicated, may hold values from -0.5 to 0.5
- w_up: bfloat16 [128, 512], replicated, may hold values from -0.5 to 0.5
- w_down: bfloat16 [512, 128], replicated, may hold values from -0.25 to 0.25
Outputs:
- updated: bfloat16 [256, 256, 128], P('row', 'col')
The draws below stay inside these ranges and needn't reach their ends.
All inputs are finite; a program needn't handle non-finite values.
Results may differ from the reference program's by a relative error of at most 0.0059.
Values may be sent and summed in bfloat16 or wider, within the bound.
No kernel may reach another device: no remote copies, remote signals or barrier semaphores. Data moves between devices by JAX's collectives and lax.ppermute only.
A program may use at most 64 MiB of HBM per device.

```python
import jax
import jax.numpy as jnp
from jax import lax

C = 128
HID = 128
TRANS = 512
N = 256
N_ROW = 8


def set_ends(array, rng, low, high):
    place = [jax.random.randint(jax.random.fold_in(rng, axis), (), 0, length) for axis, length in enumerate(array.shape)]
    main_axis = array.shape.index(max(array.shape))
    neighbour = place[:main_axis] + [(place[main_axis] + 1) % array.shape[main_axis]] + place[main_axis + 1:]
    return array.at[tuple(place)].set(low).at[tuple(neighbour)].set(high)


def level_of(own_key, shape, split, least, top_value):
    factor_of, own = 1.0, jax.random.fold_in(own_key, 6)
    for position, parts in split:
        steps = jnp.exp(jax.random.uniform(jax.random.fold_in(own, position), (parts,), jnp.float32, least / len(split), top_value / len(split)))
        factor_of = factor_of * jnp.repeat(steps, shape[position] // parts).reshape([-1 if axis == position else 1 for axis in range(len(shape))])
    return factor_of


def scatter_about(key, shape, deviation, limit, pieces=(), held_as=jnp.bfloat16):
    gain = level_of(key, shape, pieces, -0.22, 0.18) if pieces else 1.0
    entries = jax.random.normal(key, shape, jnp.float32) * deviation * gain
    return jnp.minimum(jnp.maximum(entries, -limit), limit).astype(held_as)


def setup_inputs(seed: int = 0) -> dict:
    splits = jax.random.split(jax.random.key(seed), 11)
    pair = scatter_about(splits[0], (N, N, C), 1.0, 6.0, ((0, 8), (1, 4)))
    mask = set_ends((jax.random.randint(splits[1], (N,), 0, 8) < 7).astype(jnp.int32), jax.random.fold_in(splits[1], 1), 0, 1)
    w_agate = scatter_about(splits[2], (C, HID), C ** -0.5, 0.5)
    w_aproj = scatter_about(splits[3], (C, HID), C ** -0.5, 0.5)
    w_bgate = scatter_about(splits[4], (C, HID), C ** -0.5, 0.5)
    w_bproj = scatter_about(splits[5], (C, HID), C ** -0.5, 0.5)
    w_gate = scatter_about(splits[6], (C, C), C ** -0.5, 0.5)
    w_out = scatter_about(splits[7], (HID, C), HID ** -0.5, 0.5)
    w_up = scatter_about(splits[8], (C, TRANS), C ** -0.5, 0.5)
    w_down = scatter_about(splits[9], (TRANS, C), TRANS ** -0.5, 0.25)
    return dict(pair=pair, mask=mask, w_agate=w_agate, w_aproj=w_aproj, w_bgate=w_bgate, w_bproj=w_bproj, w_gate=w_gate, w_out=w_out, w_up=w_up, w_down=w_down)


def layer_norm(values):
    center = values - lax.optimization_barrier(jnp.mean(values, axis=-1, keepdims=True))
    spread = lax.optimization_barrier(jnp.mean(center * center, axis=-1, keepdims=True))
    return center * lax.rsqrt(spread + 1e-05)

def reference(pair, mask, w_agate, w_aproj, w_bgate, w_bproj, w_gate, w_out, w_up, w_down):
    size = pair.shape[0]
    width = pair.shape[2]
    block = size // N_ROW
    present = mask.astype(jnp.float32)
    starts = (jnp.arange(N_ROW) * block).astype(jnp.int32)

    def project_block(start):
        rows = lax.dynamic_slice_in_dim(pair, start, block, 0).astype(jnp.float32)
        normed = layer_norm(rows).astype(jnp.bfloat16).reshape(block * size, width)
        row_mask = lax.dynamic_slice_in_dim(present, start, block, 0)
        pair_mask = (row_mask[:, None] * present[None, :]).reshape(block * size, 1)
        left = jax.nn.sigmoid(jnp.dot(normed, w_agate, preferred_element_type=jnp.float32)) * jnp.dot(normed, w_aproj, preferred_element_type=jnp.float32) * pair_mask
        right = jax.nn.sigmoid(jnp.dot(normed, w_bgate, preferred_element_type=jnp.float32)) * jnp.dot(normed, w_bproj, preferred_element_type=jnp.float32) * pair_mask
        return (left.astype(jnp.bfloat16).reshape(block, size, -1), right.astype(jnp.bfloat16).reshape(block, size, -1))
    left, right = lax.map(project_block, starts)
    left = jnp.transpose(left.reshape(size, size, -1), (2, 0, 1))
    right = jnp.transpose(right.reshape(size, size, -1), (2, 0, 1))

    def product(operands):
        return jnp.dot(operands[0], operands[1].T, preferred_element_type=jnp.float32).astype(jnp.bfloat16)
    mixed = lax.map(product, (left, right))

    def finish(start):
        rows = lax.dynamic_slice_in_dim(pair, start, block, 0).astype(jnp.float32).reshape(block * size, width)
        normed = layer_norm(rows).astype(jnp.bfloat16)
        gate = jax.nn.sigmoid(jnp.dot(normed, w_gate, preferred_element_type=jnp.float32))
        mixed_rows = lax.dynamic_slice_in_dim(mixed, start, block, 1)
        mixed_rows = jnp.transpose(mixed_rows, (1, 2, 0)).astype(jnp.float32).reshape(block * size, -1)
        mixed_normed = layer_norm(mixed_rows).astype(jnp.bfloat16)
        middle = rows + gate * jnp.dot(mixed_normed, w_out, preferred_element_type=jnp.float32)
        trans_in = layer_norm(middle).astype(jnp.bfloat16)
        trans_hidden = jax.nn.relu(jnp.dot(trans_in, w_up, preferred_element_type=jnp.float32)).astype(jnp.bfloat16)
        result = middle + jnp.dot(trans_hidden, w_down, preferred_element_type=jnp.float32)
        return result.astype(jnp.bfloat16).reshape(block, size, width)
    return lax.map(finish, starts).reshape(size, size, width)
```

```python
import functools

import jax
import jax.numpy as jnp
from jax import lax
from jax.sharding import PartitionSpec as P


def layer_norm(values):
    center = values - jnp.mean(values, axis=-1, keepdims=True)
    spread = jnp.mean(center * center, axis=-1, keepdims=True)
    return center * lax.rsqrt(spread + 1e-05)


def project(pair, mask, w_agate, w_aproj, w_bgate, w_bproj, w_gate):
    rows, cols, width = pair.shape
    present = mask.astype(jnp.float32)
    row_start = lax.axis_index("row") * rows
    col_start = lax.axis_index("col") * cols
    row_mask = lax.dynamic_slice_in_dim(present, row_start, rows, 0)
    col_mask = lax.dynamic_slice_in_dim(present, col_start, cols, 0)
    pair_mask = (row_mask[:, None] * col_mask[None, :]).reshape(rows * cols, 1)
    pair_flat = pair.astype(jnp.float32).reshape(rows * cols, width)
    normed = layer_norm(pair_flat).astype(jnp.bfloat16)
    gate = jax.nn.sigmoid(jnp.dot(normed, w_gate, preferred_element_type=jnp.float32))
    left = (
        jax.nn.sigmoid(jnp.dot(normed, w_agate, preferred_element_type=jnp.float32))
        * jnp.dot(normed, w_aproj, preferred_element_type=jnp.float32)
        * pair_mask
    )
    right = (
        jax.nn.sigmoid(jnp.dot(normed, w_bgate, preferred_element_type=jnp.float32))
        * jnp.dot(normed, w_bproj, preferred_element_type=jnp.float32)
        * pair_mask
    )
    return pair_flat, gate, left.astype(jnp.bfloat16), right.astype(jnp.bfloat16)


def transition(pair_flat, gate, mixed_rows, w_out, w_up, w_down):
    mixed_normed = layer_norm(mixed_rows).astype(jnp.bfloat16)
    middle = pair_flat + gate * jnp.dot(mixed_normed, w_out, preferred_element_type=jnp.float32)
    trans_in = layer_norm(middle).astype(jnp.bfloat16)
    trans_hidden = jax.nn.relu(jnp.dot(trans_in, w_up, preferred_element_type=jnp.float32)).astype(
        jnp.bfloat16
    )
    return middle + jnp.dot(trans_hidden, w_down, preferred_element_type=jnp.float32)


def body_split(pair, mask, w_agate, w_aproj, w_bgate, w_bproj, w_gate, w_out, w_up, w_down, *, n_row, n_col):
    rows, cols, width = pair.shape
    n_dev = n_row * n_col
    pair_flat, gate, left, right = project(pair, mask, w_agate, w_aproj, w_bgate, w_bproj, w_gate)
    hid = left.shape[-1]
    group = hid // n_dev
    edges = jnp.stack([left, right], axis=0).reshape(2, rows, cols, n_dev, group)
    edges = jnp.transpose(edges, (3, 0, 4, 1, 2))
    edges = lax.all_to_all(edges, ("row", "col"), split_axis=0, concat_axis=0, tiled=True)
    edges = edges.reshape(n_row, n_col, 2, group, rows, cols)
    edges = jnp.transpose(edges, (2, 3, 0, 4, 1, 5)).reshape(2, group, n_row * rows, n_col * cols)
    mixed = jnp.einsum(
        "cik,cjk->cij", edges[0], edges[1], preferred_element_type=jnp.float32
    ).astype(jnp.bfloat16)
    mixed = mixed.reshape(group, n_row, rows, n_col, cols)
    mixed = jnp.transpose(mixed, (1, 3, 0, 2, 4)).reshape(n_dev, group, rows, cols)
    mixed = lax.all_to_all(mixed, ("row", "col"), split_axis=0, concat_axis=0, tiled=True)
    mixed_rows = jnp.transpose(mixed.reshape(hid, rows, cols), (1, 2, 0))
    mixed_rows = mixed_rows.astype(jnp.float32).reshape(rows * cols, hid)
    result = transition(pair_flat, gate, mixed_rows, w_out, w_up, w_down)
    return result.astype(jnp.bfloat16).reshape(rows, cols, width)


def body_rows(pair, mask, w_agate, w_aproj, w_bgate, w_bproj, w_gate, w_out, w_up, w_down):
    rows, cols, width = pair.shape
    pair_flat, gate, left, right = project(pair, mask, w_agate, w_aproj, w_bgate, w_bproj, w_gate)
    left_major = jnp.transpose(left.reshape(rows, cols, -1), (2, 0, 1))
    right_major = jnp.transpose(right.reshape(rows, cols, -1), (2, 0, 1))
    left_spread, right_spread = (
        lax.all_to_all(
            lax.all_to_all(left_major, "row", split_axis=0, concat_axis=1, tiled=True),
            "col",
            split_axis=1,
            concat_axis=2,
            tiled=True,
        ),
        lax.all_to_all(
            lax.all_to_all(right_major, "row", split_axis=0, concat_axis=1, tiled=True),
            "col",
            split_axis=1,
            concat_axis=2,
            tiled=True,
        ),
    )
    mixed = jnp.einsum(
        "cik,cjk->cij",
        lax.all_gather(left_spread, "col", axis=1, tiled=True),
        right_spread,
        preferred_element_type=jnp.float32,
    ).astype(jnp.bfloat16)
    mixed = lax.all_to_all(mixed, "row", split_axis=1, concat_axis=0, tiled=True)
    mixed_rows = jnp.transpose(mixed, (1, 2, 0)).astype(jnp.float32).reshape(rows * cols, -1)
    result = transition(pair_flat, gate, mixed_rows, w_out, w_up, w_down)
    return result.astype(jnp.bfloat16).reshape(rows, cols, width)


def solution(mesh):
    placed = (P("row", "col", None), P(), P(), P(), P(), P(), P(), P(), P(), P())
    n_row, n_col = mesh.shape["row"], mesh.shape["col"]

    def run(pair, mask, w_agate, *weights):
        hid = w_agate.shape[1]
        if hid % (n_row * n_col) == 0:
            body = functools.partial(body_split, n_row=n_row, n_col=n_col)
        else:
            body = body_rows
        mapped = jax.shard_map(
            body, mesh=mesh, in_specs=placed, out_specs=P("row", "col", None), check_vma=False
        )
        return mapped(pair, mask, w_agate, *weights)

    return run
```

```python
import functools

import jax
import jax.numpy as jnp
from jax import lax
from jax.experimental import pallas as pl
from jax.sharding import PartitionSpec as P


def layer_norm(values):
    center = values - jnp.mean(values, axis=-1, keepdims=True)
    spread = jnp.mean(center * center, axis=-1, keepdims=True)
    return center * lax.rsqrt(spread + 1e-05)


def project(pair, mask, w_agate, w_aproj, w_bgate, w_bproj, w_gate):
    rows, cols, width = pair.shape
    present = mask.astype(jnp.float32)
    row_start = lax.axis_index("row") * rows
    col_start = lax.axis_index("col") * cols
    row_mask = lax.dynamic_slice_in_dim(present, row_start, rows, 0)
    col_mask = lax.dynamic_slice_in_dim(present, col_start, cols, 0)
    pair_mask = (row_mask[:, None] * col_mask[None, :]).reshape(rows * cols, 1)
    pair_flat = pair.astype(jnp.float32).reshape(rows * cols, width)
    normed = layer_norm(pair_flat).astype(jnp.bfloat16)
    gate = jax.nn.sigmoid(jnp.dot(normed, w_gate, preferred_element_type=jnp.float32))
    left = (
        jax.nn.sigmoid(jnp.dot(normed, w_agate, preferred_element_type=jnp.float32))
        * jnp.dot(normed, w_aproj, preferred_element_type=jnp.float32)
        * pair_mask
    )
    right = (
        jax.nn.sigmoid(jnp.dot(normed, w_bgate, preferred_element_type=jnp.float32))
        * jnp.dot(normed, w_bproj, preferred_element_type=jnp.float32)
        * pair_mask
    )
    return pair_flat, gate, left.astype(jnp.bfloat16), right.astype(jnp.bfloat16)


def transition(pair_flat, gate, mixed_rows, w_out, w_up, w_down):
    mixed_normed = layer_norm(mixed_rows).astype(jnp.bfloat16)
    middle = pair_flat + gate * jnp.dot(mixed_normed, w_out, preferred_element_type=jnp.float32)
    trans_in = layer_norm(middle).astype(jnp.bfloat16)
    trans_hidden = jax.nn.relu(jnp.dot(trans_in, w_up, preferred_element_type=jnp.float32)).astype(
        jnp.bfloat16
    )
    return middle + jnp.dot(trans_hidden, w_down, preferred_element_type=jnp.float32)


def body_split(pair, mask, w_agate, w_aproj, w_bgate, w_bproj, w_gate, w_out, w_up, w_down, *, n_row, n_col):
    rows, cols, width = pair.shape
    n_dev = n_row * n_col
    pair_flat, gate, left, right = project(pair, mask, w_agate, w_aproj, w_bgate, w_bproj, w_gate)
    hid = left.shape[-1]
    group = hid // n_dev
    edges = jnp.stack([left, right], axis=0).reshape(2, rows, cols, n_dev, group)
    edges = jnp.transpose(edges, (3, 0, 4, 1, 2))
    edges = lax.all_to_all(edges, ("row", "col"), split_axis=0, concat_axis=0, tiled=True)
    edges = edges.reshape(n_row, n_col, 2, group, rows, cols)
    edges = jnp.transpose(edges, (2, 3, 0, 4, 1, 5)).reshape(2, group, n_row * rows, n_col * cols)
    mixed = jnp.einsum(
        "cik,cjk->cij", edges[0], edges[1], preferred_element_type=jnp.float32
    ).astype(jnp.bfloat16)
    mixed = mixed.reshape(group, n_row, rows, n_col, cols)
    mixed = jnp.transpose(mixed, (1, 3, 0, 2, 4)).reshape(n_dev, group, rows, cols)
    mixed = lax.all_to_all(mixed, ("row", "col"), split_axis=0, concat_axis=0, tiled=True)
    mixed_rows = jnp.transpose(mixed.reshape(hid, rows, cols), (1, 2, 0))
    mixed_rows = mixed_rows.astype(jnp.float32).reshape(rows * cols, hid)
    result = transition(pair_flat, gate, mixed_rows, w_out, w_up, w_down)
    return result.astype(jnp.bfloat16).reshape(rows, cols, width)


def mix_kernel(edges_ref, out_ref, *, n_col):
    n_dev, _, pairs, rows, lanes = edges_ref.shape
    n_row = n_dev // n_col
    cols = lanes // 2
    parity = (lax.broadcasted_iota(jnp.int32, (1, n_col * lanes), 1) // cols) % 2
    for hp in range(pairs):

        def whole(side):
            return jnp.concatenate(
                [
                    jnp.concatenate([edges_ref[r * n_col + c, side, hp] for c in range(n_col)], axis=1)
                    for r in range(n_row)
                ],
                axis=0,
            )

        left = whole(0)
        right = whole(1)
        right_even = jnp.where(parity == 0, right, jnp.zeros_like(right))
        right_odd = jnp.where(parity == 1, right, jnp.zeros_like(right))
        for c in range(n_col):
            block = slice(c * cols, (c + 1) * cols)
            rhs = jnp.concatenate([right_even[block], right_odd[block]], axis=0)
            mixed = lax.dot_general(
                left, rhs, (((1,), (1,)), ((), ())), preferred_element_type=jnp.float32
            ).astype(out_ref.dtype)
            for r in range(n_row):
                out_ref[r * n_col + c, hp] = mixed[r * rows : (r + 1) * rows]


def body_kernel(pair, mask, w_agate, w_aproj, w_bgate, w_bproj, w_gate, w_out, w_up, w_down, *, n_row, n_col):
    rows, cols, width = pair.shape
    n_dev = n_row * n_col
    pair_flat, gate, left, right = project(pair, mask, w_agate, w_aproj, w_bgate, w_bproj, w_gate)
    hid = left.shape[-1]
    pairs = hid // n_dev // 2

    def chunks(edges):
        edges = jnp.transpose(edges.reshape(rows, cols, n_dev, pairs, 2), (2, 3, 0, 4, 1))
        return edges.reshape(n_dev, pairs, rows, 2 * cols)

    edges = jnp.stack([chunks(left), chunks(right)], axis=1)
    edges = lax.all_to_all(edges, ("row", "col"), split_axis=0, concat_axis=0, tiled=True)
    mixed = pl.pallas_call(
        functools.partial(mix_kernel, n_col=n_col),
        out_shape=jax.ShapeDtypeStruct((n_dev, pairs, rows, 2 * cols), jnp.bfloat16),
    )(edges)
    mixed = lax.all_to_all(mixed, ("row", "col"), split_axis=0, concat_axis=0, tiled=True)
    mixed = jnp.transpose(mixed.reshape(n_dev, pairs, rows, 2, cols), (2, 4, 0, 1, 3))
    mixed_rows = mixed.astype(jnp.float32).reshape(rows * cols, hid)
    result = transition(pair_flat, gate, mixed_rows, w_out, w_up, w_down)
    return result.astype(jnp.bfloat16).reshape(rows, cols, width)


def body_rows(pair, mask, w_agate, w_aproj, w_bgate, w_bproj, w_gate, w_out, w_up, w_down):
    rows, cols, width = pair.shape
    pair_flat, gate, left, right = project(pair, mask, w_agate, w_aproj, w_bgate, w_bproj, w_gate)
    left_major = jnp.transpose(left.reshape(rows, cols, -1), (2, 0, 1))
    right_major = jnp.transpose(right.reshape(rows, cols, -1), (2, 0, 1))
    left_spread, right_spread = (
        lax.all_to_all(
            lax.all_to_all(left_major, "row", split_axis=0, concat_axis=1, tiled=True),
            "col",
            split_axis=1,
            concat_axis=2,
            tiled=True,
        ),
        lax.all_to_all(
            lax.all_to_all(right_major, "row", split_axis=0, concat_axis=1, tiled=True),
            "col",
            split_axis=1,
            concat_axis=2,
            tiled=True,
        ),
    )
    mixed = jnp.einsum(
        "cik,cjk->cij",
        lax.all_gather(left_spread, "col", axis=1, tiled=True),
        right_spread,
        preferred_element_type=jnp.float32,
    ).astype(jnp.bfloat16)
    mixed = lax.all_to_all(mixed, "row", split_axis=1, concat_axis=0, tiled=True)
    mixed_rows = jnp.transpose(mixed, (1, 2, 0)).astype(jnp.float32).reshape(rows * cols, -1)
    result = transition(pair_flat, gate, mixed_rows, w_out, w_up, w_down)
    return result.astype(jnp.bfloat16).reshape(rows, cols, width)


def solution(mesh):
    placed = (P("row", "col", None), P(), P(), P(), P(), P(), P(), P(), P(), P())
    n_row, n_col = mesh.shape["row"], mesh.shape["col"]

    def run(pair, mask, w_agate, *weights):
        hid = w_agate.shape[1]
        rows, cols = pair.shape[0] // n_row, pair.shape[1] // n_col
        if hid % (2 * n_row * n_col) == 0 and 2 * cols == 128 and rows % 16 == 0 and n_row * rows == n_col * cols:
            body = functools.partial(body_kernel, n_row=n_row, n_col=n_col)
        elif hid % (n_row * n_col) == 0:
            body = functools.partial(body_split, n_row=n_row, n_col=n_col)
        else:
            body = body_rows
        mapped = jax.shard_map(
            body, mesh=mesh, in_specs=placed, out_specs=P("row", "col", None), check_vma=False
        )
        return mapped(pair, mask, w_agate, *weights)

    return run
```

```python
import functools

import jax
import jax.numpy as jnp
from jax import lax
from jax.experimental import pallas as pl
from jax.sharding import PartitionSpec as P


def layer_norm(values):
    center = values - jnp.mean(values, axis=-1, keepdims=True)
    spread = jnp.mean(center * center, axis=-1, keepdims=True)
    return center * lax.rsqrt(spread + 1e-05)


def project(pair, mask, w_agate, w_aproj, w_bgate, w_bproj, w_gate):
    rows, cols, width = pair.shape
    present = mask.astype(jnp.float32)
    row_start = lax.axis_index("row") * rows
    col_start = lax.axis_index("col") * cols
    row_mask = lax.dynamic_slice_in_dim(present, row_start, rows, 0)
    col_mask = lax.dynamic_slice_in_dim(present, col_start, cols, 0)
    pair_mask = (row_mask[:, None] * col_mask[None, :]).reshape(rows * cols, 1)
    pair_flat = pair.astype(jnp.float32).reshape(rows * cols, width)
    normed = layer_norm(pair_flat).astype(jnp.bfloat16)
    gate = jax.nn.sigmoid(jnp.dot(normed, w_gate, preferred_element_type=jnp.float32))
    left = (
        jax.nn.sigmoid(jnp.dot(normed, w_agate, preferred_element_type=jnp.float32))
        * jnp.dot(normed, w_aproj, preferred_element_type=jnp.float32)
        * pair_mask
    )
    right = (
        jax.nn.sigmoid(jnp.dot(normed, w_bgate, preferred_element_type=jnp.float32))
        * jnp.dot(normed, w_bproj, preferred_element_type=jnp.float32)
        * pair_mask
    )
    return pair_flat, gate, left.astype(jnp.bfloat16), right.astype(jnp.bfloat16)


def transition(pair_flat, gate, mixed_rows, w_out, w_up, w_down):
    mixed_normed = layer_norm(mixed_rows).astype(jnp.bfloat16)
    middle = pair_flat + gate * jnp.dot(mixed_normed, w_out, preferred_element_type=jnp.float32)
    trans_in = layer_norm(middle).astype(jnp.bfloat16)
    trans_hidden = jax.nn.relu(jnp.dot(trans_in, w_up, preferred_element_type=jnp.float32)).astype(
        jnp.bfloat16
    )
    return middle + jnp.dot(trans_hidden, w_down, preferred_element_type=jnp.float32)


def body_split(pair, mask, w_agate, w_aproj, w_bgate, w_bproj, w_gate, w_out, w_up, w_down, *, n_row, n_col):
    rows, cols, width = pair.shape
    n_dev = n_row * n_col
    pair_flat, gate, left, right = project(pair, mask, w_agate, w_aproj, w_bgate, w_bproj, w_gate)
    hid = left.shape[-1]
    group = hid // n_dev
    edges = jnp.stack([left, right], axis=0).reshape(2, rows, cols, n_dev, group)
    edges = jnp.transpose(edges, (3, 0, 4, 1, 2))
    edges = lax.all_to_all(edges, ("row", "col"), split_axis=0, concat_axis=0, tiled=True)
    edges = edges.reshape(n_row, n_col, 2, group, rows, cols)
    edges = jnp.transpose(edges, (2, 3, 0, 4, 1, 5)).reshape(2, group, n_row * rows, n_col * cols)
    mixed = jnp.einsum(
        "cik,cjk->cij", edges[0], edges[1], preferred_element_type=jnp.float32
    ).astype(jnp.bfloat16)
    mixed = mixed.reshape(group, n_row, rows, n_col, cols)
    mixed = jnp.transpose(mixed, (1, 3, 0, 2, 4)).reshape(n_dev, group, rows, cols)
    mixed = lax.all_to_all(mixed, ("row", "col"), split_axis=0, concat_axis=0, tiled=True)
    mixed_rows = jnp.transpose(mixed.reshape(hid, rows, cols), (1, 2, 0))
    mixed_rows = mixed_rows.astype(jnp.float32).reshape(rows * cols, hid)
    result = transition(pair_flat, gate, mixed_rows, w_out, w_up, w_down)
    return result.astype(jnp.bfloat16).reshape(rows, cols, width)


def mix_kernel(edges_ref, out_ref, *, n_col):
    n_dev, _, pairs, rows, lanes = edges_ref.shape
    n_row = n_dev // n_col
    cols = lanes // 2
    parity = (lax.broadcasted_iota(jnp.int32, (1, n_col * lanes), 1) // cols) % 2
    for hp in range(pairs):

        def whole(side):
            return jnp.concatenate(
                [
                    jnp.concatenate([edges_ref[r * n_col + c, side, hp] for c in range(n_col)], axis=1)
                    for r in range(n_row)
                ],
                axis=0,
            )

        left = whole(0)
        right = whole(1)
        right_even = jnp.where(parity == 0, right, jnp.zeros_like(right))
        right_odd = jnp.where(parity == 1, right, jnp.zeros_like(right))
        for c in range(n_col):
            block = slice(c * cols, (c + 1) * cols)
            rhs = jnp.concatenate([right_even[block], right_odd[block]], axis=0)
            mixed = lax.dot_general(
                left, rhs, (((1,), (1,)), ((), ())), preferred_element_type=jnp.float32
            ).astype(out_ref.dtype)
            for r in range(n_row):
                out_ref[r * n_col + c, hp] = mixed[r * rows : (r + 1) * rows]


def body_kernel(pair, mask, w_agate, w_aproj, w_bgate, w_bproj, w_gate, w_out, w_up, w_down, *, n_row, n_col):
    rows, cols, width = pair.shape
    n_dev = n_row * n_col
    pair_flat, gate, left, right = project(pair, mask, w_agate, w_aproj, w_bgate, w_bproj, w_gate)
    hid = left.shape[-1]
    pairs = hid // n_dev // 2

    def chunks(edges):
        edges = jnp.transpose(edges.reshape(rows, cols, n_dev, pairs, 2), (2, 3, 0, 4, 1))
        return edges.reshape(n_dev, pairs, rows, 2 * cols)

    edges = jnp.stack([chunks(left), chunks(right)], axis=1)
    edges = lax.all_to_all(edges, ("row", "col"), split_axis=0, concat_axis=0, tiled=True)
    mixed = pl.pallas_call(
        functools.partial(mix_kernel, n_col=n_col),
        out_shape=jax.ShapeDtypeStruct((n_dev, pairs, rows, 2 * cols), jnp.bfloat16),
    )(edges)
    mixed = lax.all_to_all(mixed, ("row", "col"), split_axis=0, concat_axis=0, tiled=True)
    mixed = jnp.transpose(mixed.reshape(n_dev, pairs, rows, 2, cols), (2, 4, 0, 1, 3))
    mixed_rows = mixed.astype(jnp.float32).reshape(rows * cols, hid)
    result = transition(pair_flat, gate, mixed_rows, w_out, w_up, w_down)
    return result.astype(jnp.bfloat16).reshape(rows, cols, width)


def project_kernel(pair_ref, mask_ref, w2_ref, wg_ref, z_ref, gate_ref):
    rows, cols, width = pair_ref.shape
    quarter = w2_ref.shape[0] // 4

    def row(i, carry):
        values = pair_ref[i].astype(jnp.float32)
        center = values - jnp.mean(values, axis=-1, keepdims=True)
        spread = jnp.mean(center * center, axis=-1, keepdims=True)
        normed = (center * lax.rsqrt(spread + 1e-05)).astype(jnp.bfloat16)
        gate_ref[i] = jax.nn.sigmoid(jnp.dot(normed, wg_ref[...], preferred_element_type=jnp.float32))
        zeros = jnp.zeros_like(normed)
        doubled = jnp.concatenate(
            [jnp.concatenate([normed, zeros], axis=1), jnp.concatenate([zeros, normed], axis=1)], axis=0
        )
        proj = lax.dot_general(
            w2_ref[...], doubled, (((1,), (1,)), ((), ())), preferred_element_type=jnp.float32
        )
        present = mask_ref[pl.ds(i, 1), :]
        left = jax.nn.sigmoid(proj[0:quarter]) * proj[quarter : 2 * quarter] * present
        right = jax.nn.sigmoid(proj[2 * quarter : 3 * quarter]) * proj[3 * quarter :] * present
        z_ref[i] = jnp.concatenate([left, right], axis=0).astype(z_ref.dtype)
        return carry

    lax.fori_loop(0, rows, row, 0)


def body_fused(pair, mask, w_agate, w_aproj, w_bgate, w_bproj, w_gate, w_out, w_up, w_down, *, n_row, n_col):
    rows, cols, width = pair.shape
    n_dev = n_row * n_col
    hid = w_agate.shape[1]
    pairs = hid // n_dev // 2
    present = mask.astype(jnp.float32)
    row_mask = lax.dynamic_slice_in_dim(present, lax.axis_index("row") * rows, rows, 0)
    col_mask = lax.dynamic_slice_in_dim(present, lax.axis_index("col") * cols, cols, 0)
    lane_mask = row_mask[:, None] * jnp.concatenate([col_mask, col_mask])[None, :]

    def paired(w):
        return jnp.transpose(w.reshape(width, hid // 2, 2), (1, 2, 0)).reshape(hid // 2, 2 * width)

    w2 = jnp.concatenate([paired(w) for w in (w_agate, w_aproj, w_bgate, w_bproj)], axis=0)
    z, gate = pl.pallas_call(
        project_kernel,
        out_shape=(
            jax.ShapeDtypeStruct((rows, hid, 2 * cols), jnp.bfloat16),
            jax.ShapeDtypeStruct((rows, cols, width), jnp.float32),
        ),
    )(pair, lane_mask, w2, w_gate)
    edges = jnp.transpose(z.reshape(rows, 2, n_dev, pairs, 2 * cols), (2, 1, 3, 0, 4))
    edges = lax.all_to_all(edges, ("row", "col"), split_axis=0, concat_axis=0, tiled=True)
    mixed = pl.pallas_call(
        functools.partial(mix_kernel, n_col=n_col),
        out_shape=jax.ShapeDtypeStruct((n_dev, pairs, rows, 2 * cols), jnp.bfloat16),
    )(edges)
    mixed = lax.all_to_all(mixed, ("row", "col"), split_axis=0, concat_axis=0, tiled=True)
    mixed = jnp.transpose(mixed.reshape(n_dev, pairs, rows, 2, cols), (2, 4, 0, 1, 3))
    mixed_rows = mixed.astype(jnp.float32).reshape(rows * cols, hid)
    pair_flat = pair.astype(jnp.float32).reshape(rows * cols, width)
    result = transition(pair_flat, gate.reshape(rows * cols, width), mixed_rows, w_out, w_up, w_down)
    return result.astype(jnp.bfloat16).reshape(rows, cols, width)


def body_rows(pair, mask, w_agate, w_aproj, w_bgate, w_bproj, w_gate, w_out, w_up, w_down):
    rows, cols, width = pair.shape
    pair_flat, gate, left, right = project(pair, mask, w_agate, w_aproj, w_bgate, w_bproj, w_gate)
    left_major = jnp.transpose(left.reshape(rows, cols, -1), (2, 0, 1))
    right_major = jnp.transpose(right.reshape(rows, cols, -1), (2, 0, 1))
    left_spread, right_spread = (
        lax.all_to_all(
            lax.all_to_all(left_major, "row", split_axis=0, concat_axis=1, tiled=True),
            "col",
            split_axis=1,
            concat_axis=2,
            tiled=True,
        ),
        lax.all_to_all(
            lax.all_to_all(right_major, "row", split_axis=0, concat_axis=1, tiled=True),
            "col",
            split_axis=1,
            concat_axis=2,
            tiled=True,
        ),
    )
    mixed = jnp.einsum(
        "cik,cjk->cij",
        lax.all_gather(left_spread, "col", axis=1, tiled=True),
        right_spread,
        preferred_element_type=jnp.float32,
    ).astype(jnp.bfloat16)
    mixed = lax.all_to_all(mixed, "row", split_axis=1, concat_axis=0, tiled=True)
    mixed_rows = jnp.transpose(mixed, (1, 2, 0)).astype(jnp.float32).reshape(rows * cols, -1)
    result = transition(pair_flat, gate, mixed_rows, w_out, w_up, w_down)
    return result.astype(jnp.bfloat16).reshape(rows, cols, width)


def solution(mesh):
    placed = (P("row", "col", None), P(), P(), P(), P(), P(), P(), P(), P(), P())
    n_row, n_col = mesh.shape["row"], mesh.shape["col"]

    def run(pair, mask, w_agate, *weights):
        hid = w_agate.shape[1]
        rows, cols = pair.shape[0] // n_row, pair.shape[1] // n_col
        if hid % (2 * n_row * n_col) == 0 and 2 * cols == 128 and rows % 16 == 0 and n_row * rows == n_col * cols:
            body = functools.partial(body_fused, n_row=n_row, n_col=n_col)
        elif hid % (n_row * n_col) == 0:
            body = functools.partial(body_split, n_row=n_row, n_col=n_col)
        else:
            body = body_rows
        mapped = jax.shard_map(
            body, mesh=mesh, in_specs=placed, out_specs=P("row", "col", None), check_vma=False
        )
        return mapped(pair, mask, w_agate, *weights)

    return run
```

```python
import functools

import jax
import jax.numpy as jnp
from jax import lax
from jax.experimental import pallas as pl
from jax.sharding import PartitionSpec as P


def layer_norm(values):
    center = values - jnp.mean(values, axis=-1, keepdims=True)
    spread = jnp.mean(center * center, axis=-1, keepdims=True)
    return center * lax.rsqrt(spread + 1e-05)


def project(pair, mask, w_agate, w_aproj, w_bgate, w_bproj, w_gate):
    rows, cols, width = pair.shape
    present = mask.astype(jnp.float32)
    row_start = lax.axis_index("row") * rows
    col_start = lax.axis_index("col") * cols
    row_mask = lax.dynamic_slice_in_dim(present, row_start, rows, 0)
    col_mask = lax.dynamic_slice_in_dim(present, col_start, cols, 0)
    pair_mask = (row_mask[:, None] * col_mask[None, :]).reshape(rows * cols, 1)
    pair_flat = pair.astype(jnp.float32).reshape(rows * cols, width)
    normed = layer_norm(pair_flat).astype(jnp.bfloat16)
    gate = jax.nn.sigmoid(jnp.dot(normed, w_gate, preferred_element_type=jnp.float32))
    left = (
        jax.nn.sigmoid(jnp.dot(normed, w_agate, preferred_element_type=jnp.float32))
        * jnp.dot(normed, w_aproj, preferred_element_type=jnp.float32)
        * pair_mask
    )
    right = (
        jax.nn.sigmoid(jnp.dot(normed, w_bgate, preferred_element_type=jnp.float32))
        * jnp.dot(normed, w_bproj, preferred_element_type=jnp.float32)
        * pair_mask
    )
    return pair_flat, gate, left.astype(jnp.bfloat16), right.astype(jnp.bfloat16)


def transition(pair_flat, gate, mixed_rows, w_out, w_up, w_down):
    mixed_normed = layer_norm(mixed_rows).astype(jnp.bfloat16)
    middle = pair_flat + gate * jnp.dot(mixed_normed, w_out, preferred_element_type=jnp.float32)
    trans_in = layer_norm(middle).astype(jnp.bfloat16)
    trans_hidden = jax.nn.relu(jnp.dot(trans_in, w_up, preferred_element_type=jnp.float32)).astype(
        jnp.bfloat16
    )
    return middle + jnp.dot(trans_hidden, w_down, preferred_element_type=jnp.float32)


def body_split(pair, mask, w_agate, w_aproj, w_bgate, w_bproj, w_gate, w_out, w_up, w_down, *, n_row, n_col):
    rows, cols, width = pair.shape
    n_dev = n_row * n_col
    pair_flat, gate, left, right = project(pair, mask, w_agate, w_aproj, w_bgate, w_bproj, w_gate)
    hid = left.shape[-1]
    group = hid // n_dev
    edges = jnp.stack([left, right], axis=0).reshape(2, rows, cols, n_dev, group)
    edges = jnp.transpose(edges, (3, 0, 4, 1, 2))
    edges = lax.all_to_all(edges, ("row", "col"), split_axis=0, concat_axis=0, tiled=True)
    edges = edges.reshape(n_row, n_col, 2, group, rows, cols)
    edges = jnp.transpose(edges, (2, 3, 0, 4, 1, 5)).reshape(2, group, n_row * rows, n_col * cols)
    mixed = jnp.einsum(
        "cik,cjk->cij", edges[0], edges[1], preferred_element_type=jnp.float32
    ).astype(jnp.bfloat16)
    mixed = mixed.reshape(group, n_row, rows, n_col, cols)
    mixed = jnp.transpose(mixed, (1, 3, 0, 2, 4)).reshape(n_dev, group, rows, cols)
    mixed = lax.all_to_all(mixed, ("row", "col"), split_axis=0, concat_axis=0, tiled=True)
    mixed_rows = jnp.transpose(mixed.reshape(hid, rows, cols), (1, 2, 0))
    mixed_rows = mixed_rows.astype(jnp.float32).reshape(rows * cols, hid)
    result = transition(pair_flat, gate, mixed_rows, w_out, w_up, w_down)
    return result.astype(jnp.bfloat16).reshape(rows, cols, width)


def mix_kernel(edges_ref, out_ref, *, n_col):
    n_dev, _, pairs, rows, lanes = edges_ref.shape
    n_row = n_dev // n_col
    cols = lanes // 2
    parity = (lax.broadcasted_iota(jnp.int32, (1, n_col * lanes), 1) // cols) % 2
    for hp in range(pairs):

        def whole(side):
            return jnp.concatenate(
                [
                    jnp.concatenate([edges_ref[r * n_col + c, side, hp] for c in range(n_col)], axis=1)
                    for r in range(n_row)
                ],
                axis=0,
            )

        left = whole(0)
        right = whole(1)
        right_even = jnp.where(parity == 0, right, jnp.zeros_like(right))
        right_odd = jnp.where(parity == 1, right, jnp.zeros_like(right))
        for c in range(n_col):
            block = slice(c * cols, (c + 1) * cols)
            rhs = jnp.concatenate([right_even[block], right_odd[block]], axis=0)
            mixed = lax.dot_general(
                left, rhs, (((1,), (1,)), ((), ())), preferred_element_type=jnp.float32
            ).astype(out_ref.dtype)
            for r in range(n_row):
                out_ref[r * n_col + c, hp] = mixed[r * rows : (r + 1) * rows]


def body_kernel(pair, mask, w_agate, w_aproj, w_bgate, w_bproj, w_gate, w_out, w_up, w_down, *, n_row, n_col):
    rows, cols, width = pair.shape
    n_dev = n_row * n_col
    pair_flat, gate, left, right = project(pair, mask, w_agate, w_aproj, w_bgate, w_bproj, w_gate)
    hid = left.shape[-1]
    pairs = hid // n_dev // 2

    def chunks(edges):
        edges = jnp.transpose(edges.reshape(rows, cols, n_dev, pairs, 2), (2, 3, 0, 4, 1))
        return edges.reshape(n_dev, pairs, rows, 2 * cols)

    edges = jnp.stack([chunks(left), chunks(right)], axis=1)
    edges = lax.all_to_all(edges, ("row", "col"), split_axis=0, concat_axis=0, tiled=True)
    mixed = pl.pallas_call(
        functools.partial(mix_kernel, n_col=n_col),
        out_shape=jax.ShapeDtypeStruct((n_dev, pairs, rows, 2 * cols), jnp.bfloat16),
    )(edges)
    mixed = lax.all_to_all(mixed, ("row", "col"), split_axis=0, concat_axis=0, tiled=True)
    mixed = jnp.transpose(mixed.reshape(n_dev, pairs, rows, 2, cols), (2, 4, 0, 1, 3))
    mixed_rows = mixed.astype(jnp.float32).reshape(rows * cols, hid)
    result = transition(pair_flat, gate, mixed_rows, w_out, w_up, w_down)
    return result.astype(jnp.bfloat16).reshape(rows, cols, width)


def project_kernel(pair_ref, mask_ref, w2_ref, wg_ref, z_ref, gate_ref, *, block):
    rows, cols, width = pair_ref.shape
    quarter = w2_ref.shape[0] // 4

    def rows_of(step, carry):
        first = pl.multiple_of(step * block, block)
        values = pair_ref[pl.ds(first, block)].astype(jnp.float32).reshape(block * cols, width)
        center = values - jnp.mean(values, axis=-1, keepdims=True)
        spread = jnp.mean(center * center, axis=-1, keepdims=True)
        normed = (center * lax.rsqrt(spread + 1e-05)).astype(jnp.bfloat16)
        gate = jax.nn.sigmoid(jnp.dot(normed, wg_ref[...], preferred_element_type=jnp.float32))
        gate_ref[pl.ds(first, block)] = gate.reshape(block, cols, width)
        zeros = jnp.zeros_like(normed)
        top = jnp.concatenate([normed, zeros], axis=1).reshape(block, cols, 2 * width)
        bottom = jnp.concatenate([zeros, normed], axis=1).reshape(block, cols, 2 * width)
        doubled = jnp.concatenate([top, bottom], axis=1).reshape(block * 2 * cols, 2 * width)
        proj = lax.dot_general(
            w2_ref[...], doubled, (((1,), (1,)), ((), ())), preferred_element_type=jnp.float32
        )
        for i in range(block):
            part = proj[:, i * 2 * cols : (i + 1) * 2 * cols]
            present = mask_ref[pl.ds(first + i, 1), :]
            left = jax.nn.sigmoid(part[0:quarter]) * part[quarter : 2 * quarter] * present
            right = jax.nn.sigmoid(part[2 * quarter : 3 * quarter]) * part[3 * quarter :] * present
            z_ref[first + i] = jnp.concatenate([left, right], axis=0).astype(z_ref.dtype)
        return carry

    lax.fori_loop(0, rows // block, rows_of, 0)


def body_fused(pair, mask, w_agate, w_aproj, w_bgate, w_bproj, w_gate, w_out, w_up, w_down, *, n_row, n_col):
    rows, cols, width = pair.shape
    n_dev = n_row * n_col
    hid = w_agate.shape[1]
    pairs = hid // n_dev // 2
    present = mask.astype(jnp.float32)
    row_mask = lax.dynamic_slice_in_dim(present, lax.axis_index("row") * rows, rows, 0)
    col_mask = lax.dynamic_slice_in_dim(present, lax.axis_index("col") * cols, cols, 0)
    lane_mask = row_mask[:, None] * jnp.concatenate([col_mask, col_mask])[None, :]

    w2 = jnp.stack([w_agate, w_aproj, w_bgate, w_bproj]).reshape(4, width, hid // 2, 2)
    w2 = jnp.transpose(w2, (0, 2, 3, 1)).reshape(2 * hid, 2 * width)
    z, gate = pl.pallas_call(
        functools.partial(project_kernel, block=8),
        out_shape=(
            jax.ShapeDtypeStruct((rows, hid, 2 * cols), jnp.bfloat16),
            jax.ShapeDtypeStruct((rows, cols, width), jnp.float32),
        ),
    )(pair, lane_mask, w2, w_gate)
    edges = jnp.transpose(z.reshape(rows, 2, n_dev, pairs, 2 * cols), (2, 1, 3, 0, 4))
    edges = lax.all_to_all(edges, ("row", "col"), split_axis=0, concat_axis=0, tiled=True)
    mixed = pl.pallas_call(
        functools.partial(mix_kernel, n_col=n_col),
        out_shape=jax.ShapeDtypeStruct((n_dev, pairs, rows, 2 * cols), jnp.bfloat16),
    )(edges)
    mixed = lax.all_to_all(mixed, ("row", "col"), split_axis=0, concat_axis=0, tiled=True)
    mixed = jnp.transpose(mixed.reshape(n_dev, pairs, rows, 2, cols), (2, 4, 0, 1, 3))
    mixed_rows = mixed.astype(jnp.float32).reshape(rows * cols, hid)
    pair_flat = pair.astype(jnp.float32).reshape(rows * cols, width)
    result = transition(pair_flat, gate.reshape(rows * cols, width), mixed_rows, w_out, w_up, w_down)
    return result.astype(jnp.bfloat16).reshape(rows, cols, width)


def body_rows(pair, mask, w_agate, w_aproj, w_bgate, w_bproj, w_gate, w_out, w_up, w_down):
    rows, cols, width = pair.shape
    pair_flat, gate, left, right = project(pair, mask, w_agate, w_aproj, w_bgate, w_bproj, w_gate)
    left_major = jnp.transpose(left.reshape(rows, cols, -1), (2, 0, 1))
    right_major = jnp.transpose(right.reshape(rows, cols, -1), (2, 0, 1))
    left_spread, right_spread = (
        lax.all_to_all(
            lax.all_to_all(left_major, "row", split_axis=0, concat_axis=1, tiled=True),
            "col",
            split_axis=1,
            concat_axis=2,
            tiled=True,
        ),
        lax.all_to_all(
            lax.all_to_all(right_major, "row", split_axis=0, concat_axis=1, tiled=True),
            "col",
            split_axis=1,
            concat_axis=2,
            tiled=True,
        ),
    )
    mixed = jnp.einsum(
        "cik,cjk->cij",
        lax.all_gather(left_spread, "col", axis=1, tiled=True),
        right_spread,
        preferred_element_type=jnp.float32,
    ).astype(jnp.bfloat16)
    mixed = lax.all_to_all(mixed, "row", split_axis=1, concat_axis=0, tiled=True)
    mixed_rows = jnp.transpose(mixed, (1, 2, 0)).astype(jnp.float32).reshape(rows * cols, -1)
    result = transition(pair_flat, gate, mixed_rows, w_out, w_up, w_down)
    return result.astype(jnp.bfloat16).reshape(rows, cols, width)


def solution(mesh):
    placed = (P("row", "col", None), P(), P(), P(), P(), P(), P(), P(), P(), P())
    n_row, n_col = mesh.shape["row"], mesh.shape["col"]

    def run(pair, mask, w_agate, *weights):
        hid = w_agate.shape[1]
        rows, cols = pair.shape[0] // n_row, pair.shape[1] // n_col
        if hid % (2 * n_row * n_col) == 0 and 2 * cols == 128 and rows % 16 == 0 and n_row * rows == n_col * cols:
            body = functools.partial(body_fused, n_row=n_row, n_col=n_col)
        elif hid % (n_row * n_col) == 0:
            body = functools.partial(body_split, n_row=n_row, n_col=n_col)
        else:
            body = body_rows
        mapped = jax.shard_map(
            body, mesh=mesh, in_specs=placed, out_specs=P("row", "col", None), check_vma=False
        )
        return mapped(pair, mask, w_agate, *weights)

    return run
```

```python
import functools

import jax
import jax.numpy as jnp
from jax import lax
from jax.experimental import pallas as pl
from jax.sharding import PartitionSpec as P


def layer_norm(values):
    center = values - jnp.mean(values, axis=-1, keepdims=True)
    spread = jnp.mean(center * center, axis=-1, keepdims=True)
    return center * lax.rsqrt(spread + 1e-05)


def project(pair, mask, w_agate, w_aproj, w_bgate, w_bproj, w_gate):
    rows, cols, width = pair.shape
    present = mask.astype(jnp.float32)
    row_start = lax.axis_index("row") * rows
    col_start = lax.axis_index("col") * cols
    row_mask = lax.dynamic_slice_in_dim(present, row_start, rows, 0)
    col_mask = lax.dynamic_slice_in_dim(present, col_start, cols, 0)
    pair_mask = (row_mask[:, None] * col_mask[None, :]).reshape(rows * cols, 1)
    pair_flat = pair.astype(jnp.float32).reshape(rows * cols, width)
    normed = layer_norm(pair_flat).astype(jnp.bfloat16)
    gate = jax.nn.sigmoid(jnp.dot(normed, w_gate, preferred_element_type=jnp.float32))
    left = (
        jax.nn.sigmoid(jnp.dot(normed, w_agate, preferred_element_type=jnp.float32))
        * jnp.dot(normed, w_aproj, preferred_element_type=jnp.float32)
        * pair_mask
    )
    right = (
        jax.nn.sigmoid(jnp.dot(normed, w_bgate, preferred_element_type=jnp.float32))
        * jnp.dot(normed, w_bproj, preferred_element_type=jnp.float32)
        * pair_mask
    )
    return pair_flat, gate, left.astype(jnp.bfloat16), right.astype(jnp.bfloat16)


def transition(pair_flat, gate, mixed_rows, w_out, w_up, w_down):
    mixed_normed = layer_norm(mixed_rows).astype(jnp.bfloat16)
    middle = pair_flat + gate * jnp.dot(mixed_normed, w_out, preferred_element_type=jnp.float32)
    trans_in = layer_norm(middle).astype(jnp.bfloat16)
    trans_hidden = jax.nn.relu(jnp.dot(trans_in, w_up, preferred_element_type=jnp.float32)).astype(
        jnp.bfloat16
    )
    return middle + jnp.dot(trans_hidden, w_down, preferred_element_type=jnp.float32)


def body_split(pair, mask, w_agate, w_aproj, w_bgate, w_bproj, w_gate, w_out, w_up, w_down, *, n_row, n_col):
    rows, cols, width = pair.shape
    n_dev = n_row * n_col
    pair_flat, gate, left, right = project(pair, mask, w_agate, w_aproj, w_bgate, w_bproj, w_gate)
    hid = left.shape[-1]
    group = hid // n_dev
    edges = jnp.stack([left, right], axis=0).reshape(2, rows, cols, n_dev, group)
    edges = jnp.transpose(edges, (3, 0, 4, 1, 2))
    edges = lax.all_to_all(edges, ("row", "col"), split_axis=0, concat_axis=0, tiled=True)
    edges = edges.reshape(n_row, n_col, 2, group, rows, cols)
    edges = jnp.transpose(edges, (2, 3, 0, 4, 1, 5)).reshape(2, group, n_row * rows, n_col * cols)
    mixed = jnp.einsum(
        "cik,cjk->cij", edges[0], edges[1], preferred_element_type=jnp.float32
    ).astype(jnp.bfloat16)
    mixed = mixed.reshape(group, n_row, rows, n_col, cols)
    mixed = jnp.transpose(mixed, (1, 3, 0, 2, 4)).reshape(n_dev, group, rows, cols)
    mixed = lax.all_to_all(mixed, ("row", "col"), split_axis=0, concat_axis=0, tiled=True)
    mixed_rows = jnp.transpose(mixed.reshape(hid, rows, cols), (1, 2, 0))
    mixed_rows = mixed_rows.astype(jnp.float32).reshape(rows * cols, hid)
    result = transition(pair_flat, gate, mixed_rows, w_out, w_up, w_down)
    return result.astype(jnp.bfloat16).reshape(rows, cols, width)


def mix_kernel(edges_ref, out_ref, *, n_col):
    n_dev, _, pairs, rows, lanes = edges_ref.shape
    n_row = n_dev // n_col
    cols = lanes // 2
    parity = (lax.broadcasted_iota(jnp.int32, (1, n_col * lanes), 1) // cols) % 2
    for hp in range(pairs):

        def whole(side):
            return jnp.concatenate(
                [
                    jnp.concatenate([edges_ref[r * n_col + c, side, hp] for c in range(n_col)], axis=1)
                    for r in range(n_row)
                ],
                axis=0,
            )

        left = whole(0)
        right = whole(1)
        right_even = jnp.where(parity == 0, right, jnp.zeros_like(right))
        right_odd = jnp.where(parity == 1, right, jnp.zeros_like(right))
        for c in range(n_col):
            block = slice(c * cols, (c + 1) * cols)
            rhs = jnp.concatenate([right_even[block], right_odd[block]], axis=0)
            mixed = lax.dot_general(
                left, rhs, (((1,), (1,)), ((), ())), preferred_element_type=jnp.float32
            ).astype(out_ref.dtype)
            for r in range(n_row):
                out_ref[r * n_col + c, hp] = mixed[r * rows : (r + 1) * rows]


def body_kernel(pair, mask, w_agate, w_aproj, w_bgate, w_bproj, w_gate, w_out, w_up, w_down, *, n_row, n_col):
    rows, cols, width = pair.shape
    n_dev = n_row * n_col
    pair_flat, gate, left, right = project(pair, mask, w_agate, w_aproj, w_bgate, w_bproj, w_gate)
    hid = left.shape[-1]
    pairs = hid // n_dev // 2

    def chunks(edges):
        edges = jnp.transpose(edges.reshape(rows, cols, n_dev, pairs, 2), (2, 3, 0, 4, 1))
        return edges.reshape(n_dev, pairs, rows, 2 * cols)

    edges = jnp.stack([chunks(left), chunks(right)], axis=1)
    edges = lax.all_to_all(edges, ("row", "col"), split_axis=0, concat_axis=0, tiled=True)
    mixed = pl.pallas_call(
        functools.partial(mix_kernel, n_col=n_col),
        out_shape=jax.ShapeDtypeStruct((n_dev, pairs, rows, 2 * cols), jnp.bfloat16),
    )(edges)
    mixed = lax.all_to_all(mixed, ("row", "col"), split_axis=0, concat_axis=0, tiled=True)
    mixed = jnp.transpose(mixed.reshape(n_dev, pairs, rows, 2, cols), (2, 4, 0, 1, 3))
    mixed_rows = mixed.astype(jnp.float32).reshape(rows * cols, hid)
    result = transition(pair_flat, gate, mixed_rows, w_out, w_up, w_down)
    return result.astype(jnp.bfloat16).reshape(rows, cols, width)


def project_kernel(pair_ref, mask_ref, wag_ref, wap_ref, wbg_ref, wbp_ref, wg_ref, z_ref, gate_ref, *, block):
    rows, cols, width = pair_ref.shape
    quarter = wag_ref.shape[1] // 2

    def paired(w_ref):
        turned = w_ref[...].astype(jnp.float32).T.astype(jnp.bfloat16)
        return jnp.concatenate([turned[:quarter], turned[quarter:]], axis=1)

    w2 = jnp.concatenate([paired(w) for w in (wag_ref, wap_ref, wbg_ref, wbp_ref)], axis=0)

    def rows_of(step, carry):
        first = pl.multiple_of(step * block, block)
        values = pair_ref[pl.ds(first, block)].astype(jnp.float32).reshape(block * cols, width)
        center = values - jnp.mean(values, axis=-1, keepdims=True)
        spread = jnp.mean(center * center, axis=-1, keepdims=True)
        normed = (center * lax.rsqrt(spread + 1e-05)).astype(jnp.bfloat16)
        gate = jax.nn.sigmoid(jnp.dot(normed, wg_ref[...], preferred_element_type=jnp.float32))
        gate_ref[pl.ds(first, block)] = gate.reshape(block, cols, width)
        zeros = jnp.zeros_like(normed)
        top = jnp.concatenate([normed, zeros], axis=1).reshape(block, cols, 2 * width)
        bottom = jnp.concatenate([zeros, normed], axis=1).reshape(block, cols, 2 * width)
        doubled = jnp.concatenate([top, bottom], axis=1).reshape(block * 2 * cols, 2 * width)
        proj = lax.dot_general(
            w2, doubled, (((1,), (1,)), ((), ())), preferred_element_type=jnp.float32
        )
        for i in range(block):
            part = proj[:, i * 2 * cols : (i + 1) * 2 * cols]
            present = mask_ref[pl.ds(first + i, 1), :]
            left = jax.nn.sigmoid(part[0:quarter]) * part[quarter : 2 * quarter] * present
            right = jax.nn.sigmoid(part[2 * quarter : 3 * quarter]) * part[3 * quarter :] * present
            z_ref[first + i] = jnp.concatenate([left, right], axis=0).astype(z_ref.dtype)
        return carry

    lax.fori_loop(0, rows // block, rows_of, 0)


def body_fused(pair, mask, w_agate, w_aproj, w_bgate, w_bproj, w_gate, w_out, w_up, w_down, *, n_row, n_col):
    rows, cols, width = pair.shape
    n_dev = n_row * n_col
    hid = w_agate.shape[1]
    pairs = hid // n_dev // 2
    present = mask.astype(jnp.float32)
    row_mask = lax.dynamic_slice_in_dim(present, lax.axis_index("row") * rows, rows, 0)
    col_mask = lax.dynamic_slice_in_dim(present, lax.axis_index("col") * cols, cols, 0)
    lane_mask = row_mask[:, None] * jnp.concatenate([col_mask, col_mask])[None, :]

    z, gate = pl.pallas_call(
        functools.partial(project_kernel, block=8),
        out_shape=(
            jax.ShapeDtypeStruct((rows, hid, 2 * cols), jnp.bfloat16),
            jax.ShapeDtypeStruct((rows, cols, width), jnp.float32),
        ),
    )(pair, lane_mask, w_agate, w_aproj, w_bgate, w_bproj, w_gate)
    edges = jnp.transpose(z.reshape(rows, 2, n_dev, pairs, 2 * cols), (2, 1, 3, 0, 4))
    edges = lax.all_to_all(edges, ("row", "col"), split_axis=0, concat_axis=0, tiled=True)
    mixed = pl.pallas_call(
        functools.partial(mix_kernel, n_col=n_col),
        out_shape=jax.ShapeDtypeStruct((n_dev, pairs, rows, 2 * cols), jnp.bfloat16),
    )(edges)
    mixed = lax.all_to_all(mixed, ("row", "col"), split_axis=0, concat_axis=0, tiled=True)
    mixed = jnp.transpose(mixed.reshape(n_dev, pairs, rows, 2, cols), (2, 4, 3, 0, 1))
    mixed_rows = mixed.astype(jnp.float32).reshape(rows * cols, hid)
    pair_flat = pair.astype(jnp.float32).reshape(rows * cols, width)
    result = transition(pair_flat, gate.reshape(rows * cols, width), mixed_rows, w_out, w_up, w_down)
    return result.astype(jnp.bfloat16).reshape(rows, cols, width)


def body_rows(pair, mask, w_agate, w_aproj, w_bgate, w_bproj, w_gate, w_out, w_up, w_down):
    rows, cols, width = pair.shape
    pair_flat, gate, left, right = project(pair, mask, w_agate, w_aproj, w_bgate, w_bproj, w_gate)
    left_major = jnp.transpose(left.reshape(rows, cols, -1), (2, 0, 1))
    right_major = jnp.transpose(right.reshape(rows, cols, -1), (2, 0, 1))
    left_spread, right_spread = (
        lax.all_to_all(
            lax.all_to_all(left_major, "row", split_axis=0, concat_axis=1, tiled=True),
            "col",
            split_axis=1,
            concat_axis=2,
            tiled=True,
        ),
        lax.all_to_all(
            lax.all_to_all(right_major, "row", split_axis=0, concat_axis=1, tiled=True),
            "col",
            split_axis=1,
            concat_axis=2,
            tiled=True,
        ),
    )
    mixed = jnp.einsum(
        "cik,cjk->cij",
        lax.all_gather(left_spread, "col", axis=1, tiled=True),
        right_spread,
        preferred_element_type=jnp.float32,
    ).astype(jnp.bfloat16)
    mixed = lax.all_to_all(mixed, "row", split_axis=1, concat_axis=0, tiled=True)
    mixed_rows = jnp.transpose(mixed, (1, 2, 0)).astype(jnp.float32).reshape(rows * cols, -1)
    result = transition(pair_flat, gate, mixed_rows, w_out, w_up, w_down)
    return result.astype(jnp.bfloat16).reshape(rows, cols, width)


def solution(mesh):
    placed = (P("row", "col", None), P(), P(), P(), P(), P(), P(), P(), P(), P())
    n_row, n_col = mesh.shape["row"], mesh.shape["col"]

    def run(pair, mask, w_agate, *weights):
        hid = w_agate.shape[1]
        rows, cols = pair.shape[0] // n_row, pair.shape[1] // n_col
        if hid % (2 * n_row * n_col) == 0 and 2 * cols == 128 and rows % 16 == 0 and n_row * rows == n_col * cols:
            body = functools.partial(body_fused, n_row=n_row, n_col=n_col)
        elif hid % (n_row * n_col) == 0:
            body = functools.partial(body_split, n_row=n_row, n_col=n_col)
        else:
            body = body_rows
        mapped = jax.shard_map(
            body, mesh=mesh, in_specs=placed, out_specs=P("row", "col", None), check_vma=False
        )
        return mapped(pair, mask, w_agate, *weights)

    return run
```

```python
import functools

import jax
import jax.numpy as jnp
from jax import lax
from jax.experimental import pallas as pl
from jax.sharding import PartitionSpec as P


def layer_norm(values):
    center = values - jnp.mean(values, axis=-1, keepdims=True)
    spread = jnp.mean(center * center, axis=-1, keepdims=True)
    return center * lax.rsqrt(spread + 1e-05)


def project(pair, mask, w_agate, w_aproj, w_bgate, w_bproj, w_gate):
    rows, cols, width = pair.shape
    present = mask.astype(jnp.float32)
    row_start = lax.axis_index("row") * rows
    col_start = lax.axis_index("col") * cols
    row_mask = lax.dynamic_slice_in_dim(present, row_start, rows, 0)
    col_mask = lax.dynamic_slice_in_dim(present, col_start, cols, 0)
    pair_mask = (row_mask[:, None] * col_mask[None, :]).reshape(rows * cols, 1)
    pair_flat = pair.astype(jnp.float32).reshape(rows * cols, width)
    normed = layer_norm(pair_flat).astype(jnp.bfloat16)
    gate = jax.nn.sigmoid(jnp.dot(normed, w_gate, preferred_element_type=jnp.float32))
    left = (
        jax.nn.sigmoid(jnp.dot(normed, w_agate, preferred_element_type=jnp.float32))
        * jnp.dot(normed, w_aproj, preferred_element_type=jnp.float32)
        * pair_mask
    )
    right = (
        jax.nn.sigmoid(jnp.dot(normed, w_bgate, preferred_element_type=jnp.float32))
        * jnp.dot(normed, w_bproj, preferred_element_type=jnp.float32)
        * pair_mask
    )
    return pair_flat, gate, left.astype(jnp.bfloat16), right.astype(jnp.bfloat16)


def transition(pair_flat, gate, mixed_rows, w_out, w_up, w_down):
    mixed_normed = layer_norm(mixed_rows).astype(jnp.bfloat16)
    middle = pair_flat + gate * jnp.dot(mixed_normed, w_out, preferred_element_type=jnp.float32)
    trans_in = layer_norm(middle).astype(jnp.bfloat16)
    trans_hidden = jax.nn.relu(jnp.dot(trans_in, w_up, preferred_element_type=jnp.float32)).astype(
        jnp.bfloat16
    )
    return middle + jnp.dot(trans_hidden, w_down, preferred_element_type=jnp.float32)


def body_split(pair, mask, w_agate, w_aproj, w_bgate, w_bproj, w_gate, w_out, w_up, w_down, *, n_row, n_col):
    rows, cols, width = pair.shape
    n_dev = n_row * n_col
    pair_flat, gate, left, right = project(pair, mask, w_agate, w_aproj, w_bgate, w_bproj, w_gate)
    hid = left.shape[-1]
    group = hid // n_dev
    edges = jnp.stack([left, right], axis=0).reshape(2, rows, cols, n_dev, group)
    edges = jnp.transpose(edges, (3, 0, 4, 1, 2))
    edges = lax.all_to_all(edges, ("row", "col"), split_axis=0, concat_axis=0, tiled=True)
    edges = edges.reshape(n_row, n_col, 2, group, rows, cols)
    edges = jnp.transpose(edges, (2, 3, 0, 4, 1, 5)).reshape(2, group, n_row * rows, n_col * cols)
    mixed = jnp.einsum(
        "cik,cjk->cij", edges[0], edges[1], preferred_element_type=jnp.float32
    ).astype(jnp.bfloat16)
    mixed = mixed.reshape(group, n_row, rows, n_col, cols)
    mixed = jnp.transpose(mixed, (1, 3, 0, 2, 4)).reshape(n_dev, group, rows, cols)
    mixed = lax.all_to_all(mixed, ("row", "col"), split_axis=0, concat_axis=0, tiled=True)
    mixed_rows = jnp.transpose(mixed.reshape(hid, rows, cols), (1, 2, 0))
    mixed_rows = mixed_rows.astype(jnp.float32).reshape(rows * cols, hid)
    result = transition(pair_flat, gate, mixed_rows, w_out, w_up, w_down)
    return result.astype(jnp.bfloat16).reshape(rows, cols, width)


def mix_kernel(edges_ref, out_ref, *, n_col):
    n_dev, _, pairs, rows, lanes = edges_ref.shape
    n_row = n_dev // n_col
    cols = lanes // 2
    parity = (lax.broadcasted_iota(jnp.int32, (1, n_col * lanes), 1) // cols) % 2
    for hp in range(pairs):

        def whole(side):
            return jnp.concatenate(
                [
                    jnp.concatenate([edges_ref[r * n_col + c, side, hp] for c in range(n_col)], axis=1)
                    for r in range(n_row)
                ],
                axis=0,
            )

        left = whole(0)
        right = whole(1)
        right_even = jnp.where(parity == 0, right, jnp.zeros_like(right))
        right_odd = jnp.where(parity == 1, right, jnp.zeros_like(right))
        for c in range(n_col):
            block = slice(c * cols, (c + 1) * cols)
            rhs = jnp.concatenate([right_even[block], right_odd[block]], axis=0)
            mixed = lax.dot_general(
                left, rhs, (((1,), (1,)), ((), ())), preferred_element_type=jnp.float32
            ).astype(out_ref.dtype)
            for r in range(n_row):
                out_ref[r * n_col + c, hp] = mixed[r * rows : (r + 1) * rows]


def body_kernel(pair, mask, w_agate, w_aproj, w_bgate, w_bproj, w_gate, w_out, w_up, w_down, *, n_row, n_col):
    rows, cols, width = pair.shape
    n_dev = n_row * n_col
    pair_flat, gate, left, right = project(pair, mask, w_agate, w_aproj, w_bgate, w_bproj, w_gate)
    hid = left.shape[-1]
    pairs = hid // n_dev // 2

    def chunks(edges):
        edges = jnp.transpose(edges.reshape(rows, cols, n_dev, pairs, 2), (2, 3, 0, 4, 1))
        return edges.reshape(n_dev, pairs, rows, 2 * cols)

    edges = jnp.stack([chunks(left), chunks(right)], axis=1)
    edges = lax.all_to_all(edges, ("row", "col"), split_axis=0, concat_axis=0, tiled=True)
    mixed = pl.pallas_call(
        functools.partial(mix_kernel, n_col=n_col),
        out_shape=jax.ShapeDtypeStruct((n_dev, pairs, rows, 2 * cols), jnp.bfloat16),
    )(edges)
    mixed = lax.all_to_all(mixed, ("row", "col"), split_axis=0, concat_axis=0, tiled=True)
    mixed = jnp.transpose(mixed.reshape(n_dev, pairs, rows, 2, cols), (2, 4, 0, 1, 3))
    mixed_rows = mixed.astype(jnp.float32).reshape(rows * cols, hid)
    result = transition(pair_flat, gate, mixed_rows, w_out, w_up, w_down)
    return result.astype(jnp.bfloat16).reshape(rows, cols, width)


def project_kernel(pair_ref, mask_ref, wag_ref, wap_ref, wbg_ref, wbp_ref, wg_ref, z_ref, gate_ref, *, block):
    rows, cols, width = pair_ref.shape
    quarter = wag_ref.shape[1] // 2

    def paired(w_ref):
        turned = w_ref[...].astype(jnp.float32).T.astype(jnp.bfloat16)
        return jnp.concatenate([turned[:quarter], turned[quarter:]], axis=1)

    w2 = jnp.concatenate([paired(w) for w in (wag_ref, wap_ref, wbg_ref, wbp_ref)], axis=0)

    def rows_of(step, carry):
        first = pl.multiple_of(step * block, block)
        values = pair_ref[pl.ds(first, block)].astype(jnp.float32).reshape(block * cols, width)
        center = values - jnp.mean(values, axis=-1, keepdims=True)
        spread = jnp.mean(center * center, axis=-1, keepdims=True)
        normed = (center * lax.rsqrt(spread + 1e-05)).astype(jnp.bfloat16)
        gate = jax.nn.sigmoid(jnp.dot(normed, wg_ref[...], preferred_element_type=jnp.float32))
        gate_ref[pl.ds(first, block)] = gate.reshape(block, cols, width)
        zeros = jnp.zeros_like(normed)
        top = jnp.concatenate([normed, zeros], axis=1).reshape(block, cols, 2 * width)
        bottom = jnp.concatenate([zeros, normed], axis=1).reshape(block, cols, 2 * width)
        doubled = jnp.concatenate([top, bottom], axis=1).reshape(block * 2 * cols, 2 * width)
        proj = lax.dot_general(
            w2, doubled, (((1,), (1,)), ((), ())), preferred_element_type=jnp.float32
        )
        for i in range(block):
            part = proj[:, i * 2 * cols : (i + 1) * 2 * cols]
            present = mask_ref[pl.ds(first + i, 1), :]
            left = jax.nn.sigmoid(part[0:quarter]) * part[quarter : 2 * quarter] * present
            right = jax.nn.sigmoid(part[2 * quarter : 3 * quarter]) * part[3 * quarter :] * present
            z_ref[first + i] = jnp.concatenate([left, right], axis=0).astype(z_ref.dtype)
        return carry

    lax.fori_loop(0, rows // block, rows_of, 0)


def transition_kernel(mixed_ref, pair_ref, gate_ref, wo_ref, wu_ref, wd_ref, out_ref, *, block):
    rows, cols, width = pair_ref.shape

    def norm(values):
        center = values - jnp.mean(values, axis=-1, keepdims=True)
        spread = jnp.mean(center * center, axis=-1, keepdims=True)
        return center * lax.rsqrt(spread + 1e-05)

    def rows_of(step, carry):
        first = pl.multiple_of(step * block, block)
        mixed = mixed_ref[pl.ds(first, block)].astype(jnp.float32).reshape(block * cols, -1)
        pair = pair_ref[pl.ds(first, block)].astype(jnp.float32).reshape(block * cols, width)
        gate = gate_ref[pl.ds(first, block)].reshape(block * cols, width)
        mixed_normed = norm(mixed).astype(jnp.bfloat16)
        middle = pair + gate * jnp.dot(mixed_normed, wo_ref[...], preferred_element_type=jnp.float32)
        trans_in = norm(middle).astype(jnp.bfloat16)
        hidden = jnp.maximum(jnp.dot(trans_in, wu_ref[...], preferred_element_type=jnp.float32), 0.0)
        result = middle + jnp.dot(hidden.astype(jnp.bfloat16), wd_ref[...], preferred_element_type=jnp.float32)
        out_ref[pl.ds(first, block)] = result.astype(out_ref.dtype).reshape(block, cols, width)
        return carry

    lax.fori_loop(0, rows // block, rows_of, 0)


def body_fused(pair, mask, w_agate, w_aproj, w_bgate, w_bproj, w_gate, w_out, w_up, w_down, *, n_row, n_col):
    rows, cols, width = pair.shape
    n_dev = n_row * n_col
    hid = w_agate.shape[1]
    pairs = hid // n_dev // 2
    present = mask.astype(jnp.float32)
    row_mask = lax.dynamic_slice_in_dim(present, lax.axis_index("row") * rows, rows, 0)
    col_mask = lax.dynamic_slice_in_dim(present, lax.axis_index("col") * cols, cols, 0)
    lane_mask = row_mask[:, None] * jnp.concatenate([col_mask, col_mask])[None, :]

    z, gate = pl.pallas_call(
        functools.partial(project_kernel, block=8),
        out_shape=(
            jax.ShapeDtypeStruct((rows, hid, 2 * cols), jnp.bfloat16),
            jax.ShapeDtypeStruct((rows, cols, width), jnp.float32),
        ),
    )(pair, lane_mask, w_agate, w_aproj, w_bgate, w_bproj, w_gate)
    edges = jnp.transpose(z.reshape(rows, 2, n_dev, pairs, 2 * cols), (2, 1, 3, 0, 4))
    edges = lax.all_to_all(edges, ("row", "col"), split_axis=0, concat_axis=0, tiled=True)
    mixed = pl.pallas_call(
        functools.partial(mix_kernel, n_col=n_col),
        out_shape=jax.ShapeDtypeStruct((n_dev, pairs, rows, 2 * cols), jnp.bfloat16),
    )(edges)
    mixed = lax.all_to_all(mixed, ("row", "col"), split_axis=0, concat_axis=0, tiled=True)
    mixed = jnp.transpose(mixed.reshape(n_dev, pairs, rows, 2, cols), (2, 4, 3, 0, 1)).reshape(rows, cols, hid)
    return pl.pallas_call(
        functools.partial(transition_kernel, block=8),
        out_shape=jax.ShapeDtypeStruct((rows, cols, width), jnp.bfloat16),
    )(mixed, pair, gate, w_out, w_up, w_down)


def body_rows(pair, mask, w_agate, w_aproj, w_bgate, w_bproj, w_gate, w_out, w_up, w_down):
    rows, cols, width = pair.shape
    pair_flat, gate, left, right = project(pair, mask, w_agate, w_aproj, w_bgate, w_bproj, w_gate)
    left_major = jnp.transpose(left.reshape(rows, cols, -1), (2, 0, 1))
    right_major = jnp.transpose(right.reshape(rows, cols, -1), (2, 0, 1))
    left_spread, right_spread = (
        lax.all_to_all(
            lax.all_to_all(left_major, "row", split_axis=0, concat_axis=1, tiled=True),
            "col",
            split_axis=1,
            concat_axis=2,
            tiled=True,
        ),
        lax.all_to_all(
            lax.all_to_all(right_major, "row", split_axis=0, concat_axis=1, tiled=True),
            "col",
            split_axis=1,
            concat_axis=2,
            tiled=True,
        ),
    )
    mixed = jnp.einsum(
        "cik,cjk->cij",
        lax.all_gather(left_spread, "col", axis=1, tiled=True),
        right_spread,
        preferred_element_type=jnp.float32,
    ).astype(jnp.bfloat16)
    mixed = lax.all_to_all(mixed, "row", split_axis=1, concat_axis=0, tiled=True)
    mixed_rows = jnp.transpose(mixed, (1, 2, 0)).astype(jnp.float32).reshape(rows * cols, -1)
    result = transition(pair_flat, gate, mixed_rows, w_out, w_up, w_down)
    return result.astype(jnp.bfloat16).reshape(rows, cols, width)


def solution(mesh):
    placed = (P("row", "col", None), P(), P(), P(), P(), P(), P(), P(), P(), P())
    n_row, n_col = mesh.shape["row"], mesh.shape["col"]

    def run(pair, mask, w_agate, *weights):
        hid = w_agate.shape[1]
        rows, cols = pair.shape[0] // n_row, pair.shape[1] // n_col
        if hid % (2 * n_row * n_col) == 0 and 2 * cols == 128 and rows % 16 == 0 and n_row * rows == n_col * cols:
            body = functools.partial(body_fused, n_row=n_row, n_col=n_col)
        elif hid % (n_row * n_col) == 0:
            body = functools.partial(body_split, n_row=n_row, n_col=n_col)
        else:
            body = body_rows
        mapped = jax.shard_map(
            body, mesh=mesh, in_specs=placed, out_specs=P("row", "col", None), check_vma=False
        )
        return mapped(pair, mask, w_agate, *weights)

    return run
```

```python
import functools

import jax
import jax.numpy as jnp
from jax import lax
from jax.experimental import pallas as pl
from jax.sharding import PartitionSpec as P


def layer_norm(values):
    center = values - jnp.mean(values, axis=-1, keepdims=True)
    spread = jnp.mean(center * center, axis=-1, keepdims=True)
    return center * lax.rsqrt(spread + 1e-05)


def project(pair, mask, w_agate, w_aproj, w_bgate, w_bproj, w_gate):
    rows, cols, width = pair.shape
    present = mask.astype(jnp.float32)
    row_start = lax.axis_index("row") * rows
    col_start = lax.axis_index("col") * cols
    row_mask = lax.dynamic_slice_in_dim(present, row_start, rows, 0)
    col_mask = lax.dynamic_slice_in_dim(present, col_start, cols, 0)
    pair_mask = (row_mask[:, None] * col_mask[None, :]).reshape(rows * cols, 1)
    pair_flat = pair.astype(jnp.float32).reshape(rows * cols, width)
    normed = layer_norm(pair_flat).astype(jnp.bfloat16)
    gate = jax.nn.sigmoid(jnp.dot(normed, w_gate, preferred_element_type=jnp.float32))
    left = (
        jax.nn.sigmoid(jnp.dot(normed, w_agate, preferred_element_type=jnp.float32))
        * jnp.dot(normed, w_aproj, preferred_element_type=jnp.float32)
        * pair_mask
    )
    right = (
        jax.nn.sigmoid(jnp.dot(normed, w_bgate, preferred_element_type=jnp.float32))
        * jnp.dot(normed, w_bproj, preferred_element_type=jnp.float32)
        * pair_mask
    )
    return pair_flat, gate, left.astype(jnp.bfloat16), right.astype(jnp.bfloat16)


def transition(pair_flat, gate, mixed_rows, w_out, w_up, w_down):
    mixed_normed = layer_norm(mixed_rows).astype(jnp.bfloat16)
    middle = pair_flat + gate * jnp.dot(mixed_normed, w_out, preferred_element_type=jnp.float32)
    trans_in = layer_norm(middle).astype(jnp.bfloat16)
    trans_hidden = jax.nn.relu(jnp.dot(trans_in, w_up, preferred_element_type=jnp.float32)).astype(
        jnp.bfloat16
    )
    return middle + jnp.dot(trans_hidden, w_down, preferred_element_type=jnp.float32)


def body_split(pair, mask, w_agate, w_aproj, w_bgate, w_bproj, w_gate, w_out, w_up, w_down, *, n_row, n_col):
    rows, cols, width = pair.shape
    n_dev = n_row * n_col
    pair_flat, gate, left, right = project(pair, mask, w_agate, w_aproj, w_bgate, w_bproj, w_gate)
    hid = left.shape[-1]
    group = hid // n_dev
    edges = jnp.stack([left, right], axis=0).reshape(2, rows, cols, n_dev, group)
    edges = jnp.transpose(edges, (3, 0, 4, 1, 2))
    edges = lax.all_to_all(edges, ("row", "col"), split_axis=0, concat_axis=0, tiled=True)
    edges = edges.reshape(n_row, n_col, 2, group, rows, cols)
    edges = jnp.transpose(edges, (2, 3, 0, 4, 1, 5)).reshape(2, group, n_row * rows, n_col * cols)
    mixed = jnp.einsum(
        "cik,cjk->cij", edges[0], edges[1], preferred_element_type=jnp.float32
    ).astype(jnp.bfloat16)
    mixed = mixed.reshape(group, n_row, rows, n_col, cols)
    mixed = jnp.transpose(mixed, (1, 3, 0, 2, 4)).reshape(n_dev, group, rows, cols)
    mixed = lax.all_to_all(mixed, ("row", "col"), split_axis=0, concat_axis=0, tiled=True)
    mixed_rows = jnp.transpose(mixed.reshape(hid, rows, cols), (1, 2, 0))
    mixed_rows = mixed_rows.astype(jnp.float32).reshape(rows * cols, hid)
    result = transition(pair_flat, gate, mixed_rows, w_out, w_up, w_down)
    return result.astype(jnp.bfloat16).reshape(rows, cols, width)


def mix_kernel(edges_ref, out_ref, *, n_col):
    n_dev, _, pairs, rows, lanes = edges_ref.shape
    n_row = n_dev // n_col
    cols = lanes // 2
    parity = (lax.broadcasted_iota(jnp.int32, (1, n_col * lanes), 1) // cols) % 2
    for hp in range(pairs):

        def whole(side):
            return jnp.concatenate(
                [
                    jnp.concatenate([edges_ref[r * n_col + c, side, hp] for c in range(n_col)], axis=1)
                    for r in range(n_row)
                ],
                axis=0,
            )

        left = whole(0)
        right = whole(1)
        right_even = jnp.where(parity == 0, right, jnp.zeros_like(right))
        right_odd = jnp.where(parity == 1, right, jnp.zeros_like(right))
        for c in range(n_col):
            block = slice(c * cols, (c + 1) * cols)
            rhs = jnp.concatenate([right_even[block], right_odd[block]], axis=0)
            mixed = lax.dot_general(
                left, rhs, (((1,), (1,)), ((), ())), preferred_element_type=jnp.float32
            ).astype(out_ref.dtype)
            for r in range(n_row):
                out_ref[r * n_col + c, hp] = mixed[r * rows : (r + 1) * rows]


def body_kernel(pair, mask, w_agate, w_aproj, w_bgate, w_bproj, w_gate, w_out, w_up, w_down, *, n_row, n_col):
    rows, cols, width = pair.shape
    n_dev = n_row * n_col
    pair_flat, gate, left, right = project(pair, mask, w_agate, w_aproj, w_bgate, w_bproj, w_gate)
    hid = left.shape[-1]
    pairs = hid // n_dev // 2

    def chunks(edges):
        edges = jnp.transpose(edges.reshape(rows, cols, n_dev, pairs, 2), (2, 3, 0, 4, 1))
        return edges.reshape(n_dev, pairs, rows, 2 * cols)

    edges = jnp.stack([chunks(left), chunks(right)], axis=1)
    edges = lax.all_to_all(edges, ("row", "col"), split_axis=0, concat_axis=0, tiled=True)
    mixed = pl.pallas_call(
        functools.partial(mix_kernel, n_col=n_col),
        out_shape=jax.ShapeDtypeStruct((n_dev, pairs, rows, 2 * cols), jnp.bfloat16),
    )(edges)
    mixed = lax.all_to_all(mixed, ("row", "col"), split_axis=0, concat_axis=0, tiled=True)
    mixed = jnp.transpose(mixed.reshape(n_dev, pairs, rows, 2, cols), (2, 4, 0, 1, 3))
    mixed_rows = mixed.astype(jnp.float32).reshape(rows * cols, hid)
    result = transition(pair_flat, gate, mixed_rows, w_out, w_up, w_down)
    return result.astype(jnp.bfloat16).reshape(rows, cols, width)


def project_kernel(pair_ref, mask_ref, wag_ref, wap_ref, wbg_ref, wbp_ref, wg_ref, z_ref, gate_ref, *, block):
    rows, cols, width = pair_ref.shape
    quarter = wag_ref.shape[1] // 2

    def paired(w_ref):
        turned = w_ref[...].astype(jnp.float32).T.astype(jnp.bfloat16)
        return jnp.concatenate([turned[:quarter], turned[quarter:]], axis=1)

    w2 = jnp.concatenate([paired(w) for w in (wag_ref, wap_ref, wbg_ref, wbp_ref)], axis=0)

    def rows_of(step, carry):
        first = pl.multiple_of(step * block, block)
        values = pair_ref[pl.ds(first, block)].astype(jnp.float32).reshape(block * cols, width)
        center = values - jnp.mean(values, axis=-1, keepdims=True)
        spread = jnp.mean(center * center, axis=-1, keepdims=True)
        normed = (center * lax.rsqrt(spread + 1e-05)).astype(jnp.bfloat16)
        gate = jax.nn.sigmoid(jnp.dot(normed, wg_ref[...], preferred_element_type=jnp.float32))
        gate_ref[pl.ds(first, block)] = gate.reshape(block, cols, width)
        zeros = jnp.zeros_like(normed)
        top = jnp.concatenate([normed, zeros], axis=1).reshape(block, cols, 2 * width)
        bottom = jnp.concatenate([zeros, normed], axis=1).reshape(block, cols, 2 * width)
        doubled = jnp.concatenate([top, bottom], axis=1).reshape(block * 2 * cols, 2 * width)
        proj = lax.dot_general(
            w2, doubled, (((1,), (1,)), ((), ())), preferred_element_type=jnp.float32
        )
        for i in range(block):
            part = proj[:, i * 2 * cols : (i + 1) * 2 * cols]
            present = mask_ref[pl.ds(first + i, 1), :]
            left = jax.nn.sigmoid(part[0:quarter]) * part[quarter : 2 * quarter] * present
            right = jax.nn.sigmoid(part[2 * quarter : 3 * quarter]) * part[3 * quarter :] * present
            z_ref[first + i] = jnp.concatenate([left, right], axis=0).astype(z_ref.dtype)
        return carry

    lax.fori_loop(0, rows // block, rows_of, 0)


def transition_kernel(mixed_ref, pair_ref, gate_ref, wo_ref, wu_ref, wd_ref, out_ref, *, block):
    rows, cols, width = pair_ref.shape

    def norm(values):
        center = values - jnp.mean(values, axis=-1, keepdims=True)
        spread = jnp.mean(center * center, axis=-1, keepdims=True)
        return center * lax.rsqrt(spread + 1e-05)

    def rows_of(step, carry):
        first = pl.multiple_of(step * block, block)
        mixed = mixed_ref[pl.ds(first, block)].astype(jnp.float32).reshape(block * cols, -1)
        pair = pair_ref[pl.ds(first, block)].astype(jnp.float32).reshape(block * cols, width)
        gate = gate_ref[pl.ds(first, block)].reshape(block * cols, width)
        mixed_normed = norm(mixed).astype(jnp.bfloat16)
        middle = pair + gate * jnp.dot(mixed_normed, wo_ref[...], preferred_element_type=jnp.float32)
        trans_in = norm(middle).astype(jnp.bfloat16)
        hidden = jnp.maximum(jnp.dot(trans_in, wu_ref[...], preferred_element_type=jnp.float32), 0.0)
        result = middle + jnp.dot(hidden.astype(jnp.bfloat16), wd_ref[...], preferred_element_type=jnp.float32)
        out_ref[pl.ds(first, block)] = result.astype(out_ref.dtype).reshape(block, cols, width)
        return carry

    lax.fori_loop(0, rows // block, rows_of, 0)


def body_fused(pair, mask, w_agate, w_aproj, w_bgate, w_bproj, w_gate, w_out, w_up, w_down, *, n_row, n_col):
    rows, cols, width = pair.shape
    n_dev = n_row * n_col
    hid = w_agate.shape[1]
    pairs = hid // n_dev // 2
    present = mask.astype(jnp.float32)
    row_mask = lax.dynamic_slice_in_dim(present, lax.axis_index("row") * rows, rows, 0)
    col_mask = lax.dynamic_slice_in_dim(present, lax.axis_index("col") * cols, cols, 0)
    lane_mask = row_mask[:, None] * jnp.concatenate([col_mask, col_mask])[None, :]

    z, gate = pl.pallas_call(
        functools.partial(project_kernel, block=rows),
        out_shape=(
            jax.ShapeDtypeStruct((rows, hid, 2 * cols), jnp.bfloat16),
            jax.ShapeDtypeStruct((rows, cols, width), jnp.float32),
        ),
    )(pair, lane_mask, w_agate, w_aproj, w_bgate, w_bproj, w_gate)
    edges = jnp.transpose(z.reshape(rows, 2, n_dev, pairs, 2 * cols), (2, 1, 3, 0, 4))
    edges = lax.all_to_all(edges, ("row", "col"), split_axis=0, concat_axis=0, tiled=True)
    mixed = pl.pallas_call(
        functools.partial(mix_kernel, n_col=n_col),
        out_shape=jax.ShapeDtypeStruct((n_dev, pairs, rows, 2 * cols), jnp.bfloat16),
    )(edges)
    mixed = lax.all_to_all(mixed, ("row", "col"), split_axis=0, concat_axis=0, tiled=True)
    mixed = jnp.transpose(mixed.reshape(n_dev, pairs, rows, 2, cols), (2, 4, 3, 0, 1)).reshape(rows, cols, hid)
    return pl.pallas_call(
        functools.partial(transition_kernel, block=rows),
        out_shape=jax.ShapeDtypeStruct((rows, cols, width), jnp.bfloat16),
    )(mixed, pair, gate, w_out, w_up, w_down)


def body_rows(pair, mask, w_agate, w_aproj, w_bgate, w_bproj, w_gate, w_out, w_up, w_down):
    rows, cols, width = pair.shape
    pair_flat, gate, left, right = project(pair, mask, w_agate, w_aproj, w_bgate, w_bproj, w_gate)
    left_major = jnp.transpose(left.reshape(rows, cols, -1), (2, 0, 1))
    right_major = jnp.transpose(right.reshape(rows, cols, -1), (2, 0, 1))
    left_spread, right_spread = (
        lax.all_to_all(
            lax.all_to_all(left_major, "row", split_axis=0, concat_axis=1, tiled=True),
            "col",
            split_axis=1,
            concat_axis=2,
            tiled=True,
        ),
        lax.all_to_all(
            lax.all_to_all(right_major, "row", split_axis=0, concat_axis=1, tiled=True),
            "col",
            split_axis=1,
            concat_axis=2,
            tiled=True,
        ),
    )
    mixed = jnp.einsum(
        "cik,cjk->cij",
        lax.all_gather(left_spread, "col", axis=1, tiled=True),
        right_spread,
        preferred_element_type=jnp.float32,
    ).astype(jnp.bfloat16)
    mixed = lax.all_to_all(mixed, "row", split_axis=1, concat_axis=0, tiled=True)
    mixed_rows = jnp.transpose(mixed, (1, 2, 0)).astype(jnp.float32).reshape(rows * cols, -1)
    result = transition(pair_flat, gate, mixed_rows, w_out, w_up, w_down)
    return result.astype(jnp.bfloat16).reshape(rows, cols, width)


def solution(mesh):
    placed = (P("row", "col", None), P(), P(), P(), P(), P(), P(), P(), P(), P())
    n_row, n_col = mesh.shape["row"], mesh.shape["col"]

    def run(pair, mask, w_agate, *weights):
        hid = w_agate.shape[1]
        rows, cols = pair.shape[0] // n_row, pair.shape[1] // n_col
        if hid % (2 * n_row * n_col) == 0 and 2 * cols == 128 and rows % 16 == 0 and n_row * rows == n_col * cols:
            body = functools.partial(body_fused, n_row=n_row, n_col=n_col)
        elif hid % (n_row * n_col) == 0:
            body = functools.partial(body_split, n_row=n_row, n_col=n_col)
        else:
            body = body_rows
        mapped = jax.shard_map(
            body, mesh=mesh, in_specs=placed, out_specs=P("row", "col", None), check_vma=False
        )
        return mapped(pair, mask, w_agate, *weights)

    return run
```

```python
import functools

import jax
import jax.numpy as jnp
from jax import lax
from jax.experimental import pallas as pl
from jax.experimental.pallas import tpu as pltpu
from jax.sharding import PartitionSpec as P


def layer_norm(values):
    center = values - jnp.mean(values, axis=-1, keepdims=True)
    spread = jnp.mean(center * center, axis=-1, keepdims=True)
    return center * lax.rsqrt(spread + 1e-05)


def project(pair, mask, w_agate, w_aproj, w_bgate, w_bproj, w_gate):
    rows, cols, width = pair.shape
    present = mask.astype(jnp.float32)
    row_start = lax.axis_index("row") * rows
    col_start = lax.axis_index("col") * cols
    row_mask = lax.dynamic_slice_in_dim(present, row_start, rows, 0)
    col_mask = lax.dynamic_slice_in_dim(present, col_start, cols, 0)
    pair_mask = (row_mask[:, None] * col_mask[None, :]).reshape(rows * cols, 1)
    pair_flat = pair.astype(jnp.float32).reshape(rows * cols, width)
    normed = layer_norm(pair_flat).astype(jnp.bfloat16)
    gate = jax.nn.sigmoid(jnp.dot(normed, w_gate, preferred_element_type=jnp.float32))
    left = (
        jax.nn.sigmoid(jnp.dot(normed, w_agate, preferred_element_type=jnp.float32))
        * jnp.dot(normed, w_aproj, preferred_element_type=jnp.float32)
        * pair_mask
    )
    right = (
        jax.nn.sigmoid(jnp.dot(normed, w_bgate, preferred_element_type=jnp.float32))
        * jnp.dot(normed, w_bproj, preferred_element_type=jnp.float32)
        * pair_mask
    )
    return pair_flat, gate, left.astype(jnp.bfloat16), right.astype(jnp.bfloat16)


def transition(pair_flat, gate, mixed_rows, w_out, w_up, w_down):
    mixed_normed = layer_norm(mixed_rows).astype(jnp.bfloat16)
    middle = pair_flat + gate * jnp.dot(mixed_normed, w_out, preferred_element_type=jnp.float32)
    trans_in = layer_norm(middle).astype(jnp.bfloat16)
    trans_hidden = jax.nn.relu(jnp.dot(trans_in, w_up, preferred_element_type=jnp.float32)).astype(
        jnp.bfloat16
    )
    return middle + jnp.dot(trans_hidden, w_down, preferred_element_type=jnp.float32)


def body_split(pair, mask, w_agate, w_aproj, w_bgate, w_bproj, w_gate, w_out, w_up, w_down, *, n_row, n_col):
    rows, cols, width = pair.shape
    n_dev = n_row * n_col
    pair_flat, gate, left, right = project(pair, mask, w_agate, w_aproj, w_bgate, w_bproj, w_gate)
    hid = left.shape[-1]
    group = hid // n_dev
    edges = jnp.stack([left, right], axis=0).reshape(2, rows, cols, n_dev, group)
    edges = jnp.transpose(edges, (3, 0, 4, 1, 2))
    edges = lax.all_to_all(edges, ("row", "col"), split_axis=0, concat_axis=0, tiled=True)
    edges = edges.reshape(n_row, n_col, 2, group, rows, cols)
    edges = jnp.transpose(edges, (2, 3, 0, 4, 1, 5)).reshape(2, group, n_row * rows, n_col * cols)
    mixed = jnp.einsum(
        "cik,cjk->cij", edges[0], edges[1], preferred_element_type=jnp.float32
    ).astype(jnp.bfloat16)
    mixed = mixed.reshape(group, n_row, rows, n_col, cols)
    mixed = jnp.transpose(mixed, (1, 3, 0, 2, 4)).reshape(n_dev, group, rows, cols)
    mixed = lax.all_to_all(mixed, ("row", "col"), split_axis=0, concat_axis=0, tiled=True)
    mixed_rows = jnp.transpose(mixed.reshape(hid, rows, cols), (1, 2, 0))
    mixed_rows = mixed_rows.astype(jnp.float32).reshape(rows * cols, hid)
    result = transition(pair_flat, gate, mixed_rows, w_out, w_up, w_down)
    return result.astype(jnp.bfloat16).reshape(rows, cols, width)


def mix_kernel(edges_ref, out_ref, *, n_col):
    n_dev, _, pairs, rows, lanes = edges_ref.shape
    n_row = n_dev // n_col
    cols = lanes // 2
    parity = (lax.broadcasted_iota(jnp.int32, (1, n_col * lanes), 1) // cols) % 2
    for hp in range(pairs):

        def whole(side):
            return jnp.concatenate(
                [
                    jnp.concatenate([edges_ref[r * n_col + c, side, hp] for c in range(n_col)], axis=1)
                    for r in range(n_row)
                ],
                axis=0,
            )

        left = whole(0)
        right = whole(1)
        right_even = jnp.where(parity == 0, right, jnp.zeros_like(right))
        right_odd = jnp.where(parity == 1, right, jnp.zeros_like(right))
        for c in range(n_col):
            block = slice(c * cols, (c + 1) * cols)
            rhs = jnp.concatenate([right_even[block], right_odd[block]], axis=0)
            mixed = lax.dot_general(
                left, rhs, (((1,), (1,)), ((), ())), preferred_element_type=jnp.float32
            ).astype(out_ref.dtype)
            for r in range(n_row):
                out_ref[r * n_col + c, hp] = mixed[r * rows : (r + 1) * rows]


def body_kernel(pair, mask, w_agate, w_aproj, w_bgate, w_bproj, w_gate, w_out, w_up, w_down, *, n_row, n_col):
    rows, cols, width = pair.shape
    n_dev = n_row * n_col
    pair_flat, gate, left, right = project(pair, mask, w_agate, w_aproj, w_bgate, w_bproj, w_gate)
    hid = left.shape[-1]
    pairs = hid // n_dev // 2

    def chunks(edges):
        edges = jnp.transpose(edges.reshape(rows, cols, n_dev, pairs, 2), (2, 3, 0, 4, 1))
        return edges.reshape(n_dev, pairs, rows, 2 * cols)

    edges = jnp.stack([chunks(left), chunks(right)], axis=1)
    edges = lax.all_to_all(edges, ("row", "col"), split_axis=0, concat_axis=0, tiled=True)
    mixed = pl.pallas_call(
        functools.partial(mix_kernel, n_col=n_col),
        out_shape=jax.ShapeDtypeStruct((n_dev, pairs, rows, 2 * cols), jnp.bfloat16),
    )(edges)
    mixed = lax.all_to_all(mixed, ("row", "col"), split_axis=0, concat_axis=0, tiled=True)
    mixed = jnp.transpose(mixed.reshape(n_dev, pairs, rows, 2, cols), (2, 4, 0, 1, 3))
    mixed_rows = mixed.astype(jnp.float32).reshape(rows * cols, hid)
    result = transition(pair_flat, gate, mixed_rows, w_out, w_up, w_down)
    return result.astype(jnp.bfloat16).reshape(rows, cols, width)


def project_kernel(mask_ref, pair_ref, wag_ref, wap_ref, wbg_ref, wbp_ref, wg_ref, z_ref, gate_ref, *, block):
    rows, cols, width = pair_ref.shape
    quarter = wag_ref.shape[1] // 2

    def paired(w_ref):
        turned = w_ref[...].astype(jnp.float32).T.astype(jnp.bfloat16)
        return jnp.concatenate([turned[:quarter], turned[quarter:]], axis=1)

    w2 = jnp.concatenate([paired(w) for w in (wag_ref, wap_ref, wbg_ref, wbp_ref)], axis=0)
    row_start = lax.axis_index("row") * rows
    col_start = lax.axis_index("col") * cols
    lane = lax.broadcasted_iota(jnp.int32, (1, 2 * cols), 1) % cols
    col_mask = jnp.zeros((1, 2 * cols), jnp.float32)
    for k in range(cols):
        col_mask = jnp.where(lane == k, mask_ref[col_start + k].astype(jnp.float32), col_mask)

    def rows_of(step, carry):
        first = pl.multiple_of(step * block, block)
        values = pair_ref[pl.ds(first, block)].astype(jnp.float32).reshape(block * cols, width)
        center = values - jnp.mean(values, axis=-1, keepdims=True)
        spread = jnp.mean(center * center, axis=-1, keepdims=True)
        normed = (center * lax.rsqrt(spread + 1e-05)).astype(jnp.bfloat16)
        gate = jax.nn.sigmoid(jnp.dot(normed, wg_ref[...], preferred_element_type=jnp.float32))
        gate_ref[pl.ds(first, block)] = gate.reshape(block, cols, width)
        zeros = jnp.zeros_like(normed)
        top = jnp.concatenate([normed, zeros], axis=1).reshape(block, cols, 2 * width)
        bottom = jnp.concatenate([zeros, normed], axis=1).reshape(block, cols, 2 * width)
        doubled = jnp.concatenate([top, bottom], axis=1).reshape(block * 2 * cols, 2 * width)
        proj = lax.dot_general(
            w2, doubled, (((1,), (1,)), ((), ())), preferred_element_type=jnp.float32
        )
        for i in range(block):
            part = proj[:, i * 2 * cols : (i + 1) * 2 * cols]
            present = col_mask * mask_ref[row_start + first + i].astype(jnp.float32)
            left = jax.nn.sigmoid(part[0:quarter]) * part[quarter : 2 * quarter] * present
            right = jax.nn.sigmoid(part[2 * quarter : 3 * quarter]) * part[3 * quarter :] * present
            z_ref[first + i] = jnp.concatenate([left, right], axis=0).astype(z_ref.dtype)
        return carry

    lax.fori_loop(0, rows // block, rows_of, 0)


def transition_kernel(mixed_ref, pair_ref, gate_ref, wo_ref, wu_ref, wd_ref, out_ref, *, block):
    rows, cols, width = pair_ref.shape

    def norm(values):
        center = values - jnp.mean(values, axis=-1, keepdims=True)
        spread = jnp.mean(center * center, axis=-1, keepdims=True)
        return center * lax.rsqrt(spread + 1e-05)

    def rows_of(step, carry):
        first = pl.multiple_of(step * block, block)
        mixed = mixed_ref[pl.ds(first, block)].astype(jnp.float32).reshape(block * cols, -1)
        pair = pair_ref[pl.ds(first, block)].astype(jnp.float32).reshape(block * cols, width)
        gate = gate_ref[pl.ds(first, block)].reshape(block * cols, width)
        mixed_normed = norm(mixed).astype(jnp.bfloat16)
        middle = pair + gate * jnp.dot(mixed_normed, wo_ref[...], preferred_element_type=jnp.float32)
        trans_in = norm(middle).astype(jnp.bfloat16)
        hidden = jnp.maximum(jnp.dot(trans_in, wu_ref[...], preferred_element_type=jnp.float32), 0.0)
        result = middle + jnp.dot(hidden.astype(jnp.bfloat16), wd_ref[...], preferred_element_type=jnp.float32)
        out_ref[pl.ds(first, block)] = result.astype(out_ref.dtype).reshape(block, cols, width)
        return carry

    lax.fori_loop(0, rows // block, rows_of, 0)


def body_fused(pair, mask, w_agate, w_aproj, w_bgate, w_bproj, w_gate, w_out, w_up, w_down, *, n_row, n_col):
    rows, cols, width = pair.shape
    n_dev = n_row * n_col
    hid = w_agate.shape[1]
    pairs = hid // n_dev // 2

    z, gate = pl.pallas_call(
        functools.partial(project_kernel, block=rows),
        out_shape=(
            jax.ShapeDtypeStruct((rows, hid, 2 * cols), jnp.bfloat16),
            jax.ShapeDtypeStruct((rows, cols, width), jnp.float32),
        ),
        in_specs=[pl.BlockSpec(memory_space=pltpu.SMEM)] + [pl.BlockSpec(memory_space=pltpu.VMEM)] * 6,
    )(mask, pair, w_agate, w_aproj, w_bgate, w_bproj, w_gate)
    edges = jnp.transpose(z.reshape(rows, 2, n_dev, pairs, 2 * cols), (2, 1, 3, 0, 4))
    edges = lax.all_to_all(edges, ("row", "col"), split_axis=0, concat_axis=0, tiled=True)
    mixed = pl.pallas_call(
        functools.partial(mix_kernel, n_col=n_col),
        out_shape=jax.ShapeDtypeStruct((n_dev, pairs, rows, 2 * cols), jnp.bfloat16),
    )(edges)
    mixed = lax.all_to_all(mixed, ("row", "col"), split_axis=0, concat_axis=0, tiled=True)
    mixed = jnp.transpose(mixed.reshape(n_dev, pairs, rows, 2, cols), (2, 4, 3, 0, 1)).reshape(rows, cols, hid)
    return pl.pallas_call(
        functools.partial(transition_kernel, block=rows),
        out_shape=jax.ShapeDtypeStruct((rows, cols, width), jnp.bfloat16),
    )(mixed, pair, gate, w_out, w_up, w_down)


def body_rows(pair, mask, w_agate, w_aproj, w_bgate, w_bproj, w_gate, w_out, w_up, w_down):
    rows, cols, width = pair.shape
    pair_flat, gate, left, right = project(pair, mask, w_agate, w_aproj, w_bgate, w_bproj, w_gate)
    left_major = jnp.transpose(left.reshape(rows, cols, -1), (2, 0, 1))
    right_major = jnp.transpose(right.reshape(rows, cols, -1), (2, 0, 1))
    left_spread, right_spread = (
        lax.all_to_all(
            lax.all_to_all(left_major, "row", split_axis=0, concat_axis=1, tiled=True),
            "col",
            split_axis=1,
            concat_axis=2,
            tiled=True,
        ),
        lax.all_to_all(
            lax.all_to_all(right_major, "row", split_axis=0, concat_axis=1, tiled=True),
            "col",
            split_axis=1,
            concat_axis=2,
            tiled=True,
        ),
    )
    mixed = jnp.einsum(
        "cik,cjk->cij",
        lax.all_gather(left_spread, "col", axis=1, tiled=True),
        right_spread,
        preferred_element_type=jnp.float32,
    ).astype(jnp.bfloat16)
    mixed = lax.all_to_all(mixed, "row", split_axis=1, concat_axis=0, tiled=True)
    mixed_rows = jnp.transpose(mixed, (1, 2, 0)).astype(jnp.float32).reshape(rows * cols, -1)
    result = transition(pair_flat, gate, mixed_rows, w_out, w_up, w_down)
    return result.astype(jnp.bfloat16).reshape(rows, cols, width)


def solution(mesh):
    placed = (P("row", "col", None), P(), P(), P(), P(), P(), P(), P(), P(), P())
    n_row, n_col = mesh.shape["row"], mesh.shape["col"]

    def run(pair, mask, w_agate, *weights):
        hid = w_agate.shape[1]
        rows, cols = pair.shape[0] // n_row, pair.shape[1] // n_col
        if hid % (2 * n_row * n_col) == 0 and 2 * cols == 128 and rows % 16 == 0 and n_row * rows == n_col * cols:
            body = functools.partial(body_fused, n_row=n_row, n_col=n_col)
        elif hid % (n_row * n_col) == 0:
            body = functools.partial(body_split, n_row=n_row, n_col=n_col)
        else:
            body = body_rows
        mapped = jax.shard_map(
            body, mesh=mesh, in_specs=placed, out_specs=P("row", "col", None), check_vma=False
        )
        return mapped(pair, mask, w_agate, *weights)

    return run
```

```python
import functools

import jax
import jax.numpy as jnp
from jax import lax
from jax.experimental import pallas as pl
from jax.experimental.pallas import tpu as pltpu
from jax.sharding import PartitionSpec as P


def layer_norm(values):
    center = values - jnp.mean(values, axis=-1, keepdims=True)
    spread = jnp.mean(center * center, axis=-1, keepdims=True)
    return center * lax.rsqrt(spread + 1e-05)


def project(pair, mask, w_agate, w_aproj, w_bgate, w_bproj, w_gate):
    rows, cols, width = pair.shape
    present = mask.astype(jnp.float32)
    row_start = lax.axis_index("row") * rows
    col_start = lax.axis_index("col") * cols
    row_mask = lax.dynamic_slice_in_dim(present, row_start, rows, 0)
    col_mask = lax.dynamic_slice_in_dim(present, col_start, cols, 0)
    pair_mask = (row_mask[:, None] * col_mask[None, :]).reshape(rows * cols, 1)
    pair_flat = pair.astype(jnp.float32).reshape(rows * cols, width)
    normed = layer_norm(pair_flat).astype(jnp.bfloat16)
    gate = jax.nn.sigmoid(jnp.dot(normed, w_gate, preferred_element_type=jnp.float32))
    left = (
        jax.nn.sigmoid(jnp.dot(normed, w_agate, preferred_element_type=jnp.float32))
        * jnp.dot(normed, w_aproj, preferred_element_type=jnp.float32)
        * pair_mask
    )
    right = (
        jax.nn.sigmoid(jnp.dot(normed, w_bgate, preferred_element_type=jnp.float32))
        * jnp.dot(normed, w_bproj, preferred_element_type=jnp.float32)
        * pair_mask
    )
    return pair_flat, gate, left.astype(jnp.bfloat16), right.astype(jnp.bfloat16)


def transition(pair_flat, gate, mixed_rows, w_out, w_up, w_down):
    mixed_normed = layer_norm(mixed_rows).astype(jnp.bfloat16)
    middle = pair_flat + gate * jnp.dot(mixed_normed, w_out, preferred_element_type=jnp.float32)
    trans_in = layer_norm(middle).astype(jnp.bfloat16)
    trans_hidden = jax.nn.relu(jnp.dot(trans_in, w_up, preferred_element_type=jnp.float32)).astype(
        jnp.bfloat16
    )
    return middle + jnp.dot(trans_hidden, w_down, preferred_element_type=jnp.float32)


def body_split(pair, mask, w_agate, w_aproj, w_bgate, w_bproj, w_gate, w_out, w_up, w_down, *, n_row, n_col):
    rows, cols, width = pair.shape
    n_dev = n_row * n_col
    pair_flat, gate, left, right = project(pair, mask, w_agate, w_aproj, w_bgate, w_bproj, w_gate)
    hid = left.shape[-1]
    group = hid // n_dev
    edges = jnp.stack([left, right], axis=0).reshape(2, rows, cols, n_dev, group)
    edges = jnp.transpose(edges, (3, 0, 4, 1, 2))
    edges = lax.all_to_all(edges, ("row", "col"), split_axis=0, concat_axis=0, tiled=True)
    edges = edges.reshape(n_row, n_col, 2, group, rows, cols)
    edges = jnp.transpose(edges, (2, 3, 0, 4, 1, 5)).reshape(2, group, n_row * rows, n_col * cols)
    mixed = jnp.einsum(
        "cik,cjk->cij", edges[0], edges[1], preferred_element_type=jnp.float32
    ).astype(jnp.bfloat16)
    mixed = mixed.reshape(group, n_row, rows, n_col, cols)
    mixed = jnp.transpose(mixed, (1, 3, 0, 2, 4)).reshape(n_dev, group, rows, cols)
    mixed = lax.all_to_all(mixed, ("row", "col"), split_axis=0, concat_axis=0, tiled=True)
    mixed_rows = jnp.transpose(mixed.reshape(hid, rows, cols), (1, 2, 0))
    mixed_rows = mixed_rows.astype(jnp.float32).reshape(rows * cols, hid)
    result = transition(pair_flat, gate, mixed_rows, w_out, w_up, w_down)
    return result.astype(jnp.bfloat16).reshape(rows, cols, width)


def mix_kernel(edges_ref, out_ref, *, n_col):
    n_dev, _, pairs, rows, lanes = edges_ref.shape
    n_row = n_dev // n_col
    cols = lanes // 2
    parity = (lax.broadcasted_iota(jnp.int32, (1, n_col * lanes), 1) // cols) % 2
    for hp in range(pairs):

        def whole(side):
            return jnp.concatenate(
                [
                    jnp.concatenate([edges_ref[r * n_col + c, side, hp] for c in range(n_col)], axis=1)
                    for r in range(n_row)
                ],
                axis=0,
            )

        left = whole(0)
        right = whole(1)
        right_even = jnp.where(parity == 0, right, jnp.zeros_like(right))
        right_odd = jnp.where(parity == 1, right, jnp.zeros_like(right))
        for c in range(n_col):
            block = slice(c * cols, (c + 1) * cols)
            rhs = jnp.concatenate([right_even[block], right_odd[block]], axis=0)
            mixed = lax.dot_general(
                left, rhs, (((1,), (1,)), ((), ())), preferred_element_type=jnp.float32
            ).astype(out_ref.dtype)
            for r in range(n_row):
                out_ref[r * n_col + c, hp] = mixed[r * rows : (r + 1) * rows]


def body_kernel(pair, mask, w_agate, w_aproj, w_bgate, w_bproj, w_gate, w_out, w_up, w_down, *, n_row, n_col):
    rows, cols, width = pair.shape
    n_dev = n_row * n_col
    pair_flat, gate, left, right = project(pair, mask, w_agate, w_aproj, w_bgate, w_bproj, w_gate)
    hid = left.shape[-1]
    pairs = hid // n_dev // 2

    def chunks(edges):
        edges = jnp.transpose(edges.reshape(rows, cols, n_dev, pairs, 2), (2, 3, 0, 4, 1))
        return edges.reshape(n_dev, pairs, rows, 2 * cols)

    edges = jnp.stack([chunks(left), chunks(right)], axis=1)
    edges = lax.all_to_all(edges, ("row", "col"), split_axis=0, concat_axis=0, tiled=True)
    mixed = pl.pallas_call(
        functools.partial(mix_kernel, n_col=n_col),
        out_shape=jax.ShapeDtypeStruct((n_dev, pairs, rows, 2 * cols), jnp.bfloat16),
    )(edges)
    mixed = lax.all_to_all(mixed, ("row", "col"), split_axis=0, concat_axis=0, tiled=True)
    mixed = jnp.transpose(mixed.reshape(n_dev, pairs, rows, 2, cols), (2, 4, 0, 1, 3))
    mixed_rows = mixed.astype(jnp.float32).reshape(rows * cols, hid)
    result = transition(pair_flat, gate, mixed_rows, w_out, w_up, w_down)
    return result.astype(jnp.bfloat16).reshape(rows, cols, width)


def project_kernel(mask_ref, pair_ref, wag_ref, wap_ref, wbg_ref, wbp_ref, z_ref, *, block):
    rows, cols, width = pair_ref.shape
    quarter = wag_ref.shape[1] // 2

    def paired(w_ref):
        turned = w_ref[...].astype(jnp.float32).T.astype(jnp.bfloat16)
        return jnp.concatenate([turned[:quarter], turned[quarter:]], axis=1)

    w2 = jnp.concatenate([paired(w) for w in (wag_ref, wap_ref, wbg_ref, wbp_ref)], axis=0)
    row_start = lax.axis_index("row") * rows
    col_start = lax.axis_index("col") * cols
    lane = lax.broadcasted_iota(jnp.int32, (1, 2 * cols), 1) % cols
    col_mask = jnp.zeros((1, 2 * cols), jnp.float32)
    for k in range(cols):
        col_mask = jnp.where(lane == k, mask_ref[col_start + k].astype(jnp.float32), col_mask)

    def rows_of(step, carry):
        first = pl.multiple_of(step * block, block)
        values = pair_ref[pl.ds(first, block)].astype(jnp.float32).reshape(block * cols, width)
        center = values - jnp.mean(values, axis=-1, keepdims=True)
        spread = jnp.mean(center * center, axis=-1, keepdims=True)
        normed = (center * lax.rsqrt(spread + 1e-05)).astype(jnp.bfloat16)
        zeros = jnp.zeros_like(normed)
        top = jnp.concatenate([normed, zeros], axis=1).reshape(block, cols, 2 * width)
        bottom = jnp.concatenate([zeros, normed], axis=1).reshape(block, cols, 2 * width)
        doubled = jnp.concatenate([top, bottom], axis=1).reshape(block * 2 * cols, 2 * width)
        proj = lax.dot_general(
            w2, doubled, (((1,), (1,)), ((), ())), preferred_element_type=jnp.float32
        )
        for i in range(block):
            part = proj[:, i * 2 * cols : (i + 1) * 2 * cols]
            present = col_mask * mask_ref[row_start + first + i].astype(jnp.float32)
            left = jax.nn.sigmoid(part[0:quarter]) * part[quarter : 2 * quarter] * present
            right = jax.nn.sigmoid(part[2 * quarter : 3 * quarter]) * part[3 * quarter :] * present
            z_ref[first + i] = jnp.concatenate([left, right], axis=0).astype(z_ref.dtype)
        return carry

    lax.fori_loop(0, rows // block, rows_of, 0)


def gate_kernel(pair_ref, wg_ref, gate_ref):
    rows, cols, width = pair_ref.shape
    values = pair_ref[...].astype(jnp.float32).reshape(rows * cols, width)
    center = values - jnp.mean(values, axis=-1, keepdims=True)
    spread = jnp.mean(center * center, axis=-1, keepdims=True)
    normed = (center * lax.rsqrt(spread + 1e-05)).astype(jnp.bfloat16)
    gate = jax.nn.sigmoid(jnp.dot(normed, wg_ref[...], preferred_element_type=jnp.float32))
    gate_ref[...] = gate.reshape(rows, cols, width)


def transition_kernel(mixed_ref, pair_ref, gate_ref, wo_ref, wu_ref, wd_ref, out_ref, *, block):
    rows, cols, width = pair_ref.shape

    def norm(values):
        center = values - jnp.mean(values, axis=-1, keepdims=True)
        spread = jnp.mean(center * center, axis=-1, keepdims=True)
        return center * lax.rsqrt(spread + 1e-05)

    def rows_of(step, carry):
        first = pl.multiple_of(step * block, block)
        mixed = mixed_ref[pl.ds(first, block)].astype(jnp.float32).reshape(block * cols, -1)
        pair = pair_ref[pl.ds(first, block)].astype(jnp.float32).reshape(block * cols, width)
        gate = gate_ref[pl.ds(first, block)].reshape(block * cols, width)
        mixed_normed = norm(mixed).astype(jnp.bfloat16)
        middle = pair + gate * jnp.dot(mixed_normed, wo_ref[...], preferred_element_type=jnp.float32)
        trans_in = norm(middle).astype(jnp.bfloat16)
        hidden = jnp.maximum(jnp.dot(trans_in, wu_ref[...], preferred_element_type=jnp.float32), 0.0)
        result = middle + jnp.dot(hidden.astype(jnp.bfloat16), wd_ref[...], preferred_element_type=jnp.float32)
        out_ref[pl.ds(first, block)] = result.astype(out_ref.dtype).reshape(block, cols, width)
        return carry

    lax.fori_loop(0, rows // block, rows_of, 0)


def body_fused(pair, mask, w_agate, w_aproj, w_bgate, w_bproj, w_gate, w_out, w_up, w_down, *, n_row, n_col):
    rows, cols, width = pair.shape
    n_dev = n_row * n_col
    hid = w_agate.shape[1]
    pairs = hid // n_dev // 2

    z = pl.pallas_call(
        functools.partial(project_kernel, block=rows),
        out_shape=jax.ShapeDtypeStruct((rows, hid, 2 * cols), jnp.bfloat16),
        in_specs=[pl.BlockSpec(memory_space=pltpu.SMEM)] + [pl.BlockSpec(memory_space=pltpu.VMEM)] * 5,
    )(mask, pair, w_agate, w_aproj, w_bgate, w_bproj)
    gate = pl.pallas_call(
        gate_kernel, out_shape=jax.ShapeDtypeStruct((rows, cols, width), jnp.float32)
    )(pair, w_gate)
    edges = jnp.transpose(z.reshape(rows, 2, n_dev, pairs, 2 * cols), (2, 1, 3, 0, 4))
    edges = lax.all_to_all(edges, ("row", "col"), split_axis=0, concat_axis=0, tiled=True)
    mixed = pl.pallas_call(
        functools.partial(mix_kernel, n_col=n_col),
        out_shape=jax.ShapeDtypeStruct((n_dev, pairs, rows, 2 * cols), jnp.bfloat16),
    )(edges)
    mixed = lax.all_to_all(mixed, ("row", "col"), split_axis=0, concat_axis=0, tiled=True)
    mixed = jnp.transpose(mixed.reshape(n_dev, pairs, rows, 2, cols), (2, 4, 3, 0, 1)).reshape(rows, cols, hid)
    return pl.pallas_call(
        functools.partial(transition_kernel, block=rows),
        out_shape=jax.ShapeDtypeStruct((rows, cols, width), jnp.bfloat16),
    )(mixed, pair, gate, w_out, w_up, w_down)


def body_rows(pair, mask, w_agate, w_aproj, w_bgate, w_bproj, w_gate, w_out, w_up, w_down):
    rows, cols, width = pair.shape
    pair_flat, gate, left, right = project(pair, mask, w_agate, w_aproj, w_bgate, w_bproj, w_gate)
    left_major = jnp.transpose(left.reshape(rows, cols, -1), (2, 0, 1))
    right_major = jnp.transpose(right.reshape(rows, cols, -1), (2, 0, 1))
    left_spread, right_spread = (
        lax.all_to_all(
            lax.all_to_all(left_major, "row", split_axis=0, concat_axis=1, tiled=True),
            "col",
            split_axis=1,
            concat_axis=2,
            tiled=True,
        ),
        lax.all_to_all(
            lax.all_to_all(right_major, "row", split_axis=0, concat_axis=1, tiled=True),
            "col",
            split_axis=1,
            concat_axis=2,
            tiled=True,
        ),
    )
    mixed = jnp.einsum(
        "cik,cjk->cij",
        lax.all_gather(left_spread, "col", axis=1, tiled=True),
        right_spread,
        preferred_element_type=jnp.float32,
    ).astype(jnp.bfloat16)
    mixed = lax.all_to_all(mixed, "row", split_axis=1, concat_axis=0, tiled=True)
    mixed_rows = jnp.transpose(mixed, (1, 2, 0)).astype(jnp.float32).reshape(rows * cols, -1)
    result = transition(pair_flat, gate, mixed_rows, w_out, w_up, w_down)
    return result.astype(jnp.bfloat16).reshape(rows, cols, width)


def solution(mesh):
    placed = (P("row", "col", None), P(), P(), P(), P(), P(), P(), P(), P(), P())
    n_row, n_col = mesh.shape["row"], mesh.shape["col"]

    def run(pair, mask, w_agate, *weights):
        hid = w_agate.shape[1]
        rows, cols = pair.shape[0] // n_row, pair.shape[1] // n_col
        if hid % (2 * n_row * n_col) == 0 and 2 * cols == 128 and rows % 16 == 0 and n_row * rows == n_col * cols:
            body = functools.partial(body_fused, n_row=n_row, n_col=n_col)
        elif hid % (n_row * n_col) == 0:
            body = functools.partial(body_split, n_row=n_row, n_col=n_col)
        else:
            body = body_rows
        mapped = jax.shard_map(
            body, mesh=mesh, in_specs=placed, out_specs=P("row", "col", None), check_vma=False
        )
        return mapped(pair, mask, w_agate, *weights)

    return run
```

```python
import functools

import jax
import jax.numpy as jnp
from jax import lax
from jax.experimental import pallas as pl
from jax.experimental.pallas import tpu as pltpu
from jax.sharding import PartitionSpec as P


def layer_norm(values):
    center = values - jnp.mean(values, axis=-1, keepdims=True)
    spread = jnp.mean(center * center, axis=-1, keepdims=True)
    return center * lax.rsqrt(spread + 1e-05)


def project(pair, mask, w_agate, w_aproj, w_bgate, w_bproj, w_gate):
    rows, cols, width = pair.shape
    present = mask.astype(jnp.float32)
    row_start = lax.axis_index("row") * rows
    col_start = lax.axis_index("col") * cols
    row_mask = lax.dynamic_slice_in_dim(present, row_start, rows, 0)
    col_mask = lax.dynamic_slice_in_dim(present, col_start, cols, 0)
    pair_mask = (row_mask[:, None] * col_mask[None, :]).reshape(rows * cols, 1)
    pair_flat = pair.astype(jnp.float32).reshape(rows * cols, width)
    normed = layer_norm(pair_flat).astype(jnp.bfloat16)
    gate = jax.nn.sigmoid(jnp.dot(normed, w_gate, preferred_element_type=jnp.float32))
    left = (
        jax.nn.sigmoid(jnp.dot(normed, w_agate, preferred_element_type=jnp.float32))
        * jnp.dot(normed, w_aproj, preferred_element_type=jnp.float32)
        * pair_mask
    )
    right = (
        jax.nn.sigmoid(jnp.dot(normed, w_bgate, preferred_element_type=jnp.float32))
        * jnp.dot(normed, w_bproj, preferred_element_type=jnp.float32)
        * pair_mask
    )
    return pair_flat, gate, left.astype(jnp.bfloat16), right.astype(jnp.bfloat16)


def transition(pair_flat, gate, mixed_rows, w_out, w_up, w_down):
    mixed_normed = layer_norm(mixed_rows).astype(jnp.bfloat16)
    middle = pair_flat + gate * jnp.dot(mixed_normed, w_out, preferred_element_type=jnp.float32)
    trans_in = layer_norm(middle).astype(jnp.bfloat16)
    trans_hidden = jax.nn.relu(jnp.dot(trans_in, w_up, preferred_element_type=jnp.float32)).astype(
        jnp.bfloat16
    )
    return middle + jnp.dot(trans_hidden, w_down, preferred_element_type=jnp.float32)


def body_split(pair, mask, w_agate, w_aproj, w_bgate, w_bproj, w_gate, w_out, w_up, w_down, *, n_row, n_col):
    rows, cols, width = pair.shape
    n_dev = n_row * n_col
    pair_flat, gate, left, right = project(pair, mask, w_agate, w_aproj, w_bgate, w_bproj, w_gate)
    hid = left.shape[-1]
    group = hid // n_dev
    edges = jnp.stack([left, right], axis=0).reshape(2, rows, cols, n_dev, group)
    edges = jnp.transpose(edges, (3, 0, 4, 1, 2))
    edges = lax.all_to_all(edges, ("row", "col"), split_axis=0, concat_axis=0, tiled=True)
    edges = edges.reshape(n_row, n_col, 2, group, rows, cols)
    edges = jnp.transpose(edges, (2, 3, 0, 4, 1, 5)).reshape(2, group, n_row * rows, n_col * cols)
    mixed = jnp.einsum(
        "cik,cjk->cij", edges[0], edges[1], preferred_element_type=jnp.float32
    ).astype(jnp.bfloat16)
    mixed = mixed.reshape(group, n_row, rows, n_col, cols)
    mixed = jnp.transpose(mixed, (1, 3, 0, 2, 4)).reshape(n_dev, group, rows, cols)
    mixed = lax.all_to_all(mixed, ("row", "col"), split_axis=0, concat_axis=0, tiled=True)
    mixed_rows = jnp.transpose(mixed.reshape(hid, rows, cols), (1, 2, 0))
    mixed_rows = mixed_rows.astype(jnp.float32).reshape(rows * cols, hid)
    result = transition(pair_flat, gate, mixed_rows, w_out, w_up, w_down)
    return result.astype(jnp.bfloat16).reshape(rows, cols, width)


def mix_kernel(edges_ref, out_ref, *, n_col):
    n_dev, _, pairs, rows, lanes = edges_ref.shape
    n_row = n_dev // n_col
    cols = lanes // 2
    parity = (lax.broadcasted_iota(jnp.int32, (1, n_col * lanes), 1) // cols) % 2
    for hp in range(pairs):

        def whole(side):
            return jnp.concatenate(
                [
                    jnp.concatenate([edges_ref[r * n_col + c, side, hp] for c in range(n_col)], axis=1)
                    for r in range(n_row)
                ],
                axis=0,
            )

        left = whole(0)
        right = whole(1)
        right_even = jnp.where(parity == 0, right, jnp.zeros_like(right))
        right_odd = jnp.where(parity == 1, right, jnp.zeros_like(right))
        for c in range(n_col):
            block = slice(c * cols, (c + 1) * cols)
            rhs = jnp.concatenate([right_even[block], right_odd[block]], axis=0)
            mixed = lax.dot_general(
                left, rhs, (((1,), (1,)), ((), ())), preferred_element_type=jnp.float32
            ).astype(out_ref.dtype)
            for r in range(n_row):
                out_ref[r * n_col + c, hp] = mixed[r * rows : (r + 1) * rows]


def body_kernel(pair, mask, w_agate, w_aproj, w_bgate, w_bproj, w_gate, w_out, w_up, w_down, *, n_row, n_col):
    rows, cols, width = pair.shape
    n_dev = n_row * n_col
    pair_flat, gate, left, right = project(pair, mask, w_agate, w_aproj, w_bgate, w_bproj, w_gate)
    hid = left.shape[-1]
    pairs = hid // n_dev // 2

    def chunks(edges):
        edges = jnp.transpose(edges.reshape(rows, cols, n_dev, pairs, 2), (2, 3, 0, 4, 1))
        return edges.reshape(n_dev, pairs, rows, 2 * cols)

    edges = jnp.stack([chunks(left), chunks(right)], axis=1)
    edges = lax.all_to_all(edges, ("row", "col"), split_axis=0, concat_axis=0, tiled=True)
    mixed = pl.pallas_call(
        functools.partial(mix_kernel, n_col=n_col),
        out_shape=jax.ShapeDtypeStruct((n_dev, pairs, rows, 2 * cols), jnp.bfloat16),
    )(edges)
    mixed = lax.all_to_all(mixed, ("row", "col"), split_axis=0, concat_axis=0, tiled=True)
    mixed = jnp.transpose(mixed.reshape(n_dev, pairs, rows, 2, cols), (2, 4, 0, 1, 3))
    mixed_rows = mixed.astype(jnp.float32).reshape(rows * cols, hid)
    result = transition(pair_flat, gate, mixed_rows, w_out, w_up, w_down)
    return result.astype(jnp.bfloat16).reshape(rows, cols, width)


def project_kernel(mask_ref, pair_ref, wag_ref, wap_ref, wbg_ref, wbp_ref, z_ref, *, block):
    rows, cols, width = pair_ref.shape
    quarter = wag_ref.shape[1] // 2

    def paired(w_ref):
        turned = w_ref[...].astype(jnp.float32).T.astype(jnp.bfloat16)
        return jnp.concatenate([turned[:quarter], turned[quarter:]], axis=1)

    w2 = jnp.concatenate([paired(w) for w in (wag_ref, wap_ref, wbg_ref, wbp_ref)], axis=0)
    row_start = lax.axis_index("row") * rows
    col_start = lax.axis_index("col") * cols
    lane = lax.broadcasted_iota(jnp.int32, (1, 2 * cols), 1) % cols
    col_mask = jnp.zeros((1, 2 * cols), jnp.float32)
    for k in range(cols):
        col_mask = jnp.where(lane == k, mask_ref[col_start + k].astype(jnp.float32), col_mask)

    def rows_of(step, carry):
        first = pl.multiple_of(step * block, block)
        values = pair_ref[pl.ds(first, block)].astype(jnp.float32).reshape(block * cols, width)
        center = values - jnp.mean(values, axis=-1, keepdims=True)
        spread = jnp.mean(center * center, axis=-1, keepdims=True)
        normed = (center * lax.rsqrt(spread + 1e-05)).astype(jnp.bfloat16)
        zeros = jnp.zeros_like(normed)
        top = jnp.concatenate([normed, zeros], axis=1).reshape(block, cols, 2 * width)
        bottom = jnp.concatenate([zeros, normed], axis=1).reshape(block, cols, 2 * width)
        doubled = jnp.concatenate([top, bottom], axis=1).reshape(block * 2 * cols, 2 * width)
        proj = lax.dot_general(
            w2, doubled, (((1,), (1,)), ((), ())), preferred_element_type=jnp.float32
        )
        for i in range(block):
            part = proj[:, i * 2 * cols : (i + 1) * 2 * cols]
            present = col_mask * mask_ref[row_start + first + i].astype(jnp.float32)
            left = jax.nn.sigmoid(part[0:quarter]) * part[quarter : 2 * quarter] * present
            right = jax.nn.sigmoid(part[2 * quarter : 3 * quarter]) * part[3 * quarter :] * present
            z_ref[first + i] = jnp.concatenate([left, right], axis=0).astype(z_ref.dtype)
        return carry

    lax.fori_loop(0, rows // block, rows_of, 0)


def gate_kernel(pair_ref, wg_ref, gate_ref):
    rows, cols, width = pair_ref.shape
    values = pair_ref[...].astype(jnp.float32).reshape(rows * cols, width)
    center = values - jnp.mean(values, axis=-1, keepdims=True)
    spread = jnp.mean(center * center, axis=-1, keepdims=True)
    normed = (center * lax.rsqrt(spread + 1e-05)).astype(jnp.bfloat16)
    gate = jax.nn.sigmoid(jnp.dot(normed, wg_ref[...], preferred_element_type=jnp.float32))
    gate_ref[...] = gate.reshape(rows, cols, width)


def transition_kernel(mixed_ref, pair_ref, gate_ref, wo_ref, wu_ref, wd_ref, out_ref):
    rows, cols, width = pair_ref.shape
    pairs = mixed_ref.shape[0] // rows

    def norm(values):
        center = values - jnp.mean(values, axis=-1, keepdims=True)
        spread = jnp.mean(center * center, axis=-1, keepdims=True)
        return center * lax.rsqrt(spread + 1e-05)

    parts = []
    for i in range(rows):
        turned = mixed_ref[pl.ds(i, pairs, stride=rows), :].astype(jnp.float32).T
        parts.append(jnp.concatenate([turned[:cols], turned[cols:]], axis=1))
    mixed = jnp.concatenate(parts, axis=0)
    pair = pair_ref[...].astype(jnp.float32).reshape(rows * cols, width)
    gate = gate_ref[...].reshape(rows * cols, width)
    mixed_normed = norm(mixed).astype(jnp.bfloat16)
    middle = pair + gate * jnp.dot(mixed_normed, wo_ref[...], preferred_element_type=jnp.float32)
    trans_in = norm(middle).astype(jnp.bfloat16)
    hidden = jnp.maximum(jnp.dot(trans_in, wu_ref[...], preferred_element_type=jnp.float32), 0.0)
    result = middle + jnp.dot(hidden.astype(jnp.bfloat16), wd_ref[...], preferred_element_type=jnp.float32)
    out_ref[...] = result.astype(out_ref.dtype).reshape(rows, cols, width)


def body_fused(pair, mask, w_agate, w_aproj, w_bgate, w_bproj, w_gate, w_out, w_up, w_down, *, n_row, n_col):
    rows, cols, width = pair.shape
    n_dev = n_row * n_col
    hid = w_agate.shape[1]
    pairs = hid // n_dev // 2

    z = pl.pallas_call(
        functools.partial(project_kernel, block=rows),
        out_shape=jax.ShapeDtypeStruct((rows, hid, 2 * cols), jnp.bfloat16),
        in_specs=[pl.BlockSpec(memory_space=pltpu.SMEM)] + [pl.BlockSpec(memory_space=pltpu.VMEM)] * 5,
    )(mask, pair, w_agate, w_aproj, w_bgate, w_bproj)
    gate = pl.pallas_call(
        gate_kernel, out_shape=jax.ShapeDtypeStruct((rows, cols, width), jnp.float32)
    )(pair, w_gate)
    edges = jnp.transpose(z.reshape(rows, 2, n_dev, pairs, 2 * cols), (2, 1, 3, 0, 4))
    edges = lax.all_to_all(edges, ("row", "col"), split_axis=0, concat_axis=0, tiled=True)
    mixed = pl.pallas_call(
        functools.partial(mix_kernel, n_col=n_col),
        out_shape=jax.ShapeDtypeStruct((n_dev, pairs, rows, 2 * cols), jnp.bfloat16),
    )(edges)
    mixed = lax.all_to_all(mixed, ("row", "col"), split_axis=0, concat_axis=0, tiled=True)
    mixed = mixed.reshape(n_dev * pairs * rows, 2 * cols)
    return pl.pallas_call(
        transition_kernel,
        out_shape=jax.ShapeDtypeStruct((rows, cols, width), jnp.bfloat16),
    )(mixed, pair, gate, w_out, w_up, w_down)


def body_rows(pair, mask, w_agate, w_aproj, w_bgate, w_bproj, w_gate, w_out, w_up, w_down):
    rows, cols, width = pair.shape
    pair_flat, gate, left, right = project(pair, mask, w_agate, w_aproj, w_bgate, w_bproj, w_gate)
    left_major = jnp.transpose(left.reshape(rows, cols, -1), (2, 0, 1))
    right_major = jnp.transpose(right.reshape(rows, cols, -1), (2, 0, 1))
    left_spread, right_spread = (
        lax.all_to_all(
            lax.all_to_all(left_major, "row", split_axis=0, concat_axis=1, tiled=True),
            "col",
            split_axis=1,
            concat_axis=2,
            tiled=True,
        ),
        lax.all_to_all(
            lax.all_to_all(right_major, "row", split_axis=0, concat_axis=1, tiled=True),
            "col",
            split_axis=1,
            concat_axis=2,
            tiled=True,
        ),
    )
    mixed = jnp.einsum(
        "cik,cjk->cij",
        lax.all_gather(left_spread, "col", axis=1, tiled=True),
        right_spread,
        preferred_element_type=jnp.float32,
    ).astype(jnp.bfloat16)
    mixed = lax.all_to_all(mixed, "row", split_axis=1, concat_axis=0, tiled=True)
    mixed_rows = jnp.transpose(mixed, (1, 2, 0)).astype(jnp.float32).reshape(rows * cols, -1)
    result = transition(pair_flat, gate, mixed_rows, w_out, w_up, w_down)
    return result.astype(jnp.bfloat16).reshape(rows, cols, width)


def solution(mesh):
    placed = (P("row", "col", None), P(), P(), P(), P(), P(), P(), P(), P(), P())
    n_row, n_col = mesh.shape["row"], mesh.shape["col"]

    def run(pair, mask, w_agate, *weights):
        hid = w_agate.shape[1]
        rows, cols = pair.shape[0] // n_row, pair.shape[1] // n_col
        if hid % (2 * n_row * n_col) == 0 and 2 * cols == 128 and rows % 16 == 0 and n_row * rows == n_col * cols:
            body = functools.partial(body_fused, n_row=n_row, n_col=n_col)
        elif hid % (n_row * n_col) == 0:
            body = functools.partial(body_split, n_row=n_row, n_col=n_col)
        else:
            body = body_rows
        mapped = jax.shard_map(
            body, mesh=mesh, in_specs=placed, out_specs=P("row", "col", None), check_vma=False
        )
        return mapped(pair, mask, w_agate, *weights)

    return run
```

```python
import functools

import jax
import jax.numpy as jnp
from jax import lax
from jax.experimental import pallas as pl
from jax.experimental.pallas import tpu as pltpu
from jax.sharding import PartitionSpec as P


def layer_norm(values):
    center = values - jnp.mean(values, axis=-1, keepdims=True)
    spread = jnp.mean(center * center, axis=-1, keepdims=True)
    return center * lax.rsqrt(spread + 1e-05)


def project(pair, mask, w_agate, w_aproj, w_bgate, w_bproj, w_gate):
    rows, cols, width = pair.shape
    present = mask.astype(jnp.float32)
    row_start = lax.axis_index("row") * rows
    col_start = lax.axis_index("col") * cols
    row_mask = lax.dynamic_slice_in_dim(present, row_start, rows, 0)
    col_mask = lax.dynamic_slice_in_dim(present, col_start, cols, 0)
    pair_mask = (row_mask[:, None] * col_mask[None, :]).reshape(rows * cols, 1)
    pair_flat = pair.astype(jnp.float32).reshape(rows * cols, width)
    normed = layer_norm(pair_flat).astype(jnp.bfloat16)
    gate = jax.nn.sigmoid(jnp.dot(normed, w_gate, preferred_element_type=jnp.float32))
    left = (
        jax.nn.sigmoid(jnp.dot(normed, w_agate, preferred_element_type=jnp.float32))
        * jnp.dot(normed, w_aproj, preferred_element_type=jnp.float32)
        * pair_mask
    )
    right = (
        jax.nn.sigmoid(jnp.dot(normed, w_bgate, preferred_element_type=jnp.float32))
        * jnp.dot(normed, w_bproj, preferred_element_type=jnp.float32)
        * pair_mask
    )
    return pair_flat, gate, left.astype(jnp.bfloat16), right.astype(jnp.bfloat16)


def transition(pair_flat, gate, mixed_rows, w_out, w_up, w_down):
    mixed_normed = layer_norm(mixed_rows).astype(jnp.bfloat16)
    middle = pair_flat + gate * jnp.dot(mixed_normed, w_out, preferred_element_type=jnp.float32)
    trans_in = layer_norm(middle).astype(jnp.bfloat16)
    trans_hidden = jax.nn.relu(jnp.dot(trans_in, w_up, preferred_element_type=jnp.float32)).astype(
        jnp.bfloat16
    )
    return middle + jnp.dot(trans_hidden, w_down, preferred_element_type=jnp.float32)


def body_split(pair, mask, w_agate, w_aproj, w_bgate, w_bproj, w_gate, w_out, w_up, w_down, *, n_row, n_col):
    rows, cols, width = pair.shape
    n_dev = n_row * n_col
    pair_flat, gate, left, right = project(pair, mask, w_agate, w_aproj, w_bgate, w_bproj, w_gate)
    hid = left.shape[-1]
    group = hid // n_dev
    edges = jnp.stack([left, right], axis=0).reshape(2, rows, cols, n_dev, group)
    edges = jnp.transpose(edges, (3, 0, 4, 1, 2))
    edges = lax.all_to_all(edges, ("row", "col"), split_axis=0, concat_axis=0, tiled=True)
    edges = edges.reshape(n_row, n_col, 2, group, rows, cols)
    edges = jnp.transpose(edges, (2, 3, 0, 4, 1, 5)).reshape(2, group, n_row * rows, n_col * cols)
    mixed = jnp.einsum(
        "cik,cjk->cij", edges[0], edges[1], preferred_element_type=jnp.float32
    ).astype(jnp.bfloat16)
    mixed = mixed.reshape(group, n_row, rows, n_col, cols)
    mixed = jnp.transpose(mixed, (1, 3, 0, 2, 4)).reshape(n_dev, group, rows, cols)
    mixed = lax.all_to_all(mixed, ("row", "col"), split_axis=0, concat_axis=0, tiled=True)
    mixed_rows = jnp.transpose(mixed.reshape(hid, rows, cols), (1, 2, 0))
    mixed_rows = mixed_rows.astype(jnp.float32).reshape(rows * cols, hid)
    result = transition(pair_flat, gate, mixed_rows, w_out, w_up, w_down)
    return result.astype(jnp.bfloat16).reshape(rows, cols, width)


def mix_kernel(edges_ref, out_ref, *, n_col, side_major=True):
    n_dev, rows, lanes = edges_ref.shape[0], edges_ref.shape[3], edges_ref.shape[4]
    pairs = edges_ref.shape[2] if side_major else edges_ref.shape[1]
    n_row = n_dev // n_col
    cols = lanes // 2
    parity = (lax.broadcasted_iota(jnp.int32, (1, n_col * lanes), 1) // cols) % 2
    for hp in range(pairs):

        def chunk(source, side):
            return edges_ref[source, side, hp] if side_major else edges_ref[source, hp, side]

        def whole(side):
            return jnp.concatenate(
                [
                    jnp.concatenate([chunk(r * n_col + c, side) for c in range(n_col)], axis=1)
                    for r in range(n_row)
                ],
                axis=0,
            )

        left = whole(0)
        right = whole(1)
        right_even = jnp.where(parity == 0, right, jnp.zeros_like(right))
        right_odd = jnp.where(parity == 1, right, jnp.zeros_like(right))
        for c in range(n_col):
            block = slice(c * cols, (c + 1) * cols)
            rhs = jnp.concatenate([right_even[block], right_odd[block]], axis=0)
            mixed = lax.dot_general(
                left, rhs, (((1,), (1,)), ((), ())), preferred_element_type=jnp.float32
            ).astype(out_ref.dtype)
            for r in range(n_row):
                out_ref[r * n_col + c, hp] = mixed[r * rows : (r + 1) * rows]


def body_kernel(pair, mask, w_agate, w_aproj, w_bgate, w_bproj, w_gate, w_out, w_up, w_down, *, n_row, n_col):
    rows, cols, width = pair.shape
    n_dev = n_row * n_col
    pair_flat, gate, left, right = project(pair, mask, w_agate, w_aproj, w_bgate, w_bproj, w_gate)
    hid = left.shape[-1]
    pairs = hid // n_dev // 2

    def chunks(edges):
        edges = jnp.transpose(edges.reshape(rows, cols, n_dev, pairs, 2), (2, 3, 0, 4, 1))
        return edges.reshape(n_dev, pairs, rows, 2 * cols)

    edges = jnp.stack([chunks(left), chunks(right)], axis=1)
    edges = lax.all_to_all(edges, ("row", "col"), split_axis=0, concat_axis=0, tiled=True)
    mixed = pl.pallas_call(
        functools.partial(mix_kernel, n_col=n_col),
        out_shape=jax.ShapeDtypeStruct((n_dev, pairs, rows, 2 * cols), jnp.bfloat16),
    )(edges)
    mixed = lax.all_to_all(mixed, ("row", "col"), split_axis=0, concat_axis=0, tiled=True)
    mixed = jnp.transpose(mixed.reshape(n_dev, pairs, rows, 2, cols), (2, 4, 0, 1, 3))
    mixed_rows = mixed.astype(jnp.float32).reshape(rows * cols, hid)
    result = transition(pair_flat, gate, mixed_rows, w_out, w_up, w_down)
    return result.astype(jnp.bfloat16).reshape(rows, cols, width)


def project_kernel(mask_ref, pair_ref, wag_ref, wap_ref, wbg_ref, wbp_ref, z_ref, staged_ref, *, block):
    rows, cols, width = pair_ref.shape
    quarter = wag_ref.shape[1] // 2

    def paired(w_ref):
        turned = w_ref[...].astype(jnp.float32).T.astype(jnp.bfloat16)
        return jnp.concatenate([turned[:quarter], turned[quarter:]], axis=1)

    w2 = jnp.concatenate([paired(w) for w in (wag_ref, wap_ref, wbg_ref, wbp_ref)], axis=0)
    row_start = lax.axis_index("row") * rows
    col_start = lax.axis_index("col") * cols
    lane = lax.broadcasted_iota(jnp.int32, (1, 2 * cols), 1) % cols
    col_mask = jnp.zeros((1, 2 * cols), jnp.float32)
    for k in range(cols):
        col_mask = jnp.where(lane == k, mask_ref[col_start + k].astype(jnp.float32), col_mask)

    def rows_of(step, carry):
        first = pl.multiple_of(step * block, block)
        values = pair_ref[pl.ds(first, block)].astype(jnp.float32).reshape(block * cols, width)
        center = values - jnp.mean(values, axis=-1, keepdims=True)
        spread = jnp.mean(center * center, axis=-1, keepdims=True)
        normed = (center * lax.rsqrt(spread + 1e-05)).astype(jnp.bfloat16)
        zeros = jnp.zeros_like(normed)
        top = jnp.concatenate([normed, zeros], axis=1).reshape(block, cols, 2 * width)
        bottom = jnp.concatenate([zeros, normed], axis=1).reshape(block, cols, 2 * width)
        doubled = jnp.concatenate([top, bottom], axis=1).reshape(block * 2 * cols, 2 * width)
        proj = lax.dot_general(
            w2, doubled, (((1,), (1,)), ((), ())), preferred_element_type=jnp.float32
        )
        for i in range(block):
            part = proj[:, i * 2 * cols : (i + 1) * 2 * cols]
            present = col_mask * mask_ref[row_start + first + i].astype(jnp.float32)
            left = jax.nn.sigmoid(part[0:quarter]) * part[quarter : 2 * quarter] * present
            right = jax.nn.sigmoid(part[2 * quarter : 3 * quarter]) * part[3 * quarter :] * present
            staged_ref[pl.ds(first + i, quarter, stride=2 * rows), :] = left
            staged_ref[pl.ds(rows + first + i, quarter, stride=2 * rows), :] = right
        return carry

    lax.fori_loop(0, rows // block, rows_of, 0)
    z_ref[...] = staged_ref[...].astype(z_ref.dtype)


def gate_kernel(pair_ref, wg_ref, gate_ref):
    rows, cols, width = pair_ref.shape
    values = pair_ref[...].astype(jnp.float32).reshape(rows * cols, width)
    center = values - jnp.mean(values, axis=-1, keepdims=True)
    spread = jnp.mean(center * center, axis=-1, keepdims=True)
    normed = (center * lax.rsqrt(spread + 1e-05)).astype(jnp.bfloat16)
    gate = jax.nn.sigmoid(jnp.dot(normed, wg_ref[...], preferred_element_type=jnp.float32))
    gate_ref[...] = gate.reshape(rows, cols, width)


def transition_kernel(mixed_ref, pair_ref, gate_ref, wo_ref, wu_ref, wd_ref, out_ref):
    rows, cols, width = pair_ref.shape
    pairs = mixed_ref.shape[0] // rows

    def norm(values):
        center = values - jnp.mean(values, axis=-1, keepdims=True)
        spread = jnp.mean(center * center, axis=-1, keepdims=True)
        return center * lax.rsqrt(spread + 1e-05)

    parts = []
    for i in range(rows):
        turned = mixed_ref[pl.ds(i, pairs, stride=rows), :].astype(jnp.float32).T
        parts.append(jnp.concatenate([turned[:cols], turned[cols:]], axis=1))
    mixed = jnp.concatenate(parts, axis=0)
    pair = pair_ref[...].astype(jnp.float32).reshape(rows * cols, width)
    gate = gate_ref[...].reshape(rows * cols, width)
    mixed_normed = norm(mixed).astype(jnp.bfloat16)
    middle = pair + gate * jnp.dot(mixed_normed, wo_ref[...], preferred_element_type=jnp.float32)
    trans_in = norm(middle).astype(jnp.bfloat16)
    hidden = jnp.maximum(jnp.dot(trans_in, wu_ref[...], preferred_element_type=jnp.float32), 0.0)
    result = middle + jnp.dot(hidden.astype(jnp.bfloat16), wd_ref[...], preferred_element_type=jnp.float32)
    out_ref[...] = result.astype(out_ref.dtype).reshape(rows, cols, width)


def body_fused(pair, mask, w_agate, w_aproj, w_bgate, w_bproj, w_gate, w_out, w_up, w_down, *, n_row, n_col):
    rows, cols, width = pair.shape
    n_dev = n_row * n_col
    hid = w_agate.shape[1]
    pairs = hid // n_dev // 2

    z = pl.pallas_call(
        functools.partial(project_kernel, block=rows),
        out_shape=jax.ShapeDtypeStruct((hid * rows, 2 * cols), jnp.bfloat16),
        in_specs=[pl.BlockSpec(memory_space=pltpu.SMEM)] + [pl.BlockSpec(memory_space=pltpu.VMEM)] * 5,
        scratch_shapes=[pltpu.VMEM((hid * rows, 2 * cols), jnp.float32)],
    )(mask, pair, w_agate, w_aproj, w_bgate, w_bproj)
    gate = pl.pallas_call(
        gate_kernel, out_shape=jax.ShapeDtypeStruct((rows, cols, width), jnp.float32)
    )(pair, w_gate)
    edges = z.reshape(n_dev, pairs, 2, rows, 2 * cols)
    edges = lax.all_to_all(edges, ("row", "col"), split_axis=0, concat_axis=0, tiled=True)
    mixed = pl.pallas_call(
        functools.partial(mix_kernel, n_col=n_col, side_major=False),
        out_shape=jax.ShapeDtypeStruct((n_dev, pairs, rows, 2 * cols), jnp.bfloat16),
    )(edges)
    mixed = lax.all_to_all(mixed, ("row", "col"), split_axis=0, concat_axis=0, tiled=True)
    mixed = mixed.reshape(n_dev * pairs * rows, 2 * cols)
    return pl.pallas_call(
        transition_kernel,
        out_shape=jax.ShapeDtypeStruct((rows, cols, width), jnp.bfloat16),
    )(mixed, pair, gate, w_out, w_up, w_down)


def body_rows(pair, mask, w_agate, w_aproj, w_bgate, w_bproj, w_gate, w_out, w_up, w_down):
    rows, cols, width = pair.shape
    pair_flat, gate, left, right = project(pair, mask, w_agate, w_aproj, w_bgate, w_bproj, w_gate)
    left_major = jnp.transpose(left.reshape(rows, cols, -1), (2, 0, 1))
    right_major = jnp.transpose(right.reshape(rows, cols, -1), (2, 0, 1))
    left_spread, right_spread = (
        lax.all_to_all(
            lax.all_to_all(left_major, "row", split_axis=0, concat_axis=1, tiled=True),
            "col",
            split_axis=1,
            concat_axis=2,
            tiled=True,
        ),
        lax.all_to_all(
            lax.all_to_all(right_major, "row", split_axis=0, concat_axis=1, tiled=True),
            "col",
            split_axis=1,
            concat_axis=2,
            tiled=True,
        ),
    )
    mixed = jnp.einsum(
        "cik,cjk->cij",
        lax.all_gather(left_spread, "col", axis=1, tiled=True),
        right_spread,
        preferred_element_type=jnp.float32,
    ).astype(jnp.bfloat16)
    mixed = lax.all_to_all(mixed, "row", split_axis=1, concat_axis=0, tiled=True)
    mixed_rows = jnp.transpose(mixed, (1, 2, 0)).astype(jnp.float32).reshape(rows * cols, -1)
    result = transition(pair_flat, gate, mixed_rows, w_out, w_up, w_down)
    return result.astype(jnp.bfloat16).reshape(rows, cols, width)


def solution(mesh):
    placed = (P("row", "col", None), P(), P(), P(), P(), P(), P(), P(), P(), P())
    n_row, n_col = mesh.shape["row"], mesh.shape["col"]

    def run(pair, mask, w_agate, *weights):
        hid = w_agate.shape[1]
        rows, cols = pair.shape[0] // n_row, pair.shape[1] // n_col
        if hid % (2 * n_row * n_col) == 0 and 2 * cols == 128 and rows % 16 == 0 and n_row * rows == n_col * cols:
            body = functools.partial(body_fused, n_row=n_row, n_col=n_col)
        elif hid % (n_row * n_col) == 0:
            body = functools.partial(body_split, n_row=n_row, n_col=n_col)
        else:
            body = body_rows
        mapped = jax.shard_map(
            body, mesh=mesh, in_specs=placed, out_specs=P("row", "col", None), check_vma=False
        )
        return mapped(pair, mask, w_agate, *weights)

    return run
```

```python
import functools

import jax
import jax.numpy as jnp
from jax import lax
from jax.experimental import pallas as pl
from jax.experimental.pallas import tpu as pltpu
from jax.sharding import PartitionSpec as P


def layer_norm(values):
    center = values - jnp.mean(values, axis=-1, keepdims=True)
    spread = jnp.mean(center * center, axis=-1, keepdims=True)
    return center * lax.rsqrt(spread + 1e-05)


def project(pair, mask, w_agate, w_aproj, w_bgate, w_bproj, w_gate):
    rows, cols, width = pair.shape
    present = mask.astype(jnp.float32)
    row_start = lax.axis_index("row") * rows
    col_start = lax.axis_index("col") * cols
    row_mask = lax.dynamic_slice_in_dim(present, row_start, rows, 0)
    col_mask = lax.dynamic_slice_in_dim(present, col_start, cols, 0)
    pair_mask = (row_mask[:, None] * col_mask[None, :]).reshape(rows * cols, 1)
    pair_flat = pair.astype(jnp.float32).reshape(rows * cols, width)
    normed = layer_norm(pair_flat).astype(jnp.bfloat16)
    gate = jax.nn.sigmoid(jnp.dot(normed, w_gate, preferred_element_type=jnp.float32))
    left = (
        jax.nn.sigmoid(jnp.dot(normed, w_agate, preferred_element_type=jnp.float32))
        * jnp.dot(normed, w_aproj, preferred_element_type=jnp.float32)
        * pair_mask
    )
    right = (
        jax.nn.sigmoid(jnp.dot(normed, w_bgate, preferred_element_type=jnp.float32))
        * jnp.dot(normed, w_bproj, preferred_element_type=jnp.float32)
        * pair_mask
    )
    return pair_flat, gate, left.astype(jnp.bfloat16), right.astype(jnp.bfloat16)


def transition(pair_flat, gate, mixed_rows, w_out, w_up, w_down):
    mixed_normed = layer_norm(mixed_rows).astype(jnp.bfloat16)
    middle = pair_flat + gate * jnp.dot(mixed_normed, w_out, preferred_element_type=jnp.float32)
    trans_in = layer_norm(middle).astype(jnp.bfloat16)
    trans_hidden = jax.nn.relu(jnp.dot(trans_in, w_up, preferred_element_type=jnp.float32)).astype(
        jnp.bfloat16
    )
    return middle + jnp.dot(trans_hidden, w_down, preferred_element_type=jnp.float32)


def body_split(pair, mask, w_agate, w_aproj, w_bgate, w_bproj, w_gate, w_out, w_up, w_down, *, n_row, n_col):
    rows, cols, width = pair.shape
    n_dev = n_row * n_col
    pair_flat, gate, left, right = project(pair, mask, w_agate, w_aproj, w_bgate, w_bproj, w_gate)
    hid = left.shape[-1]
    group = hid // n_dev
    edges = jnp.stack([left, right], axis=0).reshape(2, rows, cols, n_dev, group)
    edges = jnp.transpose(edges, (3, 0, 4, 1, 2))
    edges = lax.all_to_all(edges, ("row", "col"), split_axis=0, concat_axis=0, tiled=True)
    edges = edges.reshape(n_row, n_col, 2, group, rows, cols)
    edges = jnp.transpose(edges, (2, 3, 0, 4, 1, 5)).reshape(2, group, n_row * rows, n_col * cols)
    mixed = jnp.einsum(
        "cik,cjk->cij", edges[0], edges[1], preferred_element_type=jnp.float32
    ).astype(jnp.bfloat16)
    mixed = mixed.reshape(group, n_row, rows, n_col, cols)
    mixed = jnp.transpose(mixed, (1, 3, 0, 2, 4)).reshape(n_dev, group, rows, cols)
    mixed = lax.all_to_all(mixed, ("row", "col"), split_axis=0, concat_axis=0, tiled=True)
    mixed_rows = jnp.transpose(mixed.reshape(hid, rows, cols), (1, 2, 0))
    mixed_rows = mixed_rows.astype(jnp.float32).reshape(rows * cols, hid)
    result = transition(pair_flat, gate, mixed_rows, w_out, w_up, w_down)
    return result.astype(jnp.bfloat16).reshape(rows, cols, width)


def mix_kernel(edges_ref, out_ref, *, n_col, side_major=True):
    n_dev, rows, lanes = edges_ref.shape[0], edges_ref.shape[3], edges_ref.shape[4]
    pairs = edges_ref.shape[2] if side_major else edges_ref.shape[1]
    n_row = n_dev // n_col
    cols = lanes // 2
    parity = (lax.broadcasted_iota(jnp.int32, (1, n_col * lanes), 1) // cols) % 2
    for hp in range(pairs):

        def chunk(source, side):
            return edges_ref[source, side, hp] if side_major else edges_ref[source, hp, side]

        def whole(side):
            return jnp.concatenate(
                [
                    jnp.concatenate([chunk(r * n_col + c, side) for c in range(n_col)], axis=1)
                    for r in range(n_row)
                ],
                axis=0,
            )

        left = whole(0)
        right = whole(1)
        right_even = jnp.where(parity == 0, right, jnp.zeros_like(right))
        right_odd = jnp.where(parity == 1, right, jnp.zeros_like(right))
        for c in range(n_col):
            block = slice(c * cols, (c + 1) * cols)
            rhs = jnp.concatenate([right_even[block], right_odd[block]], axis=0)
            mixed = lax.dot_general(
                left, rhs, (((1,), (1,)), ((), ())), preferred_element_type=jnp.float32
            ).astype(out_ref.dtype)
            for r in range(n_row):
                out_ref[r * n_col + c, hp] = mixed[r * rows : (r + 1) * rows]


def mix_blocks_kernel(edges_ref, out_ref):
    n_row, n_col, pairs, _, rows, lanes = edges_ref.shape
    cols = lanes // 2
    per = cols // rows
    parity = (lax.broadcasted_iota(jnp.int32, (1, lanes), 1) // cols) % 2
    for hp in range(pairs):
        for c in range(n_col):
            total = None
            for k in range(n_col):
                left = edges_ref[:, k, hp, 0].reshape(n_row * rows, lanes)
                right = edges_ref[c * per : (c + 1) * per, k, hp, 1].reshape(cols, lanes)
                rhs = jnp.concatenate(
                    [jnp.where(parity == 0, right, jnp.zeros_like(right)), jnp.where(parity == 1, right, jnp.zeros_like(right))],
                    axis=0,
                )
                part = lax.dot_general(left, rhs, (((1,), (1,)), ((), ())), preferred_element_type=jnp.float32)
                total = part if total is None else total + part
            mixed = total.astype(out_ref.dtype)
            for r in range(n_row):
                out_ref[r * n_col + c, hp] = mixed[r * rows : (r + 1) * rows]


def body_kernel(pair, mask, w_agate, w_aproj, w_bgate, w_bproj, w_gate, w_out, w_up, w_down, *, n_row, n_col):
    rows, cols, width = pair.shape
    n_dev = n_row * n_col
    pair_flat, gate, left, right = project(pair, mask, w_agate, w_aproj, w_bgate, w_bproj, w_gate)
    hid = left.shape[-1]
    pairs = hid // n_dev // 2

    def chunks(edges):
        edges = jnp.transpose(edges.reshape(rows, cols, n_dev, pairs, 2), (2, 3, 0, 4, 1))
        return edges.reshape(n_dev, pairs, rows, 2 * cols)

    edges = jnp.stack([chunks(left), chunks(right)], axis=1)
    edges = lax.all_to_all(edges, ("row", "col"), split_axis=0, concat_axis=0, tiled=True)
    mixed = pl.pallas_call(
        functools.partial(mix_kernel, n_col=n_col),
        out_shape=jax.ShapeDtypeStruct((n_dev, pairs, rows, 2 * cols), jnp.bfloat16),
    )(edges)
    mixed = lax.all_to_all(mixed, ("row", "col"), split_axis=0, concat_axis=0, tiled=True)
    mixed = jnp.transpose(mixed.reshape(n_dev, pairs, rows, 2, cols), (2, 4, 0, 1, 3))
    mixed_rows = mixed.astype(jnp.float32).reshape(rows * cols, hid)
    result = transition(pair_flat, gate, mixed_rows, w_out, w_up, w_down)
    return result.astype(jnp.bfloat16).reshape(rows, cols, width)


def project_kernel(mask_ref, pair_ref, wag_ref, wap_ref, wbg_ref, wbp_ref, z_ref, staged_ref, *, block):
    rows, cols, width = pair_ref.shape
    quarter = wag_ref.shape[1] // 2

    def paired(w_ref):
        turned = w_ref[...].astype(jnp.float32).T.astype(jnp.bfloat16)
        return jnp.concatenate([turned[:quarter], turned[quarter:]], axis=1)

    w2 = jnp.concatenate([paired(w) for w in (wag_ref, wap_ref, wbg_ref, wbp_ref)], axis=0)
    row_start = lax.axis_index("row") * rows
    col_start = lax.axis_index("col") * cols
    lane = lax.broadcasted_iota(jnp.int32, (1, 2 * cols), 1) % cols
    col_mask = jnp.zeros((1, 2 * cols), jnp.float32)
    for k in range(cols):
        col_mask = jnp.where(lane == k, mask_ref[col_start + k].astype(jnp.float32), col_mask)

    def rows_of(step, carry):
        first = pl.multiple_of(step * block, block)
        values = pair_ref[pl.ds(first, block)].astype(jnp.float32).reshape(block * cols, width)
        center = values - jnp.mean(values, axis=-1, keepdims=True)
        spread = jnp.mean(center * center, axis=-1, keepdims=True)
        normed = (center * lax.rsqrt(spread + 1e-05)).astype(jnp.bfloat16)
        zeros = jnp.zeros_like(normed)
        top = jnp.concatenate([normed, zeros], axis=1).reshape(block, cols, 2 * width)
        bottom = jnp.concatenate([zeros, normed], axis=1).reshape(block, cols, 2 * width)
        doubled = jnp.concatenate([top, bottom], axis=1).reshape(block * 2 * cols, 2 * width)
        proj = lax.dot_general(
            w2, doubled, (((1,), (1,)), ((), ())), preferred_element_type=jnp.float32
        )
        for i in range(block):
            part = proj[:, i * 2 * cols : (i + 1) * 2 * cols]
            present = col_mask * mask_ref[row_start + first + i].astype(jnp.float32)
            left = jax.nn.sigmoid(part[0:quarter]) * part[quarter : 2 * quarter] * present
            right = jax.nn.sigmoid(part[2 * quarter : 3 * quarter]) * part[3 * quarter :] * present
            staged_ref[pl.ds(first + i, quarter, stride=2 * rows), :] = left
            staged_ref[pl.ds(rows + first + i, quarter, stride=2 * rows), :] = right
        return carry

    lax.fori_loop(0, rows // block, rows_of, 0)
    z_ref[...] = staged_ref[...].astype(z_ref.dtype)


def gate_kernel(pair_ref, wg_ref, gate_ref):
    rows, cols, width = pair_ref.shape
    values = pair_ref[...].astype(jnp.float32).reshape(rows * cols, width)
    center = values - jnp.mean(values, axis=-1, keepdims=True)
    spread = jnp.mean(center * center, axis=-1, keepdims=True)
    normed = (center * lax.rsqrt(spread + 1e-05)).astype(jnp.bfloat16)
    gate = jax.nn.sigmoid(jnp.dot(normed, wg_ref[...], preferred_element_type=jnp.float32))
    gate_ref[...] = gate.reshape(rows, cols, width)


def transition_kernel(mixed_ref, pair_ref, gate_ref, wo_ref, wu_ref, wd_ref, out_ref):
    rows, cols, width = pair_ref.shape
    pairs = mixed_ref.shape[0] // rows

    def norm(values):
        center = values - jnp.mean(values, axis=-1, keepdims=True)
        spread = jnp.mean(center * center, axis=-1, keepdims=True)
        return center * lax.rsqrt(spread + 1e-05)

    parts = []
    for i in range(rows):
        turned = mixed_ref[pl.ds(i, pairs, stride=rows), :].astype(jnp.float32).T
        parts.append(jnp.concatenate([turned[:cols], turned[cols:]], axis=1))
    mixed = jnp.concatenate(parts, axis=0)
    pair = pair_ref[...].astype(jnp.float32).reshape(rows * cols, width)
    gate = gate_ref[...].reshape(rows * cols, width)
    mixed_normed = norm(mixed).astype(jnp.bfloat16)
    middle = pair + gate * jnp.dot(mixed_normed, wo_ref[...], preferred_element_type=jnp.float32)
    trans_in = norm(middle).astype(jnp.bfloat16)
    hidden = jnp.maximum(jnp.dot(trans_in, wu_ref[...], preferred_element_type=jnp.float32), 0.0)
    result = middle + jnp.dot(hidden.astype(jnp.bfloat16), wd_ref[...], preferred_element_type=jnp.float32)
    out_ref[...] = result.astype(out_ref.dtype).reshape(rows, cols, width)


def body_fused(pair, mask, w_agate, w_aproj, w_bgate, w_bproj, w_gate, w_out, w_up, w_down, *, n_row, n_col):
    rows, cols, width = pair.shape
    n_dev = n_row * n_col
    hid = w_agate.shape[1]
    pairs = hid // n_dev // 2

    z = pl.pallas_call(
        functools.partial(project_kernel, block=rows),
        out_shape=jax.ShapeDtypeStruct((hid * rows, 2 * cols), jnp.bfloat16),
        in_specs=[pl.BlockSpec(memory_space=pltpu.SMEM)] + [pl.BlockSpec(memory_space=pltpu.VMEM)] * 5,
        scratch_shapes=[pltpu.VMEM((hid * rows, 2 * cols), jnp.float32)],
    )(mask, pair, w_agate, w_aproj, w_bgate, w_bproj)
    gate = pl.pallas_call(
        gate_kernel, out_shape=jax.ShapeDtypeStruct((rows, cols, width), jnp.float32)
    )(pair, w_gate)
    edges = z.reshape(n_dev, pairs, 2, rows, 2 * cols)
    edges = lax.all_to_all(edges, ("row", "col"), split_axis=0, concat_axis=0, tiled=True)
    mixed = pl.pallas_call(
        mix_blocks_kernel,
        out_shape=jax.ShapeDtypeStruct((n_dev, pairs, rows, 2 * cols), jnp.bfloat16),
    )(edges.reshape(n_row, n_col, pairs, 2, rows, 2 * cols))
    mixed = lax.all_to_all(mixed, ("row", "col"), split_axis=0, concat_axis=0, tiled=True)
    mixed = mixed.reshape(n_dev * pairs * rows, 2 * cols)
    return pl.pallas_call(
        transition_kernel,
        out_shape=jax.ShapeDtypeStruct((rows, cols, width), jnp.bfloat16),
    )(mixed, pair, gate, w_out, w_up, w_down)


def body_rows(pair, mask, w_agate, w_aproj, w_bgate, w_bproj, w_gate, w_out, w_up, w_down):
    rows, cols, width = pair.shape
    pair_flat, gate, left, right = project(pair, mask, w_agate, w_aproj, w_bgate, w_bproj, w_gate)
    left_major = jnp.transpose(left.reshape(rows, cols, -1), (2, 0, 1))
    right_major = jnp.transpose(right.reshape(rows, cols, -1), (2, 0, 1))
    left_spread, right_spread = (
        lax.all_to_all(
            lax.all_to_all(left_major, "row", split_axis=0, concat_axis=1, tiled=True),
            "col",
            split_axis=1,
            concat_axis=2,
            tiled=True,
        ),
        lax.all_to_all(
            lax.all_to_all(right_major, "row", split_axis=0, concat_axis=1, tiled=True),
            "col",
            split_axis=1,
            concat_axis=2,
            tiled=True,
        ),
    )
    mixed = jnp.einsum(
        "cik,cjk->cij",
        lax.all_gather(left_spread, "col", axis=1, tiled=True),
        right_spread,
        preferred_element_type=jnp.float32,
    ).astype(jnp.bfloat16)
    mixed = lax.all_to_all(mixed, "row", split_axis=1, concat_axis=0, tiled=True)
    mixed_rows = jnp.transpose(mixed, (1, 2, 0)).astype(jnp.float32).reshape(rows * cols, -1)
    result = transition(pair_flat, gate, mixed_rows, w_out, w_up, w_down)
    return result.astype(jnp.bfloat16).reshape(rows, cols, width)


def solution(mesh):
    placed = (P("row", "col", None), P(), P(), P(), P(), P(), P(), P(), P(), P())
    n_row, n_col = mesh.shape["row"], mesh.shape["col"]

    def run(pair, mask, w_agate, *weights):
        hid = w_agate.shape[1]
        rows, cols = pair.shape[0] // n_row, pair.shape[1] // n_col
        if hid % (2 * n_row * n_col) == 0 and 2 * cols == 128 and rows % 16 == 0 and cols % rows == 0 and n_row * rows == n_col * cols:
            body = functools.partial(body_fused, n_row=n_row, n_col=n_col)
        elif hid % (n_row * n_col) == 0:
            body = functools.partial(body_split, n_row=n_row, n_col=n_col)
        else:
            body = body_rows
        mapped = jax.shard_map(
            body, mesh=mesh, in_specs=placed, out_specs=P("row", "col", None), check_vma=False
        )
        return mapped(pair, mask, w_agate, *weights)

    return run
```

```python
import functools

import jax
import jax.numpy as jnp
from jax import lax
from jax.experimental import pallas as pl
from jax.experimental.pallas import tpu as pltpu
from jax.sharding import PartitionSpec as P


def layer_norm(values):
    center = values - jnp.mean(values, axis=-1, keepdims=True)
    spread = jnp.mean(center * center, axis=-1, keepdims=True)
    return center * lax.rsqrt(spread + 1e-05)


def project(pair, mask, w_agate, w_aproj, w_bgate, w_bproj, w_gate):
    rows, cols, width = pair.shape
    present = mask.astype(jnp.float32)
    row_start = lax.axis_index("row") * rows
    col_start = lax.axis_index("col") * cols
    row_mask = lax.dynamic_slice_in_dim(present, row_start, rows, 0)
    col_mask = lax.dynamic_slice_in_dim(present, col_start, cols, 0)
    pair_mask = (row_mask[:, None] * col_mask[None, :]).reshape(rows * cols, 1)
    pair_flat = pair.astype(jnp.float32).reshape(rows * cols, width)
    normed = layer_norm(pair_flat).astype(jnp.bfloat16)
    gate = jax.nn.sigmoid(jnp.dot(normed, w_gate, preferred_element_type=jnp.float32))
    left = (
        jax.nn.sigmoid(jnp.dot(normed, w_agate, preferred_element_type=jnp.float32))
        * jnp.dot(normed, w_aproj, preferred_element_type=jnp.float32)
        * pair_mask
    )
    right = (
        jax.nn.sigmoid(jnp.dot(normed, w_bgate, preferred_element_type=jnp.float32))
        * jnp.dot(normed, w_bproj, preferred_element_type=jnp.float32)
        * pair_mask
    )
    return pair_flat, gate, left.astype(jnp.bfloat16), right.astype(jnp.bfloat16)


def transition(pair_flat, gate, mixed_rows, w_out, w_up, w_down):
    mixed_normed = layer_norm(mixed_rows).astype(jnp.bfloat16)
    middle = pair_flat + gate * jnp.dot(mixed_normed, w_out, preferred_element_type=jnp.float32)
    trans_in = layer_norm(middle).astype(jnp.bfloat16)
    trans_hidden = jax.nn.relu(jnp.dot(trans_in, w_up, preferred_element_type=jnp.float32)).astype(
        jnp.bfloat16
    )
    return middle + jnp.dot(trans_hidden, w_down, preferred_element_type=jnp.float32)


def body_split(pair, mask, w_agate, w_aproj, w_bgate, w_bproj, w_gate, w_out, w_up, w_down, *, n_row, n_col):
    rows, cols, width = pair.shape
    n_dev = n_row * n_col
    pair_flat, gate, left, right = project(pair, mask, w_agate, w_aproj, w_bgate, w_bproj, w_gate)
    hid = left.shape[-1]
    group = hid // n_dev
    edges = jnp.stack([left, right], axis=0).reshape(2, rows, cols, n_dev, group)
    edges = jnp.transpose(edges, (3, 0, 4, 1, 2))
    edges = lax.all_to_all(edges, ("row", "col"), split_axis=0, concat_axis=0, tiled=True)
    edges = edges.reshape(n_row, n_col, 2, group, rows, cols)
    edges = jnp.transpose(edges, (2, 3, 0, 4, 1, 5)).reshape(2, group, n_row * rows, n_col * cols)
    mixed = jnp.einsum(
        "cik,cjk->cij", edges[0], edges[1], preferred_element_type=jnp.float32
    ).astype(jnp.bfloat16)
    mixed = mixed.reshape(group, n_row, rows, n_col, cols)
    mixed = jnp.transpose(mixed, (1, 3, 0, 2, 4)).reshape(n_dev, group, rows, cols)
    mixed = lax.all_to_all(mixed, ("row", "col"), split_axis=0, concat_axis=0, tiled=True)
    mixed_rows = jnp.transpose(mixed.reshape(hid, rows, cols), (1, 2, 0))
    mixed_rows = mixed_rows.astype(jnp.float32).reshape(rows * cols, hid)
    result = transition(pair_flat, gate, mixed_rows, w_out, w_up, w_down)
    return result.astype(jnp.bfloat16).reshape(rows, cols, width)


def mix_kernel(edges_ref, out_ref, *, n_col, side_major=True):
    n_dev, rows, lanes = edges_ref.shape[0], edges_ref.shape[3], edges_ref.shape[4]
    pairs = edges_ref.shape[2] if side_major else edges_ref.shape[1]
    n_row = n_dev // n_col
    cols = lanes // 2
    parity = (lax.broadcasted_iota(jnp.int32, (1, n_col * lanes), 1) // cols) % 2
    for hp in range(pairs):

        def chunk(source, side):
            return edges_ref[source, side, hp] if side_major else edges_ref[source, hp, side]

        def whole(side):
            return jnp.concatenate(
                [
                    jnp.concatenate([chunk(r * n_col + c, side) for c in range(n_col)], axis=1)
                    for r in range(n_row)
                ],
                axis=0,
            )

        left = whole(0)
        right = whole(1)
        right_even = jnp.where(parity == 0, right, jnp.zeros_like(right))
        right_odd = jnp.where(parity == 1, right, jnp.zeros_like(right))
        for c in range(n_col):
            block = slice(c * cols, (c + 1) * cols)
            rhs = jnp.concatenate([right_even[block], right_odd[block]], axis=0)
            mixed = lax.dot_general(
                left, rhs, (((1,), (1,)), ((), ())), preferred_element_type=jnp.float32
            ).astype(out_ref.dtype)
            for r in range(n_row):
                out_ref[r * n_col + c, hp] = mixed[r * rows : (r + 1) * rows]


def body_kernel(pair, mask, w_agate, w_aproj, w_bgate, w_bproj, w_gate, w_out, w_up, w_down, *, n_row, n_col):
    rows, cols, width = pair.shape
    n_dev = n_row * n_col
    pair_flat, gate, left, right = project(pair, mask, w_agate, w_aproj, w_bgate, w_bproj, w_gate)
    hid = left.shape[-1]
    pairs = hid // n_dev // 2

    def chunks(edges):
        edges = jnp.transpose(edges.reshape(rows, cols, n_dev, pairs, 2), (2, 3, 0, 4, 1))
        return edges.reshape(n_dev, pairs, rows, 2 * cols)

    edges = jnp.stack([chunks(left), chunks(right)], axis=1)
    edges = lax.all_to_all(edges, ("row", "col"), split_axis=0, concat_axis=0, tiled=True)
    mixed = pl.pallas_call(
        functools.partial(mix_kernel, n_col=n_col),
        out_shape=jax.ShapeDtypeStruct((n_dev, pairs, rows, 2 * cols), jnp.bfloat16),
    )(edges)
    mixed = lax.all_to_all(mixed, ("row", "col"), split_axis=0, concat_axis=0, tiled=True)
    mixed = jnp.transpose(mixed.reshape(n_dev, pairs, rows, 2, cols), (2, 4, 0, 1, 3))
    mixed_rows = mixed.astype(jnp.float32).reshape(rows * cols, hid)
    result = transition(pair_flat, gate, mixed_rows, w_out, w_up, w_down)
    return result.astype(jnp.bfloat16).reshape(rows, cols, width)


def project_kernel(mask_ref, pair_ref, wag_ref, wap_ref, wbg_ref, wbp_ref, z_ref, staged_ref, *, block):
    rows, cols, width = pair_ref.shape
    quarter = wag_ref.shape[1] // 2

    def paired(w_ref):
        turned = w_ref[...].astype(jnp.float32).T.astype(jnp.bfloat16)
        return jnp.concatenate([turned[:quarter], turned[quarter:]], axis=1)

    w2 = jnp.concatenate([paired(w) for w in (wag_ref, wap_ref, wbg_ref, wbp_ref)], axis=0)
    row_start = lax.axis_index("row") * rows
    col_start = lax.axis_index("col") * cols
    lane = lax.broadcasted_iota(jnp.int32, (1, 2 * cols), 1) % cols
    col_mask = jnp.zeros((1, 2 * cols), jnp.float32)
    for k in range(cols):
        col_mask = jnp.where(lane == k, mask_ref[col_start + k].astype(jnp.float32), col_mask)

    def rows_of(step, carry):
        first = pl.multiple_of(step * block, block)
        values = pair_ref[pl.ds(first, block)].astype(jnp.float32).reshape(block * cols, width)
        center = values - jnp.mean(values, axis=-1, keepdims=True)
        spread = jnp.mean(center * center, axis=-1, keepdims=True)
        normed = (center * lax.rsqrt(spread + 1e-05)).astype(jnp.bfloat16)
        zeros = jnp.zeros_like(normed)
        top = jnp.concatenate([normed, zeros], axis=1).reshape(block, cols, 2 * width)
        bottom = jnp.concatenate([zeros, normed], axis=1).reshape(block, cols, 2 * width)
        doubled = jnp.concatenate([top, bottom], axis=1).reshape(block * 2 * cols, 2 * width)
        proj = lax.dot_general(
            w2, doubled, (((1,), (1,)), ((), ())), preferred_element_type=jnp.float32
        )
        for i in range(block):
            part = proj[:, i * 2 * cols : (i + 1) * 2 * cols]
            present = col_mask * mask_ref[row_start + first + i].astype(jnp.float32)
            left = jax.nn.sigmoid(part[0:quarter]) * part[quarter : 2 * quarter] * present
            right = jax.nn.sigmoid(part[2 * quarter : 3 * quarter]) * part[3 * quarter :] * present
            staged_ref[pl.ds(first + i, quarter, stride=2 * rows), :] = left
            staged_ref[pl.ds(rows + first + i, quarter, stride=2 * rows), :] = right
        return carry

    lax.fori_loop(0, rows // block, rows_of, 0)
    z_ref[...] = staged_ref[...].astype(z_ref.dtype)


def gate_kernel(pair_ref, wg_ref, gate_ref):
    rows, cols, width = pair_ref.shape
    values = pair_ref[...].astype(jnp.float32).reshape(rows * cols, width)
    center = values - jnp.mean(values, axis=-1, keepdims=True)
    spread = jnp.mean(center * center, axis=-1, keepdims=True)
    normed = (center * lax.rsqrt(spread + 1e-05)).astype(jnp.bfloat16)
    gate = jax.nn.sigmoid(jnp.dot(normed, wg_ref[...], preferred_element_type=jnp.float32))
    gate_ref[...] = gate.reshape(rows, cols, width)


def transition_kernel(mixed_ref, pair_ref, gate_ref, wo_ref, wu_ref, wd_ref, out_ref):
    rows, cols, width = pair_ref.shape
    pairs = mixed_ref.shape[0] // rows

    def norm(values):
        center = values - jnp.mean(values, axis=-1, keepdims=True)
        spread = jnp.mean(center * center, axis=-1, keepdims=True)
        return center * lax.rsqrt(spread + 1e-05)

    parts = []
    for i in range(rows):
        turned = mixed_ref[pl.ds(i, pairs, stride=rows), :].astype(jnp.float32).T
        parts.append(jnp.concatenate([turned[:cols], turned[cols:]], axis=1))
    mixed = jnp.concatenate(parts, axis=0)
    pair = pair_ref[...].astype(jnp.float32).reshape(rows * cols, width)
    gate = gate_ref[...].reshape(rows * cols, width)
    mixed_normed = norm(mixed).astype(jnp.bfloat16)
    middle = pair + gate * jnp.dot(mixed_normed, wo_ref[...], preferred_element_type=jnp.float32)
    trans_in = norm(middle).astype(jnp.bfloat16)
    hidden = jnp.maximum(jnp.dot(trans_in, wu_ref[...], preferred_element_type=jnp.float32), 0.0)
    result = middle + jnp.dot(hidden.astype(jnp.bfloat16), wd_ref[...], preferred_element_type=jnp.float32)
    out_ref[...] = result.astype(out_ref.dtype).reshape(rows, cols, width)


def body_fused(pair, mask, w_agate, w_aproj, w_bgate, w_bproj, w_gate, w_out, w_up, w_down, *, n_row, n_col):
    rows, cols, width = pair.shape
    n_dev = n_row * n_col
    hid = w_agate.shape[1]
    pairs = hid // n_dev // 2

    z = pl.pallas_call(
        functools.partial(project_kernel, block=rows),
        out_shape=jax.ShapeDtypeStruct((hid * rows, 2 * cols), jnp.bfloat16),
        in_specs=[pl.BlockSpec(memory_space=pltpu.SMEM)] + [pl.BlockSpec(memory_space=pltpu.VMEM)] * 5,
        scratch_shapes=[pltpu.VMEM((hid * rows, 2 * cols), jnp.float32)],
    )(mask, pair, w_agate, w_aproj, w_bgate, w_bproj)
    gate = pl.pallas_call(
        gate_kernel, out_shape=jax.ShapeDtypeStruct((rows, cols, width), jnp.float32)
    )(pair, w_gate)
    edges = z.reshape(n_dev, pairs, 2, rows, 2 * cols)
    edges = lax.all_to_all(edges, ("row", "col"), split_axis=0, concat_axis=0, tiled=True)
    mixed = pl.pallas_call(
        functools.partial(mix_kernel, n_col=n_col, side_major=False),
        out_shape=jax.ShapeDtypeStruct((n_dev, pairs, rows, 2 * cols), jnp.bfloat16),
        grid=(pairs,),
        in_specs=[pl.BlockSpec((n_dev, 1, 2, rows, 2 * cols), lambda hp: (0, hp, 0, 0, 0))],
        out_specs=pl.BlockSpec((n_dev, 1, rows, 2 * cols), lambda hp: (0, hp, 0, 0)),
    )(edges)
    mixed = lax.all_to_all(mixed, ("row", "col"), split_axis=0, concat_axis=0, tiled=True)
    mixed = mixed.reshape(n_dev * pairs * rows, 2 * cols)
    return pl.pallas_call(
        transition_kernel,
        out_shape=jax.ShapeDtypeStruct((rows, cols, width), jnp.bfloat16),
    )(mixed, pair, gate, w_out, w_up, w_down)


def body_rows(pair, mask, w_agate, w_aproj, w_bgate, w_bproj, w_gate, w_out, w_up, w_down):
    rows, cols, width = pair.shape
    pair_flat, gate, left, right = project(pair, mask, w_agate, w_aproj, w_bgate, w_bproj, w_gate)
    left_major = jnp.transpose(left.reshape(rows, cols, -1), (2, 0, 1))
    right_major = jnp.transpose(right.reshape(rows, cols, -1), (2, 0, 1))
    left_spread, right_spread = (
        lax.all_to_all(
            lax.all_to_all(left_major, "row", split_axis=0, concat_axis=1, tiled=True),
            "col",
            split_axis=1,
            concat_axis=2,
            tiled=True,
        ),
        lax.all_to_all(
            lax.all_to_all(right_major, "row", split_axis=0, concat_axis=1, tiled=True),
            "col",
            split_axis=1,
            concat_axis=2,
            tiled=True,
        ),
    )
    mixed = jnp.einsum(
        "cik,cjk->cij",
        lax.all_gather(left_spread, "col", axis=1, tiled=True),
        right_spread,
        preferred_element_type=jnp.float32,
    ).astype(jnp.bfloat16)
    mixed = lax.all_to_all(mixed, "row", split_axis=1, concat_axis=0, tiled=True)
    mixed_rows = jnp.transpose(mixed, (1, 2, 0)).astype(jnp.float32).reshape(rows * cols, -1)
    result = transition(pair_flat, gate, mixed_rows, w_out, w_up, w_down)
    return result.astype(jnp.bfloat16).reshape(rows, cols, width)


def solution(mesh):
    placed = (P("row", "col", None), P(), P(), P(), P(), P(), P(), P(), P(), P())
    n_row, n_col = mesh.shape["row"], mesh.shape["col"]

    def run(pair, mask, w_agate, *weights):
        hid = w_agate.shape[1]
        rows, cols = pair.shape[0] // n_row, pair.shape[1] // n_col
        if hid % (2 * n_row * n_col) == 0 and 2 * cols == 128 and rows % 16 == 0 and n_row * rows == n_col * cols:
            body = functools.partial(body_fused, n_row=n_row, n_col=n_col)
        elif hid % (n_row * n_col) == 0:
            body = functools.partial(body_split, n_row=n_row, n_col=n_col)
        else:
            body = body_rows
        mapped = jax.shard_map(
            body, mesh=mesh, in_specs=placed, out_specs=P("row", "col", None), check_vma=False
        )
        return mapped(pair, mask, w_agate, *weights)

    return run
```

```python
import functools

import jax
import jax.numpy as jnp
from jax import lax
from jax.experimental import pallas as pl
from jax.experimental.pallas import tpu as pltpu
from jax.sharding import PartitionSpec as P


def layer_norm(values):
    center = values - jnp.mean(values, axis=-1, keepdims=True)
    spread = jnp.mean(center * center, axis=-1, keepdims=True)
    return center * lax.rsqrt(spread + 1e-05)


def project(pair, mask, w_agate, w_aproj, w_bgate, w_bproj, w_gate):
    rows, cols, width = pair.shape
    present = mask.astype(jnp.float32)
    row_start = lax.axis_index("row") * rows
    col_start = lax.axis_index("col") * cols
    row_mask = lax.dynamic_slice_in_dim(present, row_start, rows, 0)
    col_mask = lax.dynamic_slice_in_dim(present, col_start, cols, 0)
    pair_mask = (row_mask[:, None] * col_mask[None, :]).reshape(rows * cols, 1)
    pair_flat = pair.astype(jnp.float32).reshape(rows * cols, width)
    normed = layer_norm(pair_flat).astype(jnp.bfloat16)
    gate = jax.nn.sigmoid(jnp.dot(normed, w_gate, preferred_element_type=jnp.float32))
    left = (
        jax.nn.sigmoid(jnp.dot(normed, w_agate, preferred_element_type=jnp.float32))
        * jnp.dot(normed, w_aproj, preferred_element_type=jnp.float32)
        * pair_mask
    )
    right = (
        jax.nn.sigmoid(jnp.dot(normed, w_bgate, preferred_element_type=jnp.float32))
        * jnp.dot(normed, w_bproj, preferred_element_type=jnp.float32)
        * pair_mask
    )
    return pair_flat, gate, left.astype(jnp.bfloat16), right.astype(jnp.bfloat16)


def transition(pair_flat, gate, mixed_rows, w_out, w_up, w_down):
    mixed_normed = layer_norm(mixed_rows).astype(jnp.bfloat16)
    middle = pair_flat + gate * jnp.dot(mixed_normed, w_out, preferred_element_type=jnp.float32)
    trans_in = layer_norm(middle).astype(jnp.bfloat16)
    trans_hidden = jax.nn.relu(jnp.dot(trans_in, w_up, preferred_element_type=jnp.float32)).astype(
        jnp.bfloat16
    )
    return middle + jnp.dot(trans_hidden, w_down, preferred_element_type=jnp.float32)


def body_split(pair, mask, w_agate, w_aproj, w_bgate, w_bproj, w_gate, w_out, w_up, w_down, *, n_row, n_col):
    rows, cols, width = pair.shape
    n_dev = n_row * n_col
    pair_flat, gate, left, right = project(pair, mask, w_agate, w_aproj, w_bgate, w_bproj, w_gate)
    hid = left.shape[-1]
    group = hid // n_dev
    edges = jnp.stack([left, right], axis=0).reshape(2, rows, cols, n_dev, group)
    edges = jnp.transpose(edges, (3, 0, 4, 1, 2))
    edges = lax.all_to_all(edges, ("row", "col"), split_axis=0, concat_axis=0, tiled=True)
    edges = edges.reshape(n_row, n_col, 2, group, rows, cols)
    edges = jnp.transpose(edges, (2, 3, 0, 4, 1, 5)).reshape(2, group, n_row * rows, n_col * cols)
    mixed = jnp.einsum(
        "cik,cjk->cij", edges[0], edges[1], preferred_element_type=jnp.float32
    ).astype(jnp.bfloat16)
    mixed = mixed.reshape(group, n_row, rows, n_col, cols)
    mixed = jnp.transpose(mixed, (1, 3, 0, 2, 4)).reshape(n_dev, group, rows, cols)
    mixed = lax.all_to_all(mixed, ("row", "col"), split_axis=0, concat_axis=0, tiled=True)
    mixed_rows = jnp.transpose(mixed.reshape(hid, rows, cols), (1, 2, 0))
    mixed_rows = mixed_rows.astype(jnp.float32).reshape(rows * cols, hid)
    result = transition(pair_flat, gate, mixed_rows, w_out, w_up, w_down)
    return result.astype(jnp.bfloat16).reshape(rows, cols, width)


def mix_kernel(edges_ref, out_ref, *, n_col, side_major=True):
    n_dev, rows, lanes = edges_ref.shape[0], edges_ref.shape[3], edges_ref.shape[4]
    pairs = edges_ref.shape[2] if side_major else edges_ref.shape[1]
    n_row = n_dev // n_col
    cols = lanes // 2
    parity = (lax.broadcasted_iota(jnp.int32, (1, n_col * lanes), 1) // cols) % 2
    for hp in range(pairs):

        def chunk(source, side):
            return edges_ref[source, side, hp] if side_major else edges_ref[source, hp, side]

        def whole(side):
            return jnp.concatenate(
                [
                    jnp.concatenate([chunk(r * n_col + c, side) for c in range(n_col)], axis=1)
                    for r in range(n_row)
                ],
                axis=0,
            )

        left = whole(0)
        right = whole(1)
        right_even = jnp.where(parity == 0, right, jnp.zeros_like(right))
        right_odd = jnp.where(parity == 1, right, jnp.zeros_like(right))
        for c in range(n_col):
            block = slice(c * cols, (c + 1) * cols)
            rhs = jnp.concatenate([right_even[block], right_odd[block]], axis=0)
            mixed = lax.dot_general(
                left, rhs, (((1,), (1,)), ((), ())), preferred_element_type=jnp.float32
            ).astype(out_ref.dtype)
            for r in range(n_row):
                out_ref[r * n_col + c, hp] = mixed[r * rows : (r + 1) * rows]


def body_kernel(pair, mask, w_agate, w_aproj, w_bgate, w_bproj, w_gate, w_out, w_up, w_down, *, n_row, n_col):
    rows, cols, width = pair.shape
    n_dev = n_row * n_col
    pair_flat, gate, left, right = project(pair, mask, w_agate, w_aproj, w_bgate, w_bproj, w_gate)
    hid = left.shape[-1]
    pairs = hid // n_dev // 2

    def chunks(edges):
        edges = jnp.transpose(edges.reshape(rows, cols, n_dev, pairs, 2), (2, 3, 0, 4, 1))
        return edges.reshape(n_dev, pairs, rows, 2 * cols)

    edges = jnp.stack([chunks(left), chunks(right)], axis=1)
    edges = lax.all_to_all(edges, ("row", "col"), split_axis=0, concat_axis=0, tiled=True)
    mixed = pl.pallas_call(
        functools.partial(mix_kernel, n_col=n_col),
        out_shape=jax.ShapeDtypeStruct((n_dev, pairs, rows, 2 * cols), jnp.bfloat16),
    )(edges)
    mixed = lax.all_to_all(mixed, ("row", "col"), split_axis=0, concat_axis=0, tiled=True)
    mixed = jnp.transpose(mixed.reshape(n_dev, pairs, rows, 2, cols), (2, 4, 0, 1, 3))
    mixed_rows = mixed.astype(jnp.float32).reshape(rows * cols, hid)
    result = transition(pair_flat, gate, mixed_rows, w_out, w_up, w_down)
    return result.astype(jnp.bfloat16).reshape(rows, cols, width)


def project_kernel(mask_ref, pair_ref, wag_ref, wap_ref, wbg_ref, wbp_ref, z_ref, staged_ref, *, block):
    rows, cols, width = pair_ref.shape
    quarter = wag_ref.shape[1] // 2

    def paired(w_ref):
        turned = w_ref[...].astype(jnp.float32).T.astype(jnp.bfloat16)
        return jnp.concatenate([turned[:quarter], turned[quarter:]], axis=1)

    w2 = jnp.concatenate([paired(w) for w in (wag_ref, wap_ref, wbg_ref, wbp_ref)], axis=0)
    row_start = lax.axis_index("row") * rows
    col_start = lax.axis_index("col") * cols
    lane = lax.broadcasted_iota(jnp.int32, (1, 2 * cols), 1) % cols
    col_mask = jnp.zeros((1, 2 * cols), jnp.float32)
    for k in range(cols):
        col_mask = jnp.where(lane == k, mask_ref[col_start + k].astype(jnp.float32), col_mask)

    def rows_of(step, carry):
        first = pl.multiple_of(step * block, block)
        values = pair_ref[pl.ds(first, block)].astype(jnp.float32).reshape(block * cols, width)
        center = values - jnp.mean(values, axis=-1, keepdims=True)
        spread = jnp.mean(center * center, axis=-1, keepdims=True)
        normed = (center * lax.rsqrt(spread + 1e-05)).astype(jnp.bfloat16)
        zeros = jnp.zeros_like(normed)
        top = jnp.concatenate([normed, zeros], axis=1).reshape(block, cols, 2 * width)
        bottom = jnp.concatenate([zeros, normed], axis=1).reshape(block, cols, 2 * width)
        doubled = jnp.concatenate([top, bottom], axis=1).reshape(block * 2 * cols, 2 * width)
        proj = lax.dot_general(
            w2, doubled, (((1,), (1,)), ((), ())), preferred_element_type=jnp.float32
        )
        for i in range(block):
            part = proj[:, i * 2 * cols : (i + 1) * 2 * cols]
            present = col_mask * mask_ref[row_start + first + i].astype(jnp.float32)
            left = jax.nn.sigmoid(part[0:quarter]) * part[quarter : 2 * quarter] * present
            right = jax.nn.sigmoid(part[2 * quarter : 3 * quarter]) * part[3 * quarter :] * present
            staged_ref[pl.ds(first + i, quarter, stride=2 * rows), :] = left
            staged_ref[pl.ds(rows + first + i, quarter, stride=2 * rows), :] = right
        return carry

    lax.fori_loop(0, rows // block, rows_of, 0)
    z_ref[...] = staged_ref[...].astype(z_ref.dtype)


def gate_kernel(pair_ref, wg_ref, gate_ref):
    rows, cols, width = pair_ref.shape
    values = pair_ref[...].astype(jnp.float32).reshape(rows * cols, width)
    center = values - jnp.mean(values, axis=-1, keepdims=True)
    spread = jnp.mean(center * center, axis=-1, keepdims=True)
    normed = (center * lax.rsqrt(spread + 1e-05)).astype(jnp.bfloat16)
    gate = jax.nn.sigmoid(jnp.dot(normed, wg_ref[...], preferred_element_type=jnp.float32))
    gate_ref[...] = gate.reshape(rows, cols, width)


def transition_kernel(mixed_ref, pair_ref, gate_ref, wo_ref, wu_ref, wd_ref, out_ref, gathered_ref, *, all_rows):
    rows, cols, width = pair_ref.shape
    pairs = mixed_ref.shape[0] // all_rows

    def norm(values):
        center = values - jnp.mean(values, axis=-1, keepdims=True)
        spread = jnp.mean(center * center, axis=-1, keepdims=True)
        return center * lax.rsqrt(spread + 1e-05)

    for step in range(all_rows // rows):

        @pl.when(pl.program_id(0) == step)
        def _():
            for i in range(rows):
                row = step * rows + i
                turned = mixed_ref[pl.ds(row, pairs, stride=all_rows), :].astype(jnp.float32).T
                gathered_ref[i * cols : (i + 1) * cols, :] = jnp.concatenate([turned[:cols], turned[cols:]], axis=1)

    mixed = gathered_ref[...]
    pair = pair_ref[...].astype(jnp.float32).reshape(rows * cols, width)
    gate = gate_ref[...].reshape(rows * cols, width)
    mixed_normed = norm(mixed).astype(jnp.bfloat16)
    middle = pair + gate * jnp.dot(mixed_normed, wo_ref[...], preferred_element_type=jnp.float32)
    trans_in = norm(middle).astype(jnp.bfloat16)
    hidden = jnp.maximum(jnp.dot(trans_in, wu_ref[...], preferred_element_type=jnp.float32), 0.0)
    result = middle + jnp.dot(hidden.astype(jnp.bfloat16), wd_ref[...], preferred_element_type=jnp.float32)
    out_ref[...] = result.astype(out_ref.dtype).reshape(rows, cols, width)


def body_fused(pair, mask, w_agate, w_aproj, w_bgate, w_bproj, w_gate, w_out, w_up, w_down, *, n_row, n_col):
    rows, cols, width = pair.shape
    n_dev = n_row * n_col
    hid = w_agate.shape[1]
    pairs = hid // n_dev // 2

    z = pl.pallas_call(
        functools.partial(project_kernel, block=rows),
        out_shape=jax.ShapeDtypeStruct((hid * rows, 2 * cols), jnp.bfloat16),
        in_specs=[pl.BlockSpec(memory_space=pltpu.SMEM)] + [pl.BlockSpec(memory_space=pltpu.VMEM)] * 5,
        scratch_shapes=[pltpu.VMEM((hid * rows, 2 * cols), jnp.float32)],
    )(mask, pair, w_agate, w_aproj, w_bgate, w_bproj)
    gate = pl.pallas_call(
        gate_kernel, out_shape=jax.ShapeDtypeStruct((rows, cols, width), jnp.float32)
    )(pair, w_gate)
    edges = z.reshape(n_dev, pairs, 2, rows, 2 * cols)
    edges = lax.all_to_all(edges, ("row", "col"), split_axis=0, concat_axis=0, tiled=True)
    mixed = pl.pallas_call(
        functools.partial(mix_kernel, n_col=n_col, side_major=False),
        out_shape=jax.ShapeDtypeStruct((n_dev, pairs, rows, 2 * cols), jnp.bfloat16),
        grid=(pairs,),
        in_specs=[pl.BlockSpec((n_dev, 1, 2, rows, 2 * cols), lambda hp: (0, hp, 0, 0, 0))],
        out_specs=pl.BlockSpec((n_dev, 1, rows, 2 * cols), lambda hp: (0, hp, 0, 0)),
    )(edges)
    mixed = lax.all_to_all(mixed, ("row", "col"), split_axis=0, concat_axis=0, tiled=True)
    mixed = mixed.reshape(n_dev * pairs * rows, 2 * cols)
    return pl.pallas_call(
        functools.partial(transition_kernel, all_rows=rows),
        out_shape=jax.ShapeDtypeStruct((rows, cols, width), jnp.bfloat16),
        grid=(2,),
        in_specs=[
            pl.BlockSpec(mixed.shape, lambda b: (0, 0)),
            pl.BlockSpec((rows // 2, cols, width), lambda b: (b, 0, 0)),
            pl.BlockSpec((rows // 2, cols, width), lambda b: (b, 0, 0)),
            pl.BlockSpec(w_out.shape, lambda b: (0, 0)),
            pl.BlockSpec(w_up.shape, lambda b: (0, 0)),
            pl.BlockSpec(w_down.shape, lambda b: (0, 0)),
        ],
        out_specs=pl.BlockSpec((rows // 2, cols, width), lambda b: (b, 0, 0)),
        scratch_shapes=[pltpu.VMEM((rows // 2 * cols, hid), jnp.float32)],
    )(mixed, pair, gate, w_out, w_up, w_down)


def body_rows(pair, mask, w_agate, w_aproj, w_bgate, w_bproj, w_gate, w_out, w_up, w_down):
    rows, cols, width = pair.shape
    pair_flat, gate, left, right = project(pair, mask, w_agate, w_aproj, w_bgate, w_bproj, w_gate)
    left_major = jnp.transpose(left.reshape(rows, cols, -1), (2, 0, 1))
    right_major = jnp.transpose(right.reshape(rows, cols, -1), (2, 0, 1))
    left_spread, right_spread = (
        lax.all_to_all(
            lax.all_to_all(left_major, "row", split_axis=0, concat_axis=1, tiled=True),
            "col",
            split_axis=1,
            concat_axis=2,
            tiled=True,
        ),
        lax.all_to_all(
            lax.all_to_all(right_major, "row", split_axis=0, concat_axis=1, tiled=True),
            "col",
            split_axis=1,
            concat_axis=2,
            tiled=True,
        ),
    )
    mixed = jnp.einsum(
        "cik,cjk->cij",
        lax.all_gather(left_spread, "col", axis=1, tiled=True),
        right_spread,
        preferred_element_type=jnp.float32,
    ).astype(jnp.bfloat16)
    mixed = lax.all_to_all(mixed, "row", split_axis=1, concat_axis=0, tiled=True)
    mixed_rows = jnp.transpose(mixed, (1, 2, 0)).astype(jnp.float32).reshape(rows * cols, -1)
    result = transition(pair_flat, gate, mixed_rows, w_out, w_up, w_down)
    return result.astype(jnp.bfloat16).reshape(rows, cols, width)


def solution(mesh):
    placed = (P("row", "col", None), P(), P(), P(), P(), P(), P(), P(), P(), P())
    n_row, n_col = mesh.shape["row"], mesh.shape["col"]

    def run(pair, mask, w_agate, *weights):
        hid = w_agate.shape[1]
        rows, cols = pair.shape[0] // n_row, pair.shape[1] // n_col
        if hid % (2 * n_row * n_col) == 0 and 2 * cols == 128 and rows % 16 == 0 and n_row * rows == n_col * cols:
            body = functools.partial(body_fused, n_row=n_row, n_col=n_col)
        elif hid % (n_row * n_col) == 0:
            body = functools.partial(body_split, n_row=n_row, n_col=n_col)
        else:
            body = body_rows
        mapped = jax.shard_map(
            body, mesh=mesh, in_specs=placed, out_specs=P("row", "col", None), check_vma=False
        )
        return mapped(pair, mask, w_agate, *weights)

    return run
```

```python
import functools

import jax
import jax.numpy as jnp
from jax import lax
from jax.experimental import pallas as pl
from jax.experimental.pallas import tpu as pltpu
from jax.sharding import PartitionSpec as P


def layer_norm(values):
    center = values - jnp.mean(values, axis=-1, keepdims=True)
    spread = jnp.mean(center * center, axis=-1, keepdims=True)
    return center * lax.rsqrt(spread + 1e-05)


def project(pair, mask, w_agate, w_aproj, w_bgate, w_bproj, w_gate):
    rows, cols, width = pair.shape
    present = mask.astype(jnp.float32)
    row_start = lax.axis_index("row") * rows
    col_start = lax.axis_index("col") * cols
    row_mask = lax.dynamic_slice_in_dim(present, row_start, rows, 0)
    col_mask = lax.dynamic_slice_in_dim(present, col_start, cols, 0)
    pair_mask = (row_mask[:, None] * col_mask[None, :]).reshape(rows * cols, 1)
    pair_flat = pair.astype(jnp.float32).reshape(rows * cols, width)
    normed = layer_norm(pair_flat).astype(jnp.bfloat16)
    gate = jax.nn.sigmoid(jnp.dot(normed, w_gate, preferred_element_type=jnp.float32))
    left = (
        jax.nn.sigmoid(jnp.dot(normed, w_agate, preferred_element_type=jnp.float32))
        * jnp.dot(normed, w_aproj, preferred_element_type=jnp.float32)
        * pair_mask
    )
    right = (
        jax.nn.sigmoid(jnp.dot(normed, w_bgate, preferred_element_type=jnp.float32))
        * jnp.dot(normed, w_bproj, preferred_element_type=jnp.float32)
        * pair_mask
    )
    return pair_flat, gate, left.astype(jnp.bfloat16), right.astype(jnp.bfloat16)


def transition(pair_flat, gate, mixed_rows, w_out, w_up, w_down):
    mixed_normed = layer_norm(mixed_rows).astype(jnp.bfloat16)
    middle = pair_flat + gate * jnp.dot(mixed_normed, w_out, preferred_element_type=jnp.float32)
    trans_in = layer_norm(middle).astype(jnp.bfloat16)
    trans_hidden = jax.nn.relu(jnp.dot(trans_in, w_up, preferred_element_type=jnp.float32)).astype(
        jnp.bfloat16
    )
    return middle + jnp.dot(trans_hidden, w_down, preferred_element_type=jnp.float32)


def body_split(pair, mask, w_agate, w_aproj, w_bgate, w_bproj, w_gate, w_out, w_up, w_down, *, n_row, n_col):
    rows, cols, width = pair.shape
    n_dev = n_row * n_col
    pair_flat, gate, left, right = project(pair, mask, w_agate, w_aproj, w_bgate, w_bproj, w_gate)
    hid = left.shape[-1]
    group = hid // n_dev
    edges = jnp.stack([left, right], axis=0).reshape(2, rows, cols, n_dev, group)
    edges = jnp.transpose(edges, (3, 0, 4, 1, 2))
    edges = lax.all_to_all(edges, ("row", "col"), split_axis=0, concat_axis=0, tiled=True)
    edges = edges.reshape(n_row, n_col, 2, group, rows, cols)
    edges = jnp.transpose(edges, (2, 3, 0, 4, 1, 5)).reshape(2, group, n_row * rows, n_col * cols)
    mixed = jnp.einsum(
        "cik,cjk->cij", edges[0], edges[1], preferred_element_type=jnp.float32
    ).astype(jnp.bfloat16)
    mixed = mixed.reshape(group, n_row, rows, n_col, cols)
    mixed = jnp.transpose(mixed, (1, 3, 0, 2, 4)).reshape(n_dev, group, rows, cols)
    mixed = lax.all_to_all(mixed, ("row", "col"), split_axis=0, concat_axis=0, tiled=True)
    mixed_rows = jnp.transpose(mixed.reshape(hid, rows, cols), (1, 2, 0))
    mixed_rows = mixed_rows.astype(jnp.float32).reshape(rows * cols, hid)
    result = transition(pair_flat, gate, mixed_rows, w_out, w_up, w_down)
    return result.astype(jnp.bfloat16).reshape(rows, cols, width)


def mix_kernel(edges_ref, out_ref, *, n_col, side_major=True):
    n_dev, rows, lanes = edges_ref.shape[0], edges_ref.shape[3], edges_ref.shape[4]
    pairs = edges_ref.shape[2] if side_major else edges_ref.shape[1]
    n_row = n_dev // n_col
    cols = lanes // 2
    parity = (lax.broadcasted_iota(jnp.int32, (1, n_col * lanes), 1) // cols) % 2
    for hp in range(pairs):

        def chunk(source, side):
            return edges_ref[source, side, hp] if side_major else edges_ref[source, hp, side]

        def whole(side):
            return jnp.concatenate(
                [
                    jnp.concatenate([chunk(r * n_col + c, side) for c in range(n_col)], axis=1)
                    for r in range(n_row)
                ],
                axis=0,
            )

        left = whole(0)
        right = whole(1)
        right_even = jnp.where(parity == 0, right, jnp.zeros_like(right))
        right_odd = jnp.where(parity == 1, right, jnp.zeros_like(right))
        for c in range(n_col):
            block = slice(c * cols, (c + 1) * cols)
            rhs = jnp.concatenate([right_even[block], right_odd[block]], axis=0)
            mixed = lax.dot_general(
                left, rhs, (((1,), (1,)), ((), ())), preferred_element_type=jnp.float32
            ).astype(out_ref.dtype)
            for r in range(n_row):
                out_ref[r * n_col + c, hp] = mixed[r * rows : (r + 1) * rows]


def body_kernel(pair, mask, w_agate, w_aproj, w_bgate, w_bproj, w_gate, w_out, w_up, w_down, *, n_row, n_col):
    rows, cols, width = pair.shape
    n_dev = n_row * n_col
    pair_flat, gate, left, right = project(pair, mask, w_agate, w_aproj, w_bgate, w_bproj, w_gate)
    hid = left.shape[-1]
    pairs = hid // n_dev // 2

    def chunks(edges):
        edges = jnp.transpose(edges.reshape(rows, cols, n_dev, pairs, 2), (2, 3, 0, 4, 1))
        return edges.reshape(n_dev, pairs, rows, 2 * cols)

    edges = jnp.stack([chunks(left), chunks(right)], axis=1)
    edges = lax.all_to_all(edges, ("row", "col"), split_axis=0, concat_axis=0, tiled=True)
    mixed = pl.pallas_call(
        functools.partial(mix_kernel, n_col=n_col),
        out_shape=jax.ShapeDtypeStruct((n_dev, pairs, rows, 2 * cols), jnp.bfloat16),
    )(edges)
    mixed = lax.all_to_all(mixed, ("row", "col"), split_axis=0, concat_axis=0, tiled=True)
    mixed = jnp.transpose(mixed.reshape(n_dev, pairs, rows, 2, cols), (2, 4, 0, 1, 3))
    mixed_rows = mixed.astype(jnp.float32).reshape(rows * cols, hid)
    result = transition(pair_flat, gate, mixed_rows, w_out, w_up, w_down)
    return result.astype(jnp.bfloat16).reshape(rows, cols, width)


def project_kernel(mask_ref, pair_ref, wag_ref, wap_ref, wbg_ref, wbp_ref, z_ref, staged_ref, *, block):
    rows, cols, width = pair_ref.shape
    quarter = wag_ref.shape[1] // 2

    def paired(w_ref):
        turned = w_ref[...].astype(jnp.float32).T.astype(jnp.bfloat16)
        return jnp.concatenate([turned[:quarter], turned[quarter:]], axis=1)

    w2 = jnp.concatenate([paired(w) for w in (wag_ref, wap_ref, wbg_ref, wbp_ref)], axis=0)
    row_start = lax.axis_index("row") * rows
    col_start = lax.axis_index("col") * cols
    lane = lax.broadcasted_iota(jnp.int32, (1, 2 * cols), 1) % cols
    col_mask = jnp.zeros((1, 2 * cols), jnp.float32)
    for k in range(cols):
        col_mask = jnp.where(lane == k, mask_ref[col_start + k].astype(jnp.float32), col_mask)

    def rows_of(step, carry):
        first = pl.multiple_of(step * block, block)
        values = pair_ref[pl.ds(first, block)].astype(jnp.float32).reshape(block * cols, width)
        center = values - jnp.mean(values, axis=-1, keepdims=True)
        spread = jnp.mean(center * center, axis=-1, keepdims=True)
        normed = (center * lax.rsqrt(spread + 1e-05)).astype(jnp.bfloat16)
        zeros = jnp.zeros_like(normed)
        top = jnp.concatenate([normed, zeros], axis=1).reshape(block, cols, 2 * width)
        bottom = jnp.concatenate([zeros, normed], axis=1).reshape(block, cols, 2 * width)
        doubled = jnp.concatenate([top, bottom], axis=1).reshape(block * 2 * cols, 2 * width)
        proj = lax.dot_general(
            w2, doubled, (((1,), (1,)), ((), ())), preferred_element_type=jnp.float32
        )
        for i in range(block):
            part = proj[:, i * 2 * cols : (i + 1) * 2 * cols]
            present = col_mask * mask_ref[row_start + first + i].astype(jnp.float32)
            left = jax.nn.sigmoid(part[0:quarter]) * part[quarter : 2 * quarter] * present
            right = jax.nn.sigmoid(part[2 * quarter : 3 * quarter]) * part[3 * quarter :] * present
            staged_ref[pl.ds(first + i, quarter, stride=2 * rows), :] = left
            staged_ref[pl.ds(rows + first + i, quarter, stride=2 * rows), :] = right
        return carry

    lax.fori_loop(0, rows // block, rows_of, 0)
    z_ref[...] = staged_ref[...].astype(z_ref.dtype)


def gate_kernel(pair_ref, wg_ref, gate_ref):
    rows, cols, width = pair_ref.shape
    values = pair_ref[...].astype(jnp.float32).reshape(rows * cols, width)
    center = values - jnp.mean(values, axis=-1, keepdims=True)
    spread = jnp.mean(center * center, axis=-1, keepdims=True)
    normed = (center * lax.rsqrt(spread + 1e-05)).astype(jnp.bfloat16)
    gate = jax.nn.sigmoid(jnp.dot(normed, wg_ref[...], preferred_element_type=jnp.float32))
    gate_ref[...] = gate.reshape(rows, cols, width)


def transition_kernel(mixed_ref, pair_ref, gate_ref, wo_ref, wu_ref, wd_ref, out_ref):
    rows, cols, width = pair_ref.shape
    pairs = mixed_ref.shape[0] // rows

    def norm(values):
        center = values - jnp.mean(values, axis=-1, keepdims=True)
        spread = jnp.mean(center * center, axis=-1, keepdims=True)
        return center * lax.rsqrt(spread + 1e-05)

    parts = []
    for i in range(rows):
        turned = mixed_ref[pl.ds(i, pairs, stride=rows), :].astype(jnp.float32).T
        parts.append(jnp.concatenate([turned[:cols], turned[cols:]], axis=1))
    mixed = jnp.concatenate(parts, axis=0)
    pair = pair_ref[...].astype(jnp.float32).reshape(rows * cols, width)
    gate = gate_ref[...].reshape(rows * cols, width)
    mixed_normed = norm(mixed).astype(jnp.bfloat16)
    middle = pair + gate * jnp.dot(mixed_normed, wo_ref[...], preferred_element_type=jnp.float32)
    trans_in = norm(middle).astype(jnp.bfloat16)
    result = middle
    span = 128 if wu_ref.shape[1] % 128 == 0 else wu_ref.shape[1]
    for t in range(wu_ref.shape[1] // span):
        cut = slice(t * span, (t + 1) * span)
        hidden = jnp.maximum(jnp.dot(trans_in, wu_ref[:, cut], preferred_element_type=jnp.float32), 0.0)
        result = result + jnp.dot(hidden.astype(jnp.bfloat16), wd_ref[cut, :], preferred_element_type=jnp.float32)
    out_ref[...] = result.astype(out_ref.dtype).reshape(rows, cols, width)


def body_fused(pair, mask, w_agate, w_aproj, w_bgate, w_bproj, w_gate, w_out, w_up, w_down, *, n_row, n_col):
    rows, cols, width = pair.shape
    n_dev = n_row * n_col
    hid = w_agate.shape[1]
    pairs = hid // n_dev // 2

    z = pl.pallas_call(
        functools.partial(project_kernel, block=rows),
        out_shape=jax.ShapeDtypeStruct((hid * rows, 2 * cols), jnp.bfloat16),
        in_specs=[pl.BlockSpec(memory_space=pltpu.SMEM)] + [pl.BlockSpec(memory_space=pltpu.VMEM)] * 5,
        scratch_shapes=[pltpu.VMEM((hid * rows, 2 * cols), jnp.float32)],
    )(mask, pair, w_agate, w_aproj, w_bgate, w_bproj)
    gate = pl.pallas_call(
        gate_kernel, out_shape=jax.ShapeDtypeStruct((rows, cols, width), jnp.float32)
    )(pair, w_gate)
    edges = z.reshape(n_dev, pairs, 2, rows, 2 * cols)
    edges = lax.all_to_all(edges, ("row", "col"), split_axis=0, concat_axis=0, tiled=True)
    mixed = pl.pallas_call(
        functools.partial(mix_kernel, n_col=n_col, side_major=False),
        out_shape=jax.ShapeDtypeStruct((n_dev, pairs, rows, 2 * cols), jnp.bfloat16),
        grid=(pairs,),
        in_specs=[pl.BlockSpec((n_dev, 1, 2, rows, 2 * cols), lambda hp: (0, hp, 0, 0, 0))],
        out_specs=pl.BlockSpec((n_dev, 1, rows, 2 * cols), lambda hp: (0, hp, 0, 0)),
    )(edges)
    mixed = lax.all_to_all(mixed, ("row", "col"), split_axis=0, concat_axis=0, tiled=True)
    mixed = mixed.reshape(n_dev * pairs * rows, 2 * cols)
    return pl.pallas_call(
        transition_kernel,
        out_shape=jax.ShapeDtypeStruct((rows, cols, width), jnp.bfloat16),
    )(mixed, pair, gate, w_out, w_up, w_down)


def body_rows(pair, mask, w_agate, w_aproj, w_bgate, w_bproj, w_gate, w_out, w_up, w_down):
    rows, cols, width = pair.shape
    pair_flat, gate, left, right = project(pair, mask, w_agate, w_aproj, w_bgate, w_bproj, w_gate)
    left_major = jnp.transpose(left.reshape(rows, cols, -1), (2, 0, 1))
    right_major = jnp.transpose(right.reshape(rows, cols, -1), (2, 0, 1))
    left_spread, right_spread = (
        lax.all_to_all(
            lax.all_to_all(left_major, "row", split_axis=0, concat_axis=1, tiled=True),
            "col",
            split_axis=1,
            concat_axis=2,
            tiled=True,
        ),
        lax.all_to_all(
            lax.all_to_all(right_major, "row", split_axis=0, concat_axis=1, tiled=True),
            "col",
            split_axis=1,
            concat_axis=2,
            tiled=True,
        ),
    )
    mixed = jnp.einsum(
        "cik,cjk->cij",
        lax.all_gather(left_spread, "col", axis=1, tiled=True),
        right_spread,
        preferred_element_type=jnp.float32,
    ).astype(jnp.bfloat16)
    mixed = lax.all_to_all(mixed, "row", split_axis=1, concat_axis=0, tiled=True)
    mixed_rows = jnp.transpose(mixed, (1, 2, 0)).astype(jnp.float32).reshape(rows * cols, -1)
    result = transition(pair_flat, gate, mixed_rows, w_out, w_up, w_down)
    return result.astype(jnp.bfloat16).reshape(rows, cols, width)


def solution(mesh):
    placed = (P("row", "col", None), P(), P(), P(), P(), P(), P(), P(), P(), P())
    n_row, n_col = mesh.shape["row"], mesh.shape["col"]

    def run(pair, mask, w_agate, *weights):
        hid = w_agate.shape[1]
        rows, cols = pair.shape[0] // n_row, pair.shape[1] // n_col
        if hid % (2 * n_row * n_col) == 0 and 2 * cols == 128 and rows % 16 == 0 and n_row * rows == n_col * cols:
            body = functools.partial(body_fused, n_row=n_row, n_col=n_col)
        elif hid % (n_row * n_col) == 0:
            body = functools.partial(body_split, n_row=n_row, n_col=n_col)
        else:
            body = body_rows
        mapped = jax.shard_map(
            body, mesh=mesh, in_specs=placed, out_specs=P("row", "col", None), check_vma=False
        )
        return mapped(pair, mask, w_agate, *weights)

    return run
```

```python
import functools

import jax
import jax.numpy as jnp
from jax import lax
from jax.experimental import pallas as pl
from jax.experimental.pallas import tpu as pltpu
from jax.sharding import PartitionSpec as P


def layer_norm(values):
    center = values - jnp.mean(values, axis=-1, keepdims=True)
    spread = jnp.mean(center * center, axis=-1, keepdims=True)
    return center * lax.rsqrt(spread + 1e-05)


def project(pair, mask, w_agate, w_aproj, w_bgate, w_bproj, w_gate):
    rows, cols, width = pair.shape
    present = mask.astype(jnp.float32)
    row_start = lax.axis_index("row") * rows
    col_start = lax.axis_index("col") * cols
    row_mask = lax.dynamic_slice_in_dim(present, row_start, rows, 0)
    col_mask = lax.dynamic_slice_in_dim(present, col_start, cols, 0)
    pair_mask = (row_mask[:, None] * col_mask[None, :]).reshape(rows * cols, 1)
    pair_flat = pair.astype(jnp.float32).reshape(rows * cols, width)
    normed = layer_norm(pair_flat).astype(jnp.bfloat16)
    gate = jax.nn.sigmoid(jnp.dot(normed, w_gate, preferred_element_type=jnp.float32))
    left = (
        jax.nn.sigmoid(jnp.dot(normed, w_agate, preferred_element_type=jnp.float32))
        * jnp.dot(normed, w_aproj, preferred_element_type=jnp.float32)
        * pair_mask
    )
    right = (
        jax.nn.sigmoid(jnp.dot(normed, w_bgate, preferred_element_type=jnp.float32))
        * jnp.dot(normed, w_bproj, preferred_element_type=jnp.float32)
        * pair_mask
    )
    return pair_flat, gate, left.astype(jnp.bfloat16), right.astype(jnp.bfloat16)


def transition(pair_flat, gate, mixed_rows, w_out, w_up, w_down):
    mixed_normed = layer_norm(mixed_rows).astype(jnp.bfloat16)
    middle = pair_flat + gate * jnp.dot(mixed_normed, w_out, preferred_element_type=jnp.float32)
    trans_in = layer_norm(middle).astype(jnp.bfloat16)
    trans_hidden = jax.nn.relu(jnp.dot(trans_in, w_up, preferred_element_type=jnp.float32)).astype(
        jnp.bfloat16
    )
    return middle + jnp.dot(trans_hidden, w_down, preferred_element_type=jnp.float32)


def body_split(pair, mask, w_agate, w_aproj, w_bgate, w_bproj, w_gate, w_out, w_up, w_down, *, n_row, n_col):
    rows, cols, width = pair.shape
    n_dev = n_row * n_col
    pair_flat, gate, left, right = project(pair, mask, w_agate, w_aproj, w_bgate, w_bproj, w_gate)
    hid = left.shape[-1]
    group = hid // n_dev
    edges = jnp.stack([left, right], axis=0).reshape(2, rows, cols, n_dev, group)
    edges = jnp.transpose(edges, (3, 0, 4, 1, 2))
    edges = lax.all_to_all(edges, ("row", "col"), split_axis=0, concat_axis=0, tiled=True)
    edges = edges.reshape(n_row, n_col, 2, group, rows, cols)
    edges = jnp.transpose(edges, (2, 3, 0, 4, 1, 5)).reshape(2, group, n_row * rows, n_col * cols)
    mixed = jnp.einsum(
        "cik,cjk->cij", edges[0], edges[1], preferred_element_type=jnp.float32
    ).astype(jnp.bfloat16)
    mixed = mixed.reshape(group, n_row, rows, n_col, cols)
    mixed = jnp.transpose(mixed, (1, 3, 0, 2, 4)).reshape(n_dev, group, rows, cols)
    mixed = lax.all_to_all(mixed, ("row", "col"), split_axis=0, concat_axis=0, tiled=True)
    mixed_rows = jnp.transpose(mixed.reshape(hid, rows, cols), (1, 2, 0))
    mixed_rows = mixed_rows.astype(jnp.float32).reshape(rows * cols, hid)
    result = transition(pair_flat, gate, mixed_rows, w_out, w_up, w_down)
    return result.astype(jnp.bfloat16).reshape(rows, cols, width)


def mix_kernel(edges_ref, out_ref, *, n_col, side_major=True):
    n_dev, rows, lanes = edges_ref.shape[0], edges_ref.shape[3], edges_ref.shape[4]
    pairs = edges_ref.shape[2] if side_major else edges_ref.shape[1]
    n_row = n_dev // n_col
    cols = lanes // 2
    parity = (lax.broadcasted_iota(jnp.int32, (1, n_col * lanes), 1) // cols) % 2
    for hp in range(pairs):

        def chunk(source, side):
            return edges_ref[source, side, hp] if side_major else edges_ref[source, hp, side]

        def whole(side):
            return jnp.concatenate(
                [
                    jnp.concatenate([chunk(r * n_col + c, side) for c in range(n_col)], axis=1)
                    for r in range(n_row)
                ],
                axis=0,
            )

        left = whole(0)
        right = whole(1)
        right_even = jnp.where(parity == 0, right, jnp.zeros_like(right))
        right_odd = jnp.where(parity == 1, right, jnp.zeros_like(right))
        for c in range(n_col):
            block = slice(c * cols, (c + 1) * cols)
            rhs = jnp.concatenate([right_even[block], right_odd[block]], axis=0)
            mixed = lax.dot_general(
                left, rhs, (((1,), (1,)), ((), ())), preferred_element_type=jnp.float32
            ).astype(out_ref.dtype)
            for r in range(n_row):
                out_ref[r * n_col + c, hp] = mixed[r * rows : (r + 1) * rows]


def body_kernel(pair, mask, w_agate, w_aproj, w_bgate, w_bproj, w_gate, w_out, w_up, w_down, *, n_row, n_col):
    rows, cols, width = pair.shape
    n_dev = n_row * n_col
    pair_flat, gate, left, right = project(pair, mask, w_agate, w_aproj, w_bgate, w_bproj, w_gate)
    hid = left.shape[-1]
    pairs = hid // n_dev // 2

    def chunks(edges):
        edges = jnp.transpose(edges.reshape(rows, cols, n_dev, pairs, 2), (2, 3, 0, 4, 1))
        return edges.reshape(n_dev, pairs, rows, 2 * cols)

    edges = jnp.stack([chunks(left), chunks(right)], axis=1)
    edges = lax.all_to_all(edges, ("row", "col"), split_axis=0, concat_axis=0, tiled=True)
    mixed = pl.pallas_call(
        functools.partial(mix_kernel, n_col=n_col),
        out_shape=jax.ShapeDtypeStruct((n_dev, pairs, rows, 2 * cols), jnp.bfloat16),
    )(edges)
    mixed = lax.all_to_all(mixed, ("row", "col"), split_axis=0, concat_axis=0, tiled=True)
    mixed = jnp.transpose(mixed.reshape(n_dev, pairs, rows, 2, cols), (2, 4, 0, 1, 3))
    mixed_rows = mixed.astype(jnp.float32).reshape(rows * cols, hid)
    result = transition(pair_flat, gate, mixed_rows, w_out, w_up, w_down)
    return result.astype(jnp.bfloat16).reshape(rows, cols, width)


def project_kernel(mask_ref, pair_ref, wag_ref, wap_ref, wbg_ref, wbp_ref, z_ref, staged_ref, *, block):
    rows, cols, width = pair_ref.shape
    quarter = wag_ref.shape[1] // 2

    def paired(w_ref):
        turned = w_ref[...].astype(jnp.float32).T.astype(jnp.bfloat16)
        return jnp.concatenate([turned[:quarter], turned[quarter:]], axis=1)

    w2 = jnp.concatenate([paired(w) for w in (wag_ref, wap_ref, wbg_ref, wbp_ref)], axis=0)
    row_start = lax.axis_index("row") * rows * pl.num_programs(0) + pl.program_id(0) * rows
    col_start = lax.axis_index("col") * cols
    lane = lax.broadcasted_iota(jnp.int32, (1, 2 * cols), 1) % cols
    col_mask = jnp.zeros((1, 2 * cols), jnp.float32)
    for k in range(cols):
        col_mask = jnp.where(lane == k, mask_ref[col_start + k].astype(jnp.float32), col_mask)

    def rows_of(step, carry):
        first = pl.multiple_of(step * block, block)
        values = pair_ref[pl.ds(first, block)].astype(jnp.float32).reshape(block * cols, width)
        center = values - jnp.mean(values, axis=-1, keepdims=True)
        spread = jnp.mean(center * center, axis=-1, keepdims=True)
        normed = (center * lax.rsqrt(spread + 1e-05)).astype(jnp.bfloat16)
        zeros = jnp.zeros_like(normed)
        top = jnp.concatenate([normed, zeros], axis=1).reshape(block, cols, 2 * width)
        bottom = jnp.concatenate([zeros, normed], axis=1).reshape(block, cols, 2 * width)
        doubled = jnp.concatenate([top, bottom], axis=1).reshape(block * 2 * cols, 2 * width)
        proj = lax.dot_general(
            w2, doubled, (((1,), (1,)), ((), ())), preferred_element_type=jnp.float32
        )
        for i in range(block):
            part = proj[:, i * 2 * cols : (i + 1) * 2 * cols]
            present = col_mask * mask_ref[row_start + first + i].astype(jnp.float32)
            left = jax.nn.sigmoid(part[0:quarter]) * part[quarter : 2 * quarter] * present
            right = jax.nn.sigmoid(part[2 * quarter : 3 * quarter]) * part[3 * quarter :] * present
            staged_ref[pl.ds(first + i, quarter, stride=2 * rows), :] = left
            staged_ref[pl.ds(rows + first + i, quarter, stride=2 * rows), :] = right
        return carry

    lax.fori_loop(0, rows // block, rows_of, 0)
    z_ref[...] = staged_ref[...].reshape(z_ref.shape).astype(z_ref.dtype)


def gate_kernel(pair_ref, wg_ref, gate_ref):
    rows, cols, width = pair_ref.shape
    values = pair_ref[...].astype(jnp.float32).reshape(rows * cols, width)
    center = values - jnp.mean(values, axis=-1, keepdims=True)
    spread = jnp.mean(center * center, axis=-1, keepdims=True)
    normed = (center * lax.rsqrt(spread + 1e-05)).astype(jnp.bfloat16)
    gate = jax.nn.sigmoid(jnp.dot(normed, wg_ref[...], preferred_element_type=jnp.float32))
    gate_ref[...] = gate.reshape(rows, cols, width)


def transition_kernel(mixed_ref, pair_ref, gate_ref, wo_ref, wu_ref, wd_ref, out_ref):
    rows, cols, width = pair_ref.shape
    pairs = mixed_ref.shape[0] // rows

    def norm(values):
        center = values - jnp.mean(values, axis=-1, keepdims=True)
        spread = jnp.mean(center * center, axis=-1, keepdims=True)
        return center * lax.rsqrt(spread + 1e-05)

    parts = []
    for i in range(rows):
        turned = mixed_ref[pl.ds(i, pairs, stride=rows), :].astype(jnp.float32).T
        parts.append(jnp.concatenate([turned[:cols], turned[cols:]], axis=1))
    mixed = jnp.concatenate(parts, axis=0)
    pair = pair_ref[...].astype(jnp.float32).reshape(rows * cols, width)
    gate = gate_ref[...].reshape(rows * cols, width)
    mixed_normed = norm(mixed).astype(jnp.bfloat16)
    middle = pair + gate * jnp.dot(mixed_normed, wo_ref[...], preferred_element_type=jnp.float32)
    trans_in = norm(middle).astype(jnp.bfloat16)
    hidden = jnp.maximum(jnp.dot(trans_in, wu_ref[...], preferred_element_type=jnp.float32), 0.0)
    result = middle + jnp.dot(hidden.astype(jnp.bfloat16), wd_ref[...], preferred_element_type=jnp.float32)
    out_ref[...] = result.astype(out_ref.dtype).reshape(rows, cols, width)


def body_fused(pair, mask, w_agate, w_aproj, w_bgate, w_bproj, w_gate, w_out, w_up, w_down, *, n_row, n_col):
    rows, cols, width = pair.shape
    n_dev = n_row * n_col
    hid = w_agate.shape[1]
    pairs = hid // n_dev // 2

    half = rows // 2
    weight = pl.BlockSpec(w_agate.shape, lambda b: (0, 0))
    z = pl.pallas_call(
        functools.partial(project_kernel, block=half),
        out_shape=jax.ShapeDtypeStruct((hid // 2, 2, rows, 2 * cols), jnp.bfloat16),
        grid=(2,),
        in_specs=[
            pl.BlockSpec(memory_space=pltpu.SMEM),
            pl.BlockSpec((half, cols, width), lambda b: (b, 0, 0)),
            weight,
            weight,
            weight,
            weight,
        ],
        out_specs=pl.BlockSpec((hid // 2, 2, half, 2 * cols), lambda b: (0, 0, b, 0)),
        scratch_shapes=[pltpu.VMEM((hid * half, 2 * cols), jnp.float32)],
    )(mask, pair, w_agate, w_aproj, w_bgate, w_bproj)
    gate = pl.pallas_call(
        gate_kernel, out_shape=jax.ShapeDtypeStruct((rows, cols, width), jnp.float32)
    )(pair, w_gate)
    edges = z.reshape(n_dev, pairs, 2, rows, 2 * cols)
    edges = lax.all_to_all(edges, ("row", "col"), split_axis=0, concat_axis=0, tiled=True)
    mixed = pl.pallas_call(
        functools.partial(mix_kernel, n_col=n_col, side_major=False),
        out_shape=jax.ShapeDtypeStruct((n_dev, pairs, rows, 2 * cols), jnp.bfloat16),
        grid=(pairs,),
        in_specs=[pl.BlockSpec((n_dev, 1, 2, rows, 2 * cols), lambda hp: (0, hp, 0, 0, 0))],
        out_specs=pl.BlockSpec((n_dev, 1, rows, 2 * cols), lambda hp: (0, hp, 0, 0)),
    )(edges)
    mixed = lax.all_to_all(mixed, ("row", "col"), split_axis=0, concat_axis=0, tiled=True)
    mixed = mixed.reshape(n_dev * pairs * rows, 2 * cols)
    return pl.pallas_call(
        transition_kernel,
        out_shape=jax.ShapeDtypeStruct((rows, cols, width), jnp.bfloat16),
    )(mixed, pair, gate, w_out, w_up, w_down)


def body_rows(pair, mask, w_agate, w_aproj, w_bgate, w_bproj, w_gate, w_out, w_up, w_down):
    rows, cols, width = pair.shape
    pair_flat, gate, left, right = project(pair, mask, w_agate, w_aproj, w_bgate, w_bproj, w_gate)
    left_major = jnp.transpose(left.reshape(rows, cols, -1), (2, 0, 1))
    right_major = jnp.transpose(right.reshape(rows, cols, -1), (2, 0, 1))
    left_spread, right_spread = (
        lax.all_to_all(
            lax.all_to_all(left_major, "row", split_axis=0, concat_axis=1, tiled=True),
            "col",
            split_axis=1,
            concat_axis=2,
            tiled=True,
        ),
        lax.all_to_all(
            lax.all_to_all(right_major, "row", split_axis=0, concat_axis=1, tiled=True),
            "col",
            split_axis=1,
            concat_axis=2,
            tiled=True,
        ),
    )
    mixed = jnp.einsum(
        "cik,cjk->cij",
        lax.all_gather(left_spread, "col", axis=1, tiled=True),
        right_spread,
        preferred_element_type=jnp.float32,
    ).astype(jnp.bfloat16)
    mixed = lax.all_to_all(mixed, "row", split_axis=1, concat_axis=0, tiled=True)
    mixed_rows = jnp.transpose(mixed, (1, 2, 0)).astype(jnp.float32).reshape(rows * cols, -1)
    result = transition(pair_flat, gate, mixed_rows, w_out, w_up, w_down)
    return result.astype(jnp.bfloat16).reshape(rows, cols, width)


def solution(mesh):
    placed = (P("row", "col", None), P(), P(), P(), P(), P(), P(), P(), P(), P())
    n_row, n_col = mesh.shape["row"], mesh.shape["col"]

    def run(pair, mask, w_agate, *weights):
        hid = w_agate.shape[1]
        rows, cols = pair.shape[0] // n_row, pair.shape[1] // n_col
        if hid % (2 * n_row * n_col) == 0 and 2 * cols == 128 and rows % 32 == 0 and n_row * rows == n_col * cols:
            body = functools.partial(body_fused, n_row=n_row, n_col=n_col)
        elif hid % (n_row * n_col) == 0:
            body = functools.partial(body_split, n_row=n_row, n_col=n_col)
        else:
            body = body_rows
        mapped = jax.shard_map(
            body, mesh=mesh, in_specs=placed, out_specs=P("row", "col", None), check_vma=False
        )
        return mapped(pair, mask, w_agate, *weights)

    return run
```

```python
import functools

import jax
import jax.numpy as jnp
from jax import lax
from jax.experimental import pallas as pl
from jax.experimental.pallas import tpu as pltpu
from jax.sharding import PartitionSpec as P


def layer_norm(values):
    center = values - jnp.mean(values, axis=-1, keepdims=True)
    spread = jnp.mean(center * center, axis=-1, keepdims=True)
    return center * lax.rsqrt(spread + 1e-05)


def project(pair, mask, w_agate, w_aproj, w_bgate, w_bproj, w_gate):
    rows, cols, width = pair.shape
    present = mask.astype(jnp.float32)
    row_start = lax.axis_index("row") * rows
    col_start = lax.axis_index("col") * cols
    row_mask = lax.dynamic_slice_in_dim(present, row_start, rows, 0)
    col_mask = lax.dynamic_slice_in_dim(present, col_start, cols, 0)
    pair_mask = (row_mask[:, None] * col_mask[None, :]).reshape(rows * cols, 1)
    pair_flat = pair.astype(jnp.float32).reshape(rows * cols, width)
    normed = layer_norm(pair_flat).astype(jnp.bfloat16)
    gate = jax.nn.sigmoid(jnp.dot(normed, w_gate, preferred_element_type=jnp.float32))
    left = (
        jax.nn.sigmoid(jnp.dot(normed, w_agate, preferred_element_type=jnp.float32))
        * jnp.dot(normed, w_aproj, preferred_element_type=jnp.float32)
        * pair_mask
    )
    right = (
        jax.nn.sigmoid(jnp.dot(normed, w_bgate, preferred_element_type=jnp.float32))
        * jnp.dot(normed, w_bproj, preferred_element_type=jnp.float32)
        * pair_mask
    )
    return pair_flat, gate, left.astype(jnp.bfloat16), right.astype(jnp.bfloat16)


def transition(pair_flat, gate, mixed_rows, w_out, w_up, w_down):
    mixed_normed = layer_norm(mixed_rows).astype(jnp.bfloat16)
    middle = pair_flat + gate * jnp.dot(mixed_normed, w_out, preferred_element_type=jnp.float32)
    trans_in = layer_norm(middle).astype(jnp.bfloat16)
    trans_hidden = jax.nn.relu(jnp.dot(trans_in, w_up, preferred_element_type=jnp.float32)).astype(
        jnp.bfloat16
    )
    return middle + jnp.dot(trans_hidden, w_down, preferred_element_type=jnp.float32)


def body_split(pair, mask, w_agate, w_aproj, w_bgate, w_bproj, w_gate, w_out, w_up, w_down, *, n_row, n_col):
    rows, cols, width = pair.shape
    n_dev = n_row * n_col
    pair_flat, gate, left, right = project(pair, mask, w_agate, w_aproj, w_bgate, w_bproj, w_gate)
    hid = left.shape[-1]
    group = hid // n_dev
    edges = jnp.stack([left, right], axis=0).reshape(2, rows, cols, n_dev, group)
    edges = jnp.transpose(edges, (3, 0, 4, 1, 2))
    edges = lax.all_to_all(edges, ("row", "col"), split_axis=0, concat_axis=0, tiled=True)
    edges = edges.reshape(n_row, n_col, 2, group, rows, cols)
    edges = jnp.transpose(edges, (2, 3, 0, 4, 1, 5)).reshape(2, group, n_row * rows, n_col * cols)
    mixed = jnp.einsum(
        "cik,cjk->cij", edges[0], edges[1], preferred_element_type=jnp.float32
    ).astype(jnp.bfloat16)
    mixed = mixed.reshape(group, n_row, rows, n_col, cols)
    mixed = jnp.transpose(mixed, (1, 3, 0, 2, 4)).reshape(n_dev, group, rows, cols)
    mixed = lax.all_to_all(mixed, ("row", "col"), split_axis=0, concat_axis=0, tiled=True)
    mixed_rows = jnp.transpose(mixed.reshape(hid, rows, cols), (1, 2, 0))
    mixed_rows = mixed_rows.astype(jnp.float32).reshape(rows * cols, hid)
    result = transition(pair_flat, gate, mixed_rows, w_out, w_up, w_down)
    return result.astype(jnp.bfloat16).reshape(rows, cols, width)


def mix_kernel(edges_ref, out_ref, *, n_col, side_major=True):
    n_dev, rows, lanes = edges_ref.shape[0], edges_ref.shape[3], edges_ref.shape[4]
    pairs = edges_ref.shape[2] if side_major else edges_ref.shape[1]
    n_row = n_dev // n_col
    cols = lanes // 2
    parity = (lax.broadcasted_iota(jnp.int32, (1, n_col * lanes), 1) // cols) % 2
    for hp in range(pairs):

        def chunk(source, side):
            return edges_ref[source, side, hp] if side_major else edges_ref[source, hp, side]

        def whole(side):
            return jnp.concatenate(
                [
                    jnp.concatenate([chunk(r * n_col + c, side) for c in range(n_col)], axis=1)
                    for r in range(n_row)
                ],
                axis=0,
            )

        left = whole(0)
        right = whole(1)
        right_even = jnp.where(parity == 0, right, jnp.zeros_like(right))
        right_odd = jnp.where(parity == 1, right, jnp.zeros_like(right))
        for c in range(n_col):
            block = slice(c * cols, (c + 1) * cols)
            rhs = jnp.concatenate([right_even[block], right_odd[block]], axis=0)
            mixed = lax.dot_general(
                left, rhs, (((1,), (1,)), ((), ())), preferred_element_type=jnp.float32
            ).astype(out_ref.dtype)
            for r in range(n_row):
                out_ref[r * n_col + c, hp] = mixed[r * rows : (r + 1) * rows]


def body_kernel(pair, mask, w_agate, w_aproj, w_bgate, w_bproj, w_gate, w_out, w_up, w_down, *, n_row, n_col):
    rows, cols, width = pair.shape
    n_dev = n_row * n_col
    pair_flat, gate, left, right = project(pair, mask, w_agate, w_aproj, w_bgate, w_bproj, w_gate)
    hid = left.shape[-1]
    pairs = hid // n_dev // 2

    def chunks(edges):
        edges = jnp.transpose(edges.reshape(rows, cols, n_dev, pairs, 2), (2, 3, 0, 4, 1))
        return edges.reshape(n_dev, pairs, rows, 2 * cols)

    edges = jnp.stack([chunks(left), chunks(right)], axis=1)
    edges = lax.all_to_all(edges, ("row", "col"), split_axis=0, concat_axis=0, tiled=True)
    mixed = pl.pallas_call(
        functools.partial(mix_kernel, n_col=n_col),
        out_shape=jax.ShapeDtypeStruct((n_dev, pairs, rows, 2 * cols), jnp.bfloat16),
    )(edges)
    mixed = lax.all_to_all(mixed, ("row", "col"), split_axis=0, concat_axis=0, tiled=True)
    mixed = jnp.transpose(mixed.reshape(n_dev, pairs, rows, 2, cols), (2, 4, 0, 1, 3))
    mixed_rows = mixed.astype(jnp.float32).reshape(rows * cols, hid)
    result = transition(pair_flat, gate, mixed_rows, w_out, w_up, w_down)
    return result.astype(jnp.bfloat16).reshape(rows, cols, width)


def project_kernel(mask_ref, pair_ref, wag_ref, wap_ref, wbg_ref, wbp_ref, z_ref, staged_ref, *, block):
    rows, cols, width = pair_ref.shape
    quarter = wag_ref.shape[1] // 2

    def paired(w_ref):
        turned = w_ref[...].astype(jnp.float32).T.astype(jnp.bfloat16)
        return jnp.concatenate([turned[:quarter], turned[quarter:]], axis=1)

    w2 = jnp.concatenate([paired(w) for w in (wag_ref, wap_ref, wbg_ref, wbp_ref)], axis=0)
    row_start = lax.axis_index("row") * rows
    col_start = lax.axis_index("col") * cols
    lane = lax.broadcasted_iota(jnp.int32, (1, 2 * cols), 1) % cols
    col_mask = jnp.zeros((1, 2 * cols), jnp.float32)
    for k in range(cols):
        col_mask = jnp.where(lane == k, mask_ref[col_start + k].astype(jnp.float32), col_mask)

    def rows_of(step, carry):
        first = pl.multiple_of(step * block, block)
        values = pair_ref[pl.ds(first, block)].astype(jnp.float32).reshape(block * cols, width)
        center = values - jnp.mean(values, axis=-1, keepdims=True)
        spread = jnp.mean(center * center, axis=-1, keepdims=True)
        normed = (center * lax.rsqrt(spread + 1e-05)).astype(jnp.bfloat16)
        zeros = jnp.zeros_like(normed)
        top = jnp.concatenate([normed, zeros], axis=1).reshape(block, cols, 2 * width)
        bottom = jnp.concatenate([zeros, normed], axis=1).reshape(block, cols, 2 * width)
        doubled = jnp.concatenate([top, bottom], axis=1).reshape(block * 2 * cols, 2 * width)
        proj = lax.dot_general(
            w2, doubled, (((1,), (1,)), ((), ())), preferred_element_type=jnp.float32
        )
        for i in range(block):
            part = proj[:, i * 2 * cols : (i + 1) * 2 * cols]
            present = col_mask * mask_ref[row_start + first + i].astype(jnp.float32)
            left = jax.nn.sigmoid(part[0:quarter]) * part[quarter : 2 * quarter] * present
            right = jax.nn.sigmoid(part[2 * quarter : 3 * quarter]) * part[3 * quarter :] * present
            staged_ref[pl.ds(first + i, quarter, stride=2 * rows), :] = left
            staged_ref[pl.ds(rows + first + i, quarter, stride=2 * rows), :] = right
        return carry

    lax.fori_loop(0, rows // block, rows_of, 0)
    z_ref[...] = staged_ref[...].astype(z_ref.dtype)


def gate_kernel(pair_ref, wg_ref, gate_ref):
    rows, cols, width = pair_ref.shape
    values = pair_ref[...].astype(jnp.float32).reshape(rows * cols, width)
    center = values - jnp.mean(values, axis=-1, keepdims=True)
    spread = jnp.mean(center * center, axis=-1, keepdims=True)
    normed = (center * lax.rsqrt(spread + 1e-05)).astype(jnp.bfloat16)
    gate = jax.nn.sigmoid(jnp.dot(normed, wg_ref[...], preferred_element_type=jnp.float32))
    gate_ref[...] = gate.reshape(rows, cols, width)


def transition_kernel(mixed_ref, pair_ref, wg_ref, wo_ref, wu_ref, wd_ref, out_ref):
    rows, cols, width = pair_ref.shape
    pairs = mixed_ref.shape[0] // rows

    def norm(values):
        center = values - jnp.mean(values, axis=-1, keepdims=True)
        spread = jnp.mean(center * center, axis=-1, keepdims=True)
        return center * lax.rsqrt(spread + 1e-05)

    parts = []
    for i in range(rows):
        turned = mixed_ref[pl.ds(i, pairs, stride=rows), :].astype(jnp.float32).T
        parts.append(jnp.concatenate([turned[:cols], turned[cols:]], axis=1))
    mixed = jnp.concatenate(parts, axis=0)
    pair = pair_ref[...].astype(jnp.float32).reshape(rows * cols, width)
    gate = jax.nn.sigmoid(jnp.dot(norm(pair).astype(jnp.bfloat16), wg_ref[...], preferred_element_type=jnp.float32))
    mixed_normed = norm(mixed).astype(jnp.bfloat16)
    middle = pair + gate * jnp.dot(mixed_normed, wo_ref[...], preferred_element_type=jnp.float32)
    trans_in = norm(middle).astype(jnp.bfloat16)
    hidden = jnp.maximum(jnp.dot(trans_in, wu_ref[...], preferred_element_type=jnp.float32), 0.0)
    result = middle + jnp.dot(hidden.astype(jnp.bfloat16), wd_ref[...], preferred_element_type=jnp.float32)
    out_ref[...] = result.astype(out_ref.dtype).reshape(rows, cols, width)


def body_fused(pair, mask, w_agate, w_aproj, w_bgate, w_bproj, w_gate, w_out, w_up, w_down, *, n_row, n_col):
    rows, cols, width = pair.shape
    n_dev = n_row * n_col
    hid = w_agate.shape[1]
    pairs = hid // n_dev // 2

    z = pl.pallas_call(
        functools.partial(project_kernel, block=rows),
        out_shape=jax.ShapeDtypeStruct((hid * rows, 2 * cols), jnp.bfloat16),
        in_specs=[pl.BlockSpec(memory_space=pltpu.SMEM)] + [pl.BlockSpec(memory_space=pltpu.VMEM)] * 5,
        scratch_shapes=[pltpu.VMEM((hid * rows, 2 * cols), jnp.float32)],
    )(mask, pair, w_agate, w_aproj, w_bgate, w_bproj)
    edges = z.reshape(n_dev, pairs, 2, rows, 2 * cols)
    edges = lax.all_to_all(edges, ("row", "col"), split_axis=0, concat_axis=0, tiled=True)
    mixed = pl.pallas_call(
        functools.partial(mix_kernel, n_col=n_col, side_major=False),
        out_shape=jax.ShapeDtypeStruct((n_dev, pairs, rows, 2 * cols), jnp.bfloat16),
        grid=(pairs,),
        in_specs=[pl.BlockSpec((n_dev, 1, 2, rows, 2 * cols), lambda hp: (0, hp, 0, 0, 0))],
        out_specs=pl.BlockSpec((n_dev, 1, rows, 2 * cols), lambda hp: (0, hp, 0, 0)),
    )(edges)
    mixed = lax.all_to_all(mixed, ("row", "col"), split_axis=0, concat_axis=0, tiled=True)
    mixed = mixed.reshape(n_dev * pairs * rows, 2 * cols)
    return pl.pallas_call(
        transition_kernel,
        out_shape=jax.ShapeDtypeStruct((rows, cols, width), jnp.bfloat16),
    )(mixed, pair, w_gate, w_out, w_up, w_down)


def body_rows(pair, mask, w_agate, w_aproj, w_bgate, w_bproj, w_gate, w_out, w_up, w_down):
    rows, cols, width = pair.shape
    pair_flat, gate, left, right = project(pair, mask, w_agate, w_aproj, w_bgate, w_bproj, w_gate)
    left_major = jnp.transpose(left.reshape(rows, cols, -1), (2, 0, 1))
    right_major = jnp.transpose(right.reshape(rows, cols, -1), (2, 0, 1))
    left_spread, right_spread = (
        lax.all_to_all(
            lax.all_to_all(left_major, "row", split_axis=0, concat_axis=1, tiled=True),
            "col",
            split_axis=1,
            concat_axis=2,
            tiled=True,
        ),
        lax.all_to_all(
            lax.all_to_all(right_major, "row", split_axis=0, concat_axis=1, tiled=True),
            "col",
            split_axis=1,
            concat_axis=2,
            tiled=True,
        ),
    )
    mixed = jnp.einsum(
        "cik,cjk->cij",
        lax.all_gather(left_spread, "col", axis=1, tiled=True),
        right_spread,
        preferred_element_type=jnp.float32,
    ).astype(jnp.bfloat16)
    mixed = lax.all_to_all(mixed, "row", split_axis=1, concat_axis=0, tiled=True)
    mixed_rows = jnp.transpose(mixed, (1, 2, 0)).astype(jnp.float32).reshape(rows * cols, -1)
    result = transition(pair_flat, gate, mixed_rows, w_out, w_up, w_down)
    return result.astype(jnp.bfloat16).reshape(rows, cols, width)


def solution(mesh):
    placed = (P("row", "col", None), P(), P(), P(), P(), P(), P(), P(), P(), P())
    n_row, n_col = mesh.shape["row"], mesh.shape["col"]

    def run(pair, mask, w_agate, *weights):
        hid = w_agate.shape[1]
        rows, cols = pair.shape[0] // n_row, pair.shape[1] // n_col
        if hid % (2 * n_row * n_col) == 0 and 2 * cols == 128 and rows % 16 == 0 and n_row * rows == n_col * cols:
            body = functools.partial(body_fused, n_row=n_row, n_col=n_col)
        elif hid % (n_row * n_col) == 0:
            body = functools.partial(body_split, n_row=n_row, n_col=n_col)
        else:
            body = body_rows
        mapped = jax.shard_map(
            body, mesh=mesh, in_specs=placed, out_specs=P("row", "col", None), check_vma=False
        )
        return mapped(pair, mask, w_agate, *weights)

    return run
```
